32 devices in a mesh: ctx: 8 (over z, y), head: 4 (over x, core).
Axes of the slice: x: 2, y: 2, z: 4, core: 2. Of those that a mesh axis runs over, the one named last changes fastest.
Arguments:
- x_pool: bfloat16 [3072, 5120], P(('ctx', 'head')), may hold values from -6 to 6
- pool_dest: int32 [3072], replicated, may hold values from -1 to 2047, as said below
- seq_len: int32 [8, 8], P('ctx'), may hold values from 1 to 128, 256 in all within a row
- norm_gain: float32 [5120], replicated, may hold values from 0.1 to 1.9
- w_query: bfloat16 [5120, 2560], P(None, 'head'), may hold values from -0.078125 to 0.078125
- q_bias: float32 [2560], P('head'), may hold values from -102 to 102
- key_projection_weight: bfloat16 [5120, 512], P(None, 'head'), may hold values from -0.078125 to 0.078125
- key_bias_vector: float32 [512], P('head'), may hold values from -5 to 5
- value_projection_weight: bfloat16 [5120, 512], P(None, 'head'), may hold values from -0.078125 to 0.078125
- value_bias_vector: float32 [512], P('head'), may hold values from -3 to 3
- w_out: bfloat16 [2560, 5120], P('head'), may hold values from -0.125 to 0.125
Outputs:
- attn_out: bfloat16 [2048, 5120], P('ctx', 'head')
The draws below stay inside these ranges and needn't reach their ends.
Inputs may be any that keep to these rules, and one draw needn't show every extreme that they name: `pool_dest`: each value is -1 for an empty pool row or o * 256 + j for slot j of context shard o; every slot of every shard is named by exactly one pool row; the pool rows of one device name at most 12 slots of any one shard. `seq_len`: each shard's lengths sum to 256.
All inputs are finite; a program needn't handle non-finite values.
Results may differ from the reference program's by a relative error of at most 0.005.
The reference program's roundings to bfloat16 on the way count: a program that leaves them out, or rounds other values in their place, can miss the bound.
Values may be sent and summed in bfloat16 or wider, within the bound.
No kernel may reach another device: no remote copies, remote signals or barrier semaphores. Data moves between devices by JAX's collectives and lax.ppermute only.
A program may use at most 128 MiB of HBM per device.

```python
import math
import jax
import jax.numpy as jnp
import numpy as np
from jax import lax

MODEL_WIDTH = 5120
HEAD_SIZE = 128
QUERY_HEADS = 20
KEY_VALUE_HEADS = 4
PACKED_SLOTS = 256
SEQ_CTX = 8
CAP = 12
POOL = 3072
N_CTX = 8
N_HEAD = 4


def draw_pool_dest(key, part):
    device_count = N_CTX * N_HEAD
    seat_count = device_count * CAP

    def one_owner(owner_key):
        rank_key, device_key = jax.random.split(owner_key)
        seat_rank = jax.random.permutation(rank_key, seat_count).astype(jnp.int32)
        full_device = jax.random.randint(device_key, (), 0, device_count)
        seat_device = jnp.arange(seat_count, dtype=jnp.int32) // CAP
        priority = jnp.where(seat_device == full_device, 0, seat_count) + seat_rank
        chosen_order = jnp.argsort(priority, stable=True)
        seat_place = jnp.argsort(chosen_order, stable=True).astype(jnp.int32)
        return jnp.where(seat_place < PACKED_SLOTS, seat_place, -1)
    owner_keys = jax.random.split(jax.random.fold_in(key, 11), N_CTX)
    slot_grid = jax.vmap(one_owner)(owner_keys)
    dest_grid = jnp.where(slot_grid >= 0, jnp.arange(N_CTX, dtype=jnp.int32)[:, None] * PACKED_SLOTS + slot_grid, -1)
    dest_grid = dest_grid.reshape(N_CTX, device_count, CAP).transpose(1, 0, 2).reshape(device_count, N_CTX * CAP)
    row_keys = jax.random.split(jax.random.fold_in(key, 12), device_count)
    shuffles = jax.vmap(lambda row_key: jax.random.permutation(row_key, N_CTX * CAP))(row_keys)
    shuffled = jnp.take_along_axis(dest_grid, shuffles, axis=1)
    return shuffled.reshape(-1).astype(jnp.int32)


def draw_q_bias(key, part):
    head_key, entry_key = jax.random.split(jax.random.fold_in(key, 21))
    spread = jnp.exp(jax.random.uniform(head_key, (QUERY_HEADS, 1), minval=math.log(0.3), maxval=math.log(3.0)))
    entries = jnp.clip(jax.random.normal(entry_key, (QUERY_HEADS, HEAD_SIZE)), -5.0, 5.0)
    return (spread * entries).reshape(QUERY_HEADS * HEAD_SIZE).astype(jnp.float32)


def block_levels(key, extent, cuts, least, high):
    factor_of, own = 1.0, jax.random.fold_in(key, 6)
    for dim, blocks in cuts:
        draws = jnp.exp(jax.random.uniform(jax.random.fold_in(own, dim), (blocks,), jnp.float32, least / len(cuts), high / len(cuts)))
        factor_of = factor_of * jnp.repeat(draws, extent[dim] // blocks).reshape([-1 if axis == dim else 1 for axis in range(len(extent))])
    return factor_of


def length_profile(count, total, most, slope):
    portions = [(1 << 20) // math.isqrt(standing ** slope) + 1 for standing in range(2, count + 1)]
    surplus, holding = total - most - (count - 1), [1] * (count - 1)
    while surplus > 0:
        free = [i for i in range(count - 1) if holding[i] < most]
        mass, left = sum([portions[i] for i in free]), surplus
        for i in free:
            addition = min(most - holding[i], max(1, left * portions[i] // mass), surplus)
            holding[i] = holding[i] + addition
            surplus = surplus - addition
    return np.array([most] + holding)


def uneven(rng, count, total, bound, skew):
    if count == 2:
        one = jax.random.randint(rng, (), max(1, total - bound), min(bound, total - 1) + 1)
        return jnp.stack([one, total - one])
    lengths = jnp.asarray(length_profile(count, total, bound, skew), jnp.int32)
    pairs = (count - 1) // 2
    giver, sink = lengths[1:1 + 2 * pairs:2], lengths[2:2 + 2 * pairs:2]
    slack = jnp.minimum(giver - 1, bound - sink)
    passed = jax.random.randint(jax.random.fold_in(rng, 1), (pairs,), 0, 1 << 20) % (slack + 1)
    lengths = lengths.at[1:1 + 2 * pairs:2].set(giver - passed).at[2:2 + 2 * pairs:2].set(sink + passed)
    return lengths[jax.random.permutation(jax.random.fold_in(rng, 2), count)]


def normal_values(rng, dims, width, reach, pieces=(), held_as=jnp.bfloat16):
    gain = block_levels(rng, dims, pieces, -0.22, 0.18) if pieces else 1.0
    values = jax.random.normal(rng, dims, jnp.float32) * width * gain
    return jnp.minimum(jnp.maximum(values, -reach), reach).astype(held_as)


def setup_inputs(seed: int = 0) -> dict:
    key_of = jax.random.split(jax.random.key(seed), 12)
    x_pool = normal_values(key_of[0], (POOL, MODEL_WIDTH), 1.0, 6.0, ((0, 32),))
    pool_dest = draw_pool_dest(jax.random.fold_in(key_of[11], 71), 0)
    seq_len = jax.vmap(lambda own: uneven(own, SEQ_CTX, PACKED_SLOTS, PACKED_SLOTS // 2, 2))(jax.random.split(key_of[2], N_CTX)).reshape((N_CTX, SEQ_CTX)).astype(jnp.int32)
    norm_gain = jnp.clip(1.0 + 0.18 * jax.random.normal(key_of[3], (MODEL_WIDTH,), jnp.float32), 0.1, 1.9)
    w_query = normal_values(key_of[4], (MODEL_WIDTH, QUERY_HEADS * HEAD_SIZE), MODEL_WIDTH ** -0.5, 0.078125, ((1, 4),))
    q_bias = draw_q_bias(jax.random.fold_in(key_of[11], 71), 0)
    key_projection_weight = normal_values(key_of[6], (MODEL_WIDTH, KEY_VALUE_HEADS * HEAD_SIZE), MODEL_WIDTH ** -0.5, 0.078125, ((1, 4),))
    key_bias_vector = normal_values(key_of[7], (KEY_VALUE_HEADS * HEAD_SIZE,), 1.0, 5.0, ((0, 4),), jnp.float32)
    value_projection_weight = normal_values(key_of[8], (MODEL_WIDTH, KEY_VALUE_HEADS * HEAD_SIZE), MODEL_WIDTH ** -0.5, 0.078125, ((1, 4),))
    value_bias_vector = normal_values(key_of[9], (KEY_VALUE_HEADS * HEAD_SIZE,), 0.5, 3.0, ((0, 4),), jnp.float32)
    w_out = normal_values(key_of[10], (QUERY_HEADS * HEAD_SIZE, MODEL_WIDTH), (QUERY_HEADS * HEAD_SIZE) ** -0.5, 0.125, ((0, 4),))
    return {"x_pool": x_pool, "pool_dest": pool_dest, "seq_len": seq_len, "norm_gain": norm_gain, "w_query": w_query, "q_bias": q_bias, "key_projection_weight": key_projection_weight, "key_bias_vector": key_bias_vector, "value_projection_weight": value_projection_weight, "value_bias_vector": value_bias_vector, "w_out": w_out}


rope_base = 1000000.0
norm_eps = 1e-06

def positions_of(lengths_row):
    seq_ends = jnp.cumsum(lengths_row).astype(jnp.int32)
    index_col = jnp.arange(PACKED_SLOTS, dtype=jnp.int32)[:, None]
    finished = (seq_ends[None, :] <= index_col).astype(jnp.int32)
    segment = lax.optimization_barrier(jnp.sum(finished, axis=1)).astype(jnp.int32)
    sequence_starts = index_col[:, 0] - lax.optimization_barrier(jnp.sum(finished * lengths_row[None, :], axis=1)).astype(jnp.int32)
    return (segment, sequence_starts)

def apply_rotary(values, sequence_starts):
    half_dim = HEAD_SIZE // 2
    frequency = jnp.exp(jnp.arange(half_dim, dtype=jnp.float32) * (-2.0 * math.log(rope_base) / HEAD_SIZE))
    angles = sequence_starts.astype(jnp.float32)[:, None] * frequency[None, :]
    cosine = jnp.cos(angles)[:, None, :]
    sine_table = jnp.sin(angles)[:, None, :]
    first_half = values[..., :half_dim]
    second_half = values[..., half_dim:]
    return jnp.concatenate([first_half * cosine - second_half * sine_table, second_half * cosine + first_half * sine_table], axis=-1)

def one_shard(packed_x, lengths_row, norm_gain, w_query, q_bias, key_projection_weight, key_bias_vector, value_projection_weight, value_bias_vector, w_out):
    segment, sequence_starts = positions_of(lengths_row)
    values_wide = packed_x.astype(jnp.float32)
    normalized_input = (values_wide * lax.rsqrt(lax.optimization_barrier(jnp.mean(values_wide * values_wide, axis=-1, keepdims=True)) + norm_eps) * norm_gain).astype(jnp.bfloat16)
    query_matrix = jnp.dot(normalized_input, w_query, preferred_element_type=jnp.float32) + q_bias
    query_matrix = apply_rotary(query_matrix.reshape(PACKED_SLOTS, QUERY_HEADS, HEAD_SIZE), sequence_starts).astype(jnp.bfloat16)
    projected_key_rows = jnp.dot(normalized_input, key_projection_weight, preferred_element_type=jnp.float32) + key_bias_vector
    projected_key_rows = apply_rotary(projected_key_rows.reshape(PACKED_SLOTS, KEY_VALUE_HEADS, HEAD_SIZE), sequence_starts).astype(jnp.bfloat16)
    projected_value_rows = (jnp.dot(normalized_input, value_projection_weight, preferred_element_type=jnp.float32) + value_bias_vector).astype(jnp.bfloat16).reshape(PACKED_SLOTS, KEY_VALUE_HEADS, HEAD_SIZE)
    query_group_count = QUERY_HEADS // KEY_VALUE_HEADS
    expanded_query = lax.optimization_barrier(query_matrix).astype(jnp.float32).reshape(PACKED_SLOTS, KEY_VALUE_HEADS, query_group_count, HEAD_SIZE)
    key_wide = lax.optimization_barrier(projected_key_rows).astype(jnp.float32)
    value_wide = lax.optimization_barrier(projected_value_rows).astype(jnp.float32)
    scores = jnp.einsum('qkgd,tkd->kgqt', expanded_query, key_wide) * (1.0 / math.sqrt(HEAD_SIZE))
    slot_ids = jnp.arange(PACKED_SLOTS, dtype=jnp.int32)
    allowed = (segment[:, None] == segment[None, :]) & (slot_ids[None, :] <= slot_ids[:, None])
    scores = jnp.where(allowed[None, None], scores, -1e+30)
    row_max = lax.optimization_barrier(jnp.max(scores, axis=-1, keepdims=True))
    weights = jnp.exp(scores - row_max)
    row_total = lax.optimization_barrier(jnp.sum(weights, axis=-1, keepdims=True))
    probability = lax.optimization_barrier((weights / row_total).astype(jnp.bfloat16)).astype(jnp.float32)
    mixed_heads = jnp.einsum('kgqt,tkd->qkgd', probability, value_wide).astype(jnp.bfloat16).reshape(PACKED_SLOTS, QUERY_HEADS * HEAD_SIZE)
    return jnp.dot(mixed_heads, w_out, preferred_element_type=jnp.float32).astype(jnp.bfloat16)

def reference(x_pool, pool_dest, seq_len, norm_gain, w_query, q_bias, key_projection_weight, key_bias_vector, value_projection_weight, value_bias_vector, w_out):
    target = jnp.where(pool_dest >= 0, pool_dest, N_CTX * PACKED_SLOTS).astype(jnp.int32)
    packed = jnp.zeros((N_CTX * PACKED_SLOTS, MODEL_WIDTH), jnp.bfloat16).at[target].set(x_pool, mode='drop')

    def shard_out(shard_pair):
        return one_shard(shard_pair[0], shard_pair[1], norm_gain, w_query, q_bias, key_projection_weight, key_bias_vector, value_projection_weight, value_bias_vector, w_out)
    outputs = lax.map(shard_out, (packed.reshape(N_CTX, PACKED_SLOTS, MODEL_WIDTH), seq_len))
    return outputs.reshape(N_CTX * PACKED_SLOTS, MODEL_WIDTH)
```

```python
import math

import jax
import jax.numpy as jnp
from jax import lax
from jax.sharding import PartitionSpec as P

HEAD_SIZE = 128
PACKED_SLOTS = 256


rope_base = 1000000.0
norm_eps = 1e-06


def send_places(targets, owner_count, capacity, pack_len):
    is_filled = targets >= 0
    owner_ids = jnp.where(is_filled, targets // pack_len, -1)
    membership = (owner_ids[:, None] == jnp.arange(owner_count, dtype=jnp.int32)[None, :]).astype(
        jnp.int32
    )
    earlier = jnp.cumsum(membership, axis=0) - membership
    rank_in = jnp.sum(earlier * membership, axis=1)
    return jnp.where(is_filled, owner_ids * capacity + rank_in, owner_count * capacity)


def one_hot_rows(index, count):
    return (index[:, None] == jnp.arange(count, dtype=jnp.int32)[None, :]).astype(jnp.bfloat16)


def select_rows(index, values):
    picked = jnp.dot(
        one_hot_rows(index, values.shape[0]), values, preferred_element_type=jnp.float32
    )
    return picked.astype(values.dtype)


def apply_rotary(values, sequence_starts, head_dim):
    half_dim = head_dim // 2
    frequency = jnp.exp(
        jnp.arange(half_dim, dtype=jnp.float32) * (-2.0 * math.log(rope_base) / head_dim)
    )
    angles = sequence_starts.astype(jnp.float32)[:, None] * frequency[None, :]
    cosine = jnp.cos(angles)[:, None, :]
    sine_table = jnp.sin(angles)[:, None, :]
    first_half = values[..., :half_dim]
    second_half = values[..., half_dim:]
    return jnp.concatenate(
        [
            first_half * cosine - second_half * sine_table,
            second_half * cosine + first_half * sine_table,
        ],
        axis=-1,
    )


def local(
    x_pool,
    pool_dest,
    seq_len,
    norm_gain,
    w_query,
    q_bias,
    key_projection_weight,
    key_bias_vector,
    value_projection_weight,
    value_bias_vector,
    w_out,
):
    ctx_count = lax.axis_size("ctx")
    head_count = lax.axis_size("head")
    pool_rows = x_pool.shape[0]
    capacity = pool_rows // ctx_count
    group_rows = pool_rows * head_count
    group_cap = capacity * head_count
    pack_len = PACKED_SLOTS
    head_dim = HEAD_SIZE
    ctx_index = lax.axis_index("ctx")

    all_lengths = lax.all_gather(seq_len, "ctx", tiled=True)
    group_x = lax.all_gather(x_pool, "head", tiled=True)

    dest_grid = pool_dest.reshape(ctx_count, group_rows)
    my_dest = lax.dynamic_index_in_dim(dest_grid, ctx_index, 0, keepdims=False)
    is_filled = my_dest >= 0
    owner = jnp.where(is_filled, my_dest // pack_len, 0)
    slot = jnp.where(is_filled, my_dest % pack_len, 0)
    seq_ends = jnp.cumsum(all_lengths, axis=1).astype(jnp.int32)
    row_ends = jnp.take(seq_ends, owner, axis=0)
    row_lengths = jnp.take(all_lengths, owner, axis=0)
    finished = (row_ends <= slot[:, None]).astype(jnp.int32)
    sequence_starts = slot - jnp.sum(finished * row_lengths, axis=1)

    values_wide = group_x.astype(jnp.float32)
    normalized_input = (
        values_wide
        * lax.rsqrt(jnp.mean(values_wide * values_wide, axis=-1, keepdims=True) + norm_eps)
        * norm_gain
    ).astype(jnp.bfloat16)
    local_heads = w_query.shape[1] // head_dim
    local_kv = key_projection_weight.shape[1] // head_dim
    query_group_count = local_heads // local_kv
    query_matrix = jnp.dot(normalized_input, w_query, preferred_element_type=jnp.float32) + q_bias
    query_matrix = apply_rotary(
        query_matrix.reshape(group_rows, local_heads, head_dim), sequence_starts, head_dim
    ).astype(jnp.bfloat16)
    projected_key_rows = (
        jnp.dot(normalized_input, key_projection_weight, preferred_element_type=jnp.float32)
        + key_bias_vector
    )
    projected_key_rows = apply_rotary(
        projected_key_rows.reshape(group_rows, local_kv, head_dim), sequence_starts, head_dim
    ).astype(jnp.bfloat16)
    projected_value_rows = (
        jnp.dot(normalized_input, value_projection_weight, preferred_element_type=jnp.float32)
        + value_bias_vector
    ).astype(jnp.bfloat16)
    qkv = jnp.concatenate(
        [
            query_matrix.reshape(group_rows, local_heads * head_dim),
            projected_key_rows.reshape(group_rows, local_kv * head_dim),
            projected_value_rows,
        ],
        axis=1,
    )

    places = send_places(my_dest, ctx_count, group_cap, pack_len)
    send_hot = (
        places[None, :] == jnp.arange(ctx_count * group_cap, dtype=jnp.int32)[:, None]
    ).astype(jnp.bfloat16)
    outgoing = jnp.dot(send_hot, qkv, preferred_element_type=jnp.float32).astype(jnp.bfloat16)
    arrived = lax.all_to_all(outgoing, "ctx", split_axis=0, concat_axis=0, tiled=True)

    mine = (pool_dest >= 0) & (pool_dest // pack_len == ctx_index)
    mine_grid = mine.reshape(ctx_count, group_rows).astype(jnp.int32)
    rank_in = jnp.cumsum(mine_grid, axis=1) - mine_grid
    arrived_index = (
        jnp.arange(ctx_count, dtype=jnp.int32)[:, None] * group_cap + rank_in
    ).reshape(-1)
    my_slot_of_row = jnp.where(mine, pool_dest - ctx_index * pack_len, -1)
    slot_ids = jnp.arange(pack_len, dtype=jnp.int32)
    names_slot = my_slot_of_row[None, :] == slot_ids[:, None]
    source_of_slot = jnp.sum(jnp.where(names_slot, arrived_index[None, :], 0), axis=1)
    packed_qkv = select_rows(source_of_slot, arrived)

    q_width = local_heads * head_dim
    kv_width = local_kv * head_dim
    query_matrix = packed_qkv[:, :q_width].reshape(pack_len, local_kv, query_group_count, head_dim)
    projected_key_rows = packed_qkv[:, q_width : q_width + kv_width].reshape(
        pack_len, local_kv, head_dim
    )
    projected_value_rows = packed_qkv[:, q_width + kv_width :].reshape(pack_len, local_kv, head_dim)

    own_lengths = seq_len[0]
    own_ends = jnp.cumsum(own_lengths).astype(jnp.int32)
    segment = jnp.sum((own_ends[None, :] <= slot_ids[:, None]).astype(jnp.int32), axis=1)

    score_scale = 1.0 / math.sqrt(head_dim)
    scores = (
        jnp.einsum(
            "qkgd,tkd->kgqt",
            query_matrix,
            projected_key_rows,
            preferred_element_type=jnp.float32,
        )
        * score_scale
    )
    allowed = (segment[:, None] == segment[None, :]) & (slot_ids[None, :] <= slot_ids[:, None])
    scores = jnp.where(allowed[None, None], scores, -1e30)
    row_max = jnp.max(scores, axis=-1, keepdims=True)
    weights = jnp.exp(scores - row_max)
    row_total = jnp.sum(weights, axis=-1, keepdims=True)
    probability = (weights / row_total).astype(jnp.bfloat16)
    mixed_heads = jnp.einsum(
        "kgqt,tkd->qkgd", probability, projected_value_rows, preferred_element_type=jnp.float32
    )
    mixed_heads = mixed_heads.astype(jnp.bfloat16).reshape(pack_len, local_heads * head_dim)
    partial_out = jnp.dot(mixed_heads, w_out, preferred_element_type=jnp.float32)
    return lax.psum_scatter(partial_out, "head", scatter_dimension=1, tiled=True).astype(
        jnp.bfloat16
    )


def solution(mesh):
    in_specs = (
        P(("ctx", "head"), None),
        P(),
        P("ctx", None),
        P(),
        P(None, "head"),
        P("head"),
        P(None, "head"),
        P("head"),
        P(None, "head"),
        P("head"),
        P("head", None),
    )
    out_specs = P("ctx", "head")
    return jax.shard_map(local, mesh=mesh, in_specs=in_specs, out_specs=out_specs, check_vma=False)
```

```python
import math

import jax
import jax.numpy as jnp
from jax import lax
from jax.sharding import PartitionSpec as P

HEAD_SIZE = 128
PACKED_SLOTS = 256


rope_base = 1000000.0
norm_eps = 1e-06


def send_places(targets, owner_count, capacity, pack_len):
    is_filled = targets >= 0
    owner_ids = jnp.where(is_filled, targets // pack_len, -1)
    membership = (owner_ids[:, None] == jnp.arange(owner_count, dtype=jnp.int32)[None, :]).astype(
        jnp.int32
    )
    earlier = jnp.cumsum(membership, axis=0) - membership
    rank_in = jnp.sum(earlier * membership, axis=1)
    return jnp.where(is_filled, owner_ids * capacity + rank_in, owner_count * capacity)


def one_hot_rows(index, count):
    return (index[:, None] == jnp.arange(count, dtype=jnp.int32)[None, :]).astype(jnp.bfloat16)


def select_rows(index, values):
    picked = jnp.dot(
        one_hot_rows(index, values.shape[0]), values, preferred_element_type=jnp.float32
    )
    return picked.astype(values.dtype)


def apply_rotary(values, sequence_starts, head_dim):
    half_dim = head_dim // 2
    frequency = jnp.exp(
        jnp.arange(half_dim, dtype=jnp.float32) * (-2.0 * math.log(rope_base) / head_dim)
    )
    angles = sequence_starts.astype(jnp.float32)[:, None] * frequency[None, :]
    cosine = jnp.cos(angles)[:, None, :]
    sine_table = jnp.sin(angles)[:, None, :]
    first_half = values[..., :half_dim]
    second_half = values[..., half_dim:]
    return jnp.concatenate(
        [
            first_half * cosine - second_half * sine_table,
            second_half * cosine + first_half * sine_table,
        ],
        axis=-1,
    )


def local(
    x_pool,
    pool_dest,
    seq_len,
    norm_gain,
    w_query,
    q_bias,
    key_projection_weight,
    key_bias_vector,
    value_projection_weight,
    value_bias_vector,
    w_out,
):
    ctx_count = lax.axis_size("ctx")
    head_count = lax.axis_size("head")
    pool_rows = x_pool.shape[0]
    capacity = pool_rows // ctx_count
    group_rows = pool_rows * head_count
    group_cap = capacity * head_count
    pack_len = PACKED_SLOTS
    head_dim = HEAD_SIZE
    ctx_index = lax.axis_index("ctx")

    all_lengths = (
        lax.all_gather(seq_len.astype(jnp.float32), "ctx", tiled=True).astype(jnp.int32)
    )
    group_x = lax.all_gather(x_pool, "head", tiled=True)

    dest_grid = pool_dest.reshape(ctx_count, group_rows)
    my_dest = lax.dynamic_index_in_dim(dest_grid, ctx_index, 0, keepdims=False)
    is_filled = my_dest >= 0
    owner = jnp.where(is_filled, my_dest // pack_len, 0)
    slot = jnp.where(is_filled, my_dest % pack_len, 0)
    seq_ends = jnp.cumsum(all_lengths, axis=1).astype(jnp.int32)
    row_ends = jnp.take(seq_ends, owner, axis=0)
    row_lengths = jnp.take(all_lengths, owner, axis=0)
    finished = (row_ends <= slot[:, None]).astype(jnp.int32)
    sequence_starts = slot - jnp.sum(finished * row_lengths, axis=1)

    values_wide = group_x.astype(jnp.float32)
    normalized_input = (
        values_wide
        * lax.rsqrt(jnp.mean(values_wide * values_wide, axis=-1, keepdims=True) + norm_eps)
        * norm_gain
    ).astype(jnp.bfloat16)
    local_heads = w_query.shape[1] // head_dim
    local_kv = key_projection_weight.shape[1] // head_dim
    query_group_count = local_heads // local_kv
    query_matrix = jnp.dot(normalized_input, w_query, preferred_element_type=jnp.float32) + q_bias
    query_matrix = apply_rotary(
        query_matrix.reshape(group_rows, local_heads, head_dim), sequence_starts, head_dim
    ).astype(jnp.bfloat16)
    projected_key_rows = (
        jnp.dot(normalized_input, key_projection_weight, preferred_element_type=jnp.float32)
        + key_bias_vector
    )
    projected_key_rows = apply_rotary(
        projected_key_rows.reshape(group_rows, local_kv, head_dim), sequence_starts, head_dim
    ).astype(jnp.bfloat16)
    projected_value_rows = (
        jnp.dot(normalized_input, value_projection_weight, preferred_element_type=jnp.float32)
        + value_bias_vector
    ).astype(jnp.bfloat16)
    qkv = jnp.concatenate(
        [
            query_matrix.reshape(group_rows, local_heads * head_dim),
            projected_key_rows.reshape(group_rows, local_kv * head_dim),
            projected_value_rows,
        ],
        axis=1,
    )

    places = send_places(my_dest, ctx_count, group_cap, pack_len)
    send_hot = (
        places[None, :] == jnp.arange(ctx_count * group_cap, dtype=jnp.int32)[:, None]
    ).astype(jnp.bfloat16)
    outgoing = jnp.dot(send_hot, qkv, preferred_element_type=jnp.float32).astype(jnp.bfloat16)
    arrived = lax.all_to_all(outgoing, "ctx", split_axis=0, concat_axis=0, tiled=True)

    mine = (pool_dest >= 0) & (pool_dest // pack_len == ctx_index)
    mine_grid = mine.reshape(ctx_count, group_rows).astype(jnp.int32)
    rank_in = jnp.cumsum(mine_grid, axis=1) - mine_grid
    arrived_index = (
        jnp.arange(ctx_count, dtype=jnp.int32)[:, None] * group_cap + rank_in
    ).reshape(-1)
    my_slot_of_row = jnp.where(mine, pool_dest - ctx_index * pack_len, -1)
    slot_ids = jnp.arange(pack_len, dtype=jnp.int32)
    names_slot = my_slot_of_row[None, :] == slot_ids[:, None]
    source_of_slot = jnp.sum(jnp.where(names_slot, arrived_index[None, :], 0), axis=1)
    packed_qkv = select_rows(source_of_slot, arrived)

    q_width = local_heads * head_dim
    kv_width = local_kv * head_dim
    query_matrix = packed_qkv[:, :q_width].reshape(pack_len, local_kv, query_group_count, head_dim)
    projected_key_rows = packed_qkv[:, q_width : q_width + kv_width].reshape(
        pack_len, local_kv, head_dim
    )
    projected_value_rows = packed_qkv[:, q_width + kv_width :].reshape(pack_len, local_kv, head_dim)

    own_lengths = seq_len[0]
    own_ends = jnp.cumsum(own_lengths).astype(jnp.int32)
    segment = jnp.sum((own_ends[None, :] <= slot_ids[:, None]).astype(jnp.int32), axis=1)

    score_scale = 1.0 / math.sqrt(head_dim)
    scores = (
        jnp.einsum(
            "qkgd,tkd->kgqt",
            query_matrix,
            projected_key_rows,
            preferred_element_type=jnp.float32,
        )
        * score_scale
    )
    allowed = (segment[:, None] == segment[None, :]) & (slot_ids[None, :] <= slot_ids[:, None])
    scores = jnp.where(allowed[None, None], scores, -1e30)
    row_max = jnp.max(scores, axis=-1, keepdims=True)
    weights = jnp.exp(scores - row_max)
    row_total = jnp.sum(weights, axis=-1, keepdims=True)
    probability = (weights / row_total).astype(jnp.bfloat16)
    mixed_heads = jnp.einsum(
        "kgqt,tkd->qkgd", probability, projected_value_rows, preferred_element_type=jnp.float32
    )
    mixed_heads = mixed_heads.astype(jnp.bfloat16).reshape(pack_len, local_heads * head_dim)
    partial_out = jnp.dot(mixed_heads, w_out, preferred_element_type=jnp.float32)
    return halving_scatter(partial_out, "head", head_count).astype(jnp.bfloat16)


def halving_scatter(partial, axis_name, count):
    bits = count.bit_length() - 1
    if count != 1 << bits or bits == 0:
        return lax.psum_scatter(partial, axis_name, scatter_dimension=1, tiled=True)
    rows, width = partial.shape
    block = width // count
    me = lax.axis_index(axis_name)
    blocks = partial.reshape((rows,) + (2,) * bits + (block,))
    for stage in range(bits):
        axis = bits - stage
        bit = (me >> stage) & 1
        keep = lax.dynamic_index_in_dim(blocks, bit, axis, keepdims=False)
        send = lax.dynamic_index_in_dim(blocks, 1 - bit, axis, keepdims=False)
        pairs = [(i, i ^ (1 << stage)) for i in range(count)]
        blocks = keep + lax.ppermute(send, axis_name, pairs)
    return blocks.reshape(rows, block)


def solution(mesh):
    in_specs = (
        P(("ctx", "head"), None),
        P(),
        P("ctx", None),
        P(),
        P(None, "head"),
        P("head"),
        P(None, "head"),
        P("head"),
        P(None, "head"),
        P("head"),
        P("head", None),
    )
    out_specs = P("ctx", "head")
    return jax.shard_map(local, mesh=mesh, in_specs=in_specs, out_specs=out_specs, check_vma=False)
```

```python
import math

import jax
import jax.numpy as jnp
from jax import lax
from jax.sharding import PartitionSpec as P

HEAD_SIZE = 128
PACKED_SLOTS = 256


rope_base = 1000000.0
norm_eps = 1e-06


def send_places(targets, owner_count, capacity, pack_len):
    is_filled = targets >= 0
    owner_ids = jnp.where(is_filled, targets // pack_len, -1)
    membership = (owner_ids[:, None] == jnp.arange(owner_count, dtype=jnp.int32)[None, :]).astype(
        jnp.int32
    )
    earlier = jnp.cumsum(membership, axis=0) - membership
    rank_in = jnp.sum(earlier * membership, axis=1)
    return jnp.where(is_filled, owner_ids * capacity + rank_in, owner_count * capacity)


def one_hot_rows(index, count):
    return (index[:, None] == jnp.arange(count, dtype=jnp.int32)[None, :]).astype(jnp.bfloat16)


def select_rows(index, values):
    picked = jnp.dot(
        one_hot_rows(index, values.shape[0]), values, preferred_element_type=jnp.float32
    )
    return picked.astype(values.dtype)


def apply_rotary(values, sequence_starts, head_dim):
    half_dim = head_dim // 2
    frequency = jnp.exp(
        jnp.arange(half_dim, dtype=jnp.float32) * (-2.0 * math.log(rope_base) / head_dim)
    )
    angles = sequence_starts.astype(jnp.float32)[:, None] * frequency[None, :]
    cosine = jnp.cos(angles)[:, None, :]
    sine_table = jnp.sin(angles)[:, None, :]
    first_half = values[..., :half_dim]
    second_half = values[..., half_dim:]
    return jnp.concatenate(
        [
            first_half * cosine - second_half * sine_table,
            second_half * cosine + first_half * sine_table,
        ],
        axis=-1,
    )


def local(
    x_pool,
    pool_dest,
    seq_len,
    norm_gain,
    w_query,
    q_bias,
    key_projection_weight,
    key_bias_vector,
    value_projection_weight,
    value_bias_vector,
    w_out,
):
    ctx_count = lax.axis_size("ctx")
    head_count = lax.axis_size("head")
    pool_rows = x_pool.shape[0]
    capacity = pool_rows // ctx_count
    group_rows = pool_rows * head_count
    group_cap = capacity * head_count
    pack_len = PACKED_SLOTS
    head_dim = HEAD_SIZE
    ctx_index = lax.axis_index("ctx")

    length_rows = jnp.where(
        jnp.arange(ctx_count, dtype=jnp.int32)[:, None] == ctx_index,
        seq_len.astype(jnp.float32),
        0.0,
    )
    all_lengths = lax.psum(length_rows, "ctx").astype(jnp.int32)
    group_x = doubling_gather(x_pool, "head", head_count)

    dest_grid = pool_dest.reshape(ctx_count, group_rows)
    my_dest = lax.dynamic_index_in_dim(dest_grid, ctx_index, 0, keepdims=False)
    is_filled = my_dest >= 0
    owner = jnp.where(is_filled, my_dest // pack_len, 0)
    slot = jnp.where(is_filled, my_dest % pack_len, 0)
    seq_ends = jnp.cumsum(all_lengths, axis=1).astype(jnp.int32)
    row_ends = jnp.take(seq_ends, owner, axis=0)
    row_lengths = jnp.take(all_lengths, owner, axis=0)
    finished = (row_ends <= slot[:, None]).astype(jnp.int32)
    sequence_starts = slot - jnp.sum(finished * row_lengths, axis=1)

    values_wide = group_x.astype(jnp.float32)
    normalized_input = (
        values_wide
        * lax.rsqrt(jnp.mean(values_wide * values_wide, axis=-1, keepdims=True) + norm_eps)
        * norm_gain
    ).astype(jnp.bfloat16)
    local_heads = w_query.shape[1] // head_dim
    local_kv = key_projection_weight.shape[1] // head_dim
    query_group_count = local_heads // local_kv
    query_matrix = jnp.dot(normalized_input, w_query, preferred_element_type=jnp.float32) + q_bias
    query_matrix = apply_rotary(
        query_matrix.reshape(group_rows, local_heads, head_dim), sequence_starts, head_dim
    ).astype(jnp.bfloat16)
    projected_key_rows = (
        jnp.dot(normalized_input, key_projection_weight, preferred_element_type=jnp.float32)
        + key_bias_vector
    )
    projected_key_rows = apply_rotary(
        projected_key_rows.reshape(group_rows, local_kv, head_dim), sequence_starts, head_dim
    ).astype(jnp.bfloat16)
    projected_value_rows = (
        jnp.dot(normalized_input, value_projection_weight, preferred_element_type=jnp.float32)
        + value_bias_vector
    ).astype(jnp.bfloat16)
    qkv = jnp.concatenate(
        [
            query_matrix.reshape(group_rows, local_heads * head_dim),
            projected_key_rows.reshape(group_rows, local_kv * head_dim),
            projected_value_rows,
        ],
        axis=1,
    )

    places = send_places(my_dest, ctx_count, group_cap, pack_len)
    send_hot = (
        places[None, :] == jnp.arange(ctx_count * group_cap, dtype=jnp.int32)[:, None]
    ).astype(jnp.bfloat16)
    outgoing = jnp.dot(send_hot, qkv, preferred_element_type=jnp.float32).astype(jnp.bfloat16)
    arrived = lax.all_to_all(outgoing, "ctx", split_axis=0, concat_axis=0, tiled=True)

    mine = (pool_dest >= 0) & (pool_dest // pack_len == ctx_index)
    mine_grid = mine.reshape(ctx_count, group_rows).astype(jnp.int32)
    rank_in = jnp.cumsum(mine_grid, axis=1) - mine_grid
    arrived_index = (
        jnp.arange(ctx_count, dtype=jnp.int32)[:, None] * group_cap + rank_in
    ).reshape(-1)
    my_slot_of_row = jnp.where(mine, pool_dest - ctx_index * pack_len, -1)
    slot_ids = jnp.arange(pack_len, dtype=jnp.int32)
    names_slot = my_slot_of_row[None, :] == slot_ids[:, None]
    source_of_slot = jnp.sum(jnp.where(names_slot, arrived_index[None, :], 0), axis=1)
    packed_qkv = select_rows(source_of_slot, arrived)

    q_width = local_heads * head_dim
    kv_width = local_kv * head_dim
    query_matrix = packed_qkv[:, :q_width].reshape(pack_len, local_kv, query_group_count, head_dim)
    projected_key_rows = packed_qkv[:, q_width : q_width + kv_width].reshape(
        pack_len, local_kv, head_dim
    )
    projected_value_rows = packed_qkv[:, q_width + kv_width :].reshape(pack_len, local_kv, head_dim)

    own_lengths = seq_len[0]
    own_ends = jnp.cumsum(own_lengths).astype(jnp.int32)
    segment = jnp.sum((own_ends[None, :] <= slot_ids[:, None]).astype(jnp.int32), axis=1)

    score_scale = 1.0 / math.sqrt(head_dim)
    scores = (
        jnp.einsum(
            "qkgd,tkd->kgqt",
            query_matrix,
            projected_key_rows,
            preferred_element_type=jnp.float32,
        )
        * score_scale
    )
    allowed = (segment[:, None] == segment[None, :]) & (slot_ids[None, :] <= slot_ids[:, None])
    scores = jnp.where(allowed[None, None], scores, -1e30)
    row_max = jnp.max(scores, axis=-1, keepdims=True)
    weights = jnp.exp(scores - row_max)
    row_total = jnp.sum(weights, axis=-1, keepdims=True)
    probability = (weights / row_total).astype(jnp.bfloat16)
    mixed_heads = jnp.einsum(
        "kgqt,tkd->qkgd", probability, projected_value_rows, preferred_element_type=jnp.float32
    )
    mixed_heads = mixed_heads.astype(jnp.bfloat16).reshape(pack_len, local_heads * head_dim)
    partial_out = jnp.dot(mixed_heads, w_out, preferred_element_type=jnp.float32)
    return halving_scatter(partial_out, "head", head_count).astype(jnp.bfloat16)


def halving_scatter(partial, axis_name, count):
    bits = count.bit_length() - 1
    if count != 1 << bits or bits == 0:
        return lax.psum_scatter(partial, axis_name, scatter_dimension=1, tiled=True)
    block = partial.shape[1] // count
    me = lax.axis_index(axis_name)
    pieces = [(b, partial[:, b * block : (b + 1) * block]) for b in range(count)]
    for stage in range(bits):
        bit = (me >> stage) & 1
        lows = [(b, x) for b, x in pieces if not (b >> stage) & 1]
        highs = [x for b, x in pieces if (b >> stage) & 1]
        keep = [jnp.where(bit == 0, lo, hi) for (_, lo), hi in zip(lows, highs)]
        send = jnp.stack([jnp.where(bit == 0, hi, lo) for (_, lo), hi in zip(lows, highs)])
        pairs = [(i, i ^ (1 << stage)) for i in range(count)]
        got = lax.ppermute(send, axis_name, pairs)
        pieces = [(b, k + got[i]) for i, ((b, _), k) in enumerate(zip(lows, keep))]
    return pieces[0][1]


def doubling_gather(part, axis_name, count):
    bits = count.bit_length() - 1
    if count != 1 << bits or bits == 0:
        return lax.all_gather(part, axis_name, tiled=True)
    me = lax.axis_index(axis_name)
    have = part[None]
    for stage in reversed(range(bits)):
        bit = (me >> stage) & 1
        pairs = [(i, i ^ (1 << stage)) for i in range(count)]
        got = lax.ppermute(have, axis_name, pairs)
        first = jnp.where(bit == 0, have, got)
        second = jnp.where(bit == 0, got, have)
        have = jnp.stack([first, second], axis=1).reshape((-1,) + part.shape)
    return have.reshape((count * part.shape[0],) + part.shape[1:])


def solution(mesh):
    in_specs = (
        P(("ctx", "head"), None),
        P(),
        P("ctx", None),
        P(),
        P(None, "head"),
        P("head"),
        P(None, "head"),
        P("head"),
        P(None, "head"),
        P("head"),
        P("head", None),
    )
    out_specs = P("ctx", "head")
    return jax.shard_map(local, mesh=mesh, in_specs=in_specs, out_specs=out_specs, check_vma=False)
```

```python
import math

import jax
import jax.numpy as jnp
from jax import lax
from jax.sharding import PartitionSpec as P

HEAD_SIZE = 128
PACKED_SLOTS = 256


rope_base = 1000000.0
norm_eps = 1e-06


def send_places(targets, owner_count, capacity, pack_len):
    is_filled = targets >= 0
    owner_ids = jnp.where(is_filled, targets // pack_len, -1)
    membership = (owner_ids[:, None] == jnp.arange(owner_count, dtype=jnp.int32)[None, :]).astype(
        jnp.int32
    )
    earlier = jnp.cumsum(membership, axis=0) - membership
    rank_in = jnp.sum(earlier * membership, axis=1)
    return jnp.where(is_filled, owner_ids * capacity + rank_in, owner_count * capacity)


def one_hot_rows(index, count):
    return (index[:, None] == jnp.arange(count, dtype=jnp.int32)[None, :]).astype(jnp.bfloat16)


def select_rows(index, values):
    picked = jnp.dot(
        one_hot_rows(index, values.shape[0]), values, preferred_element_type=jnp.float32
    )
    return picked.astype(values.dtype)


def apply_rotary(values, sequence_starts, head_dim):
    half_dim = head_dim // 2
    frequency = jnp.exp(
        jnp.arange(half_dim, dtype=jnp.float32) * (-2.0 * math.log(rope_base) / head_dim)
    )
    angles = sequence_starts.astype(jnp.float32)[:, None] * frequency[None, :]
    cosine = jnp.cos(angles)[:, None, :]
    sine_table = jnp.sin(angles)[:, None, :]
    first_half = values[..., :half_dim]
    second_half = values[..., half_dim:]
    return jnp.concatenate(
        [
            first_half * cosine - second_half * sine_table,
            second_half * cosine + first_half * sine_table,
        ],
        axis=-1,
    )


def local(
    x_pool,
    pool_dest,
    seq_len,
    norm_gain,
    w_query,
    q_bias,
    key_projection_weight,
    key_bias_vector,
    value_projection_weight,
    value_bias_vector,
    w_out,
):
    ctx_count = lax.axis_size("ctx")
    head_count = lax.axis_size("head")
    pool_rows = x_pool.shape[0]
    capacity = pool_rows // ctx_count
    group_rows = pool_rows * head_count
    group_cap = capacity * head_count
    pack_len = PACKED_SLOTS
    head_dim = HEAD_SIZE
    ctx_index = lax.axis_index("ctx")

    all_lengths = doubling_gather(seq_len, "ctx", ctx_count)
    near_x, far_x = split_gather(x_pool, "head", head_count)
    half_rows = near_x.shape[0]

    dest_grid = pool_dest.reshape(ctx_count, group_rows)
    my_dest = lax.dynamic_index_in_dim(dest_grid, ctx_index, 0, keepdims=False)
    upper = lax.axis_index("head") >= head_count - head_count // 2
    if far_x.shape[0]:
        to_work_order = lambda v: jnp.where(upper, jnp.roll(v, -half_rows), v)
    else:
        to_work_order = lambda v: v
    work_dest = to_work_order(my_dest)
    is_filled = work_dest >= 0
    owner = jnp.where(is_filled, work_dest // pack_len, 0)
    slot = jnp.where(is_filled, work_dest % pack_len, 0)
    seq_ends = jnp.cumsum(all_lengths, axis=1).astype(jnp.int32)
    row_ends = jnp.take(seq_ends, owner, axis=0)
    row_lengths = jnp.take(all_lengths, owner, axis=0)
    finished = (row_ends <= slot[:, None]).astype(jnp.int32)
    sequence_starts = slot - jnp.sum(finished * row_lengths, axis=1)

    local_heads = w_query.shape[1] // head_dim
    local_kv = key_projection_weight.shape[1] // head_dim
    query_group_count = local_heads // local_kv

    def project(rows_x, starts):
        count = rows_x.shape[0]
        values_wide = rows_x.astype(jnp.float32)
        normalized_input = (
            values_wide
            * lax.rsqrt(jnp.mean(values_wide * values_wide, axis=-1, keepdims=True) + norm_eps)
            * norm_gain
        ).astype(jnp.bfloat16)
        query_matrix = (
            jnp.dot(normalized_input, w_query, preferred_element_type=jnp.float32) + q_bias
        )
        query_matrix = apply_rotary(
            query_matrix.reshape(count, local_heads, head_dim), starts, head_dim
        ).astype(jnp.bfloat16)
        key_rows = (
            jnp.dot(normalized_input, key_projection_weight, preferred_element_type=jnp.float32)
            + key_bias_vector
        )
        key_rows = apply_rotary(
            key_rows.reshape(count, local_kv, head_dim), starts, head_dim
        ).astype(jnp.bfloat16)
        value_rows = (
            jnp.dot(normalized_input, value_projection_weight, preferred_element_type=jnp.float32)
            + value_bias_vector
        ).astype(jnp.bfloat16)
        return jnp.concatenate(
            [
                query_matrix.reshape(count, local_heads * head_dim),
                key_rows.reshape(count, local_kv * head_dim),
                value_rows,
            ],
            axis=1,
        )

    parts = [project(near_x, sequence_starts[:half_rows])]
    if far_x.shape[0]:
        parts.append(project(far_x, sequence_starts[half_rows:]))
    qkv = jnp.concatenate(parts, axis=0)

    places = to_work_order(send_places(my_dest, ctx_count, group_cap, pack_len))
    send_hot = (
        places[None, :] == jnp.arange(ctx_count * group_cap, dtype=jnp.int32)[:, None]
    ).astype(jnp.bfloat16)
    outgoing = jnp.dot(send_hot, qkv, preferred_element_type=jnp.float32).astype(jnp.bfloat16)
    arrived = lax.all_to_all(outgoing, "ctx", split_axis=0, concat_axis=0, tiled=True)

    mine = (pool_dest >= 0) & (pool_dest // pack_len == ctx_index)
    mine_grid = mine.reshape(ctx_count, group_rows).astype(jnp.int32)
    rank_in = jnp.cumsum(mine_grid, axis=1) - mine_grid
    arrived_index = (
        jnp.arange(ctx_count, dtype=jnp.int32)[:, None] * group_cap + rank_in
    ).reshape(-1)
    my_slot_of_row = jnp.where(mine, pool_dest - ctx_index * pack_len, -1)
    slot_ids = jnp.arange(pack_len, dtype=jnp.int32)
    names_slot = my_slot_of_row[None, :] == slot_ids[:, None]
    source_of_slot = jnp.sum(jnp.where(names_slot, arrived_index[None, :], 0), axis=1)
    packed_qkv = select_rows(source_of_slot, arrived)

    q_width = local_heads * head_dim
    kv_width = local_kv * head_dim
    query_matrix = packed_qkv[:, :q_width].reshape(pack_len, local_kv, query_group_count, head_dim)
    projected_key_rows = packed_qkv[:, q_width : q_width + kv_width].reshape(
        pack_len, local_kv, head_dim
    )
    projected_value_rows = packed_qkv[:, q_width + kv_width :].reshape(pack_len, local_kv, head_dim)

    own_lengths = seq_len[0]
    own_ends = jnp.cumsum(own_lengths).astype(jnp.int32)
    segment = jnp.sum((own_ends[None, :] <= slot_ids[:, None]).astype(jnp.int32), axis=1)

    score_scale = 1.0 / math.sqrt(head_dim)
    scores = (
        jnp.einsum(
            "qkgd,tkd->kgqt",
            query_matrix,
            projected_key_rows,
            preferred_element_type=jnp.float32,
        )
        * score_scale
    )
    allowed = (segment[:, None] == segment[None, :]) & (slot_ids[None, :] <= slot_ids[:, None])
    scores = jnp.where(allowed[None, None], scores, -1e30)
    row_max = jnp.max(scores, axis=-1, keepdims=True)
    weights = jnp.exp(scores - row_max)
    row_total = jnp.sum(weights, axis=-1, keepdims=True)
    probability = (weights / row_total).astype(jnp.bfloat16)
    mixed_heads = jnp.einsum(
        "kgqt,tkd->qkgd", probability, projected_value_rows, preferred_element_type=jnp.float32
    )
    mixed_heads = mixed_heads.astype(jnp.bfloat16).reshape(pack_len, local_heads * head_dim)
    partial_out = jnp.dot(mixed_heads, w_out, preferred_element_type=jnp.float32)
    return halving_scatter(partial_out, "head", head_count).astype(jnp.bfloat16)


def halving_scatter(partial, axis_name, count):
    bits = count.bit_length() - 1
    if count != 1 << bits or bits == 0:
        return lax.psum_scatter(partial, axis_name, scatter_dimension=1, tiled=True)
    block = partial.shape[1] // count
    me = lax.axis_index(axis_name)
    pieces = [(b, partial[:, b * block : (b + 1) * block]) for b in range(count)]
    for stage in range(bits):
        bit = (me >> stage) & 1
        lows = [(b, x) for b, x in pieces if not (b >> stage) & 1]
        highs = [x for b, x in pieces if (b >> stage) & 1]
        keep = [jnp.where(bit == 0, lo, hi) for (_, lo), hi in zip(lows, highs)]
        send = jnp.stack([jnp.where(bit == 0, hi, lo) for (_, lo), hi in zip(lows, highs)])
        pairs = [(i, i ^ (1 << stage)) for i in range(count)]
        got = lax.ppermute(send, axis_name, pairs)
        pieces = [(b, k + got[i]) for i, ((b, _), k) in enumerate(zip(lows, keep))]
    return pieces[0][1]


def doubling_gather(part, axis_name, count):
    bits = count.bit_length() - 1
    if count != 1 << bits or bits == 0:
        return lax.all_gather(part, axis_name, tiled=True)
    me = lax.axis_index(axis_name)
    have = part[None]
    for stage in reversed(range(bits)):
        bit = (me >> stage) & 1
        pairs = [(i, i ^ (1 << stage)) for i in range(count)]
        got = lax.ppermute(have, axis_name, pairs)
        first = jnp.where(bit == 0, have, got)
        second = jnp.where(bit == 0, got, have)
        have = jnp.stack([first, second], axis=1).reshape((-1,) + part.shape)
    return have.reshape((count * part.shape[0],) + part.shape[1:])


def split_gather(part, axis_name, count):
    if count == 1:
        return part, part[:0]
    half = count // 2
    if count % 2 or half & (half - 1):
        gathered = lax.all_gather(part, axis_name, tiled=True)
        return gathered, gathered[:0]
    me = lax.axis_index(axis_name)
    crossed = lax.ppermute(part, axis_name, [(i, (i + half) % count) for i in range(count)])
    if half == 1:
        return part, crossed
    near = doubling_gather_within(part, axis_name, half)
    far = doubling_gather_within(crossed, axis_name, half)
    return near, far


def doubling_gather_within(part, axis_name, span):
    bits = span.bit_length() - 1
    me = lax.axis_index(axis_name)
    count = lax.axis_size(axis_name)
    have = part[None]
    for stage in reversed(range(bits)):
        bit = (me >> stage) & 1
        pairs = [(i, i ^ (1 << stage)) for i in range(count)]
        got = lax.ppermute(have, axis_name, pairs)
        first = jnp.where(bit == 0, have, got)
        second = jnp.where(bit == 0, got, have)
        have = jnp.stack([first, second], axis=1).reshape((-1,) + part.shape)
    return have.reshape((span * part.shape[0],) + part.shape[1:])


def solution(mesh):
    in_specs = (
        P(("ctx", "head"), None),
        P(),
        P("ctx", None),
        P(),
        P(None, "head"),
        P("head"),
        P(None, "head"),
        P("head"),
        P(None, "head"),
        P("head"),
        P("head", None),
    )
    out_specs = P("ctx", "head")
    return jax.shard_map(local, mesh=mesh, in_specs=in_specs, out_specs=out_specs, check_vma=False)
```

```python
import math

import jax
import jax.numpy as jnp
from jax import lax
from jax.sharding import PartitionSpec as P

HEAD_SIZE = 128
PACKED_SLOTS = 256


rope_base = 1000000.0
norm_eps = 1e-06


def send_places(targets, owner_count, capacity, pack_len):
    is_filled = targets >= 0
    owner_ids = jnp.where(is_filled, targets // pack_len, -1)
    membership = (owner_ids[:, None] == jnp.arange(owner_count, dtype=jnp.int32)[None, :]).astype(
        jnp.int32
    )
    earlier = jnp.cumsum(membership, axis=0) - membership
    rank_in = jnp.sum(earlier * membership, axis=1)
    return jnp.where(is_filled, owner_ids * capacity + rank_in, owner_count * capacity)


def one_hot_rows(index, count):
    return (index[:, None] == jnp.arange(count, dtype=jnp.int32)[None, :]).astype(jnp.bfloat16)


def select_rows(index, values):
    picked = jnp.dot(
        one_hot_rows(index, values.shape[0]), values, preferred_element_type=jnp.float32
    )
    return picked.astype(values.dtype)


def apply_rotary(values, sequence_starts, head_dim):
    half_dim = head_dim // 2
    frequency = jnp.exp(
        jnp.arange(half_dim, dtype=jnp.float32) * (-2.0 * math.log(rope_base) / head_dim)
    )
    angles = sequence_starts.astype(jnp.float32)[:, None] * frequency[None, :]
    cosine = jnp.cos(angles)[:, None, :]
    sine_table = jnp.sin(angles)[:, None, :]
    first_half = values[..., :half_dim]
    second_half = values[..., half_dim:]
    return jnp.concatenate(
        [
            first_half * cosine - second_half * sine_table,
            second_half * cosine + first_half * sine_table,
        ],
        axis=-1,
    )


def local(
    x_pool,
    pool_dest,
    seq_len,
    norm_gain,
    w_query,
    q_bias,
    key_projection_weight,
    key_bias_vector,
    value_projection_weight,
    value_bias_vector,
    w_out,
):
    ctx_count = lax.axis_size("ctx")
    head_count = lax.axis_size("head")
    pool_rows = x_pool.shape[0]
    capacity = pool_rows // ctx_count
    group_rows = pool_rows * head_count
    group_cap = capacity * head_count
    pack_len = PACKED_SLOTS
    head_dim = HEAD_SIZE
    ctx_index = lax.axis_index("ctx")

    all_lengths = doubling_gather(seq_len, "ctx", ctx_count)
    near_x, crossed, finish_far = split_gather(x_pool, "head", head_count)
    half_rows = near_x.shape[0]

    dest_grid = pool_dest.reshape(ctx_count, group_rows)
    my_dest = lax.dynamic_index_in_dim(dest_grid, ctx_index, 0, keepdims=False)
    upper = lax.axis_index("head") >= head_count - head_count // 2
    if crossed.shape[0]:
        to_work_order = lambda v: jnp.where(upper, jnp.roll(v, -half_rows), v)
    else:
        to_work_order = lambda v: v
    work_dest = to_work_order(my_dest)
    is_filled = work_dest >= 0
    owner = jnp.where(is_filled, work_dest // pack_len, 0)
    slot = jnp.where(is_filled, work_dest % pack_len, 0)
    seq_ends = jnp.cumsum(all_lengths, axis=1).astype(jnp.int32)
    row_ends = jnp.take(seq_ends, owner, axis=0)
    row_lengths = jnp.take(all_lengths, owner, axis=0)
    finished = (row_ends <= slot[:, None]).astype(jnp.int32)
    sequence_starts = slot - jnp.sum(finished * row_lengths, axis=1)

    local_heads = w_query.shape[1] // head_dim
    local_kv = key_projection_weight.shape[1] // head_dim
    query_group_count = local_heads // local_kv

    def project(rows_x, starts):
        count = rows_x.shape[0]
        values_wide = rows_x.astype(jnp.float32)
        normalized_input = (
            values_wide
            * lax.rsqrt(jnp.mean(values_wide * values_wide, axis=-1, keepdims=True) + norm_eps)
            * norm_gain
        ).astype(jnp.bfloat16)
        query_matrix = (
            jnp.dot(normalized_input, w_query, preferred_element_type=jnp.float32) + q_bias
        )
        query_matrix = apply_rotary(
            query_matrix.reshape(count, local_heads, head_dim), starts, head_dim
        ).astype(jnp.bfloat16)
        key_rows = (
            jnp.dot(normalized_input, key_projection_weight, preferred_element_type=jnp.float32)
            + key_bias_vector
        )
        key_rows = apply_rotary(
            key_rows.reshape(count, local_kv, head_dim), starts, head_dim
        ).astype(jnp.bfloat16)
        value_rows = (
            jnp.dot(normalized_input, value_projection_weight, preferred_element_type=jnp.float32)
            + value_bias_vector
        ).astype(jnp.bfloat16)
        return jnp.concatenate(
            [
                query_matrix.reshape(count, local_heads * head_dim),
                key_rows.reshape(count, local_kv * head_dim),
                value_rows,
            ],
            axis=1,
        )

    halves = [(near_x, work_dest[:half_rows], sequence_starts[:half_rows])]
    if crossed.shape[0]:
        halves.append((crossed, work_dest[half_rows:], sequence_starts[half_rows:]))
    half_cap = group_cap // len(halves)
    arrivals = []
    for rows_x, rows_dest, starts in halves:
        if arrivals:
            rows_x, _ = lax.optimization_barrier((rows_x, outgoing))
            rows_x = finish_far(rows_x)
        part_qkv = project(rows_x, starts)
        places = send_places(rows_dest, ctx_count, half_cap, pack_len)
        send_hot = (
            places[None, :] == jnp.arange(ctx_count * half_cap, dtype=jnp.int32)[:, None]
        ).astype(jnp.bfloat16)
        outgoing = jnp.dot(send_hot, part_qkv, preferred_element_type=jnp.float32).astype(
            jnp.bfloat16
        )
        arrivals.append(lax.all_to_all(outgoing, "ctx", split_axis=0, concat_axis=0, tiled=True))
    arrived = jnp.concatenate(arrivals, axis=0)

    mine = (pool_dest >= 0) & (pool_dest // pack_len == ctx_index)
    row_head = (jnp.arange(pool_dest.shape[0], dtype=jnp.int32) // pool_rows) % head_count
    in_near = (row_head >= head_count - head_count // 2) == upper
    if len(halves) == 1:
        in_near = jnp.ones_like(in_near)
    group_base = jnp.arange(ctx_count, dtype=jnp.int32)[:, None] * half_cap
    arrived_index = 0
    for k, member in enumerate([in_near, ~in_near][: len(halves)]):
        taken = (mine & member).reshape(ctx_count, group_rows).astype(jnp.int32)
        rank_in = jnp.cumsum(taken, axis=1) - taken
        arrived_index = arrived_index + taken * (k * ctx_count * half_cap + group_base + rank_in)
    arrived_index = arrived_index.reshape(-1)
    my_slot_of_row = jnp.where(mine, pool_dest - ctx_index * pack_len, -1)
    slot_ids = jnp.arange(pack_len, dtype=jnp.int32)
    names_slot = my_slot_of_row[None, :] == slot_ids[:, None]
    source_of_slot = jnp.sum(jnp.where(names_slot, arrived_index[None, :], 0), axis=1)
    packed_qkv = select_rows(source_of_slot, arrived)

    q_width = local_heads * head_dim
    kv_width = local_kv * head_dim
    query_matrix = packed_qkv[:, :q_width].reshape(pack_len, local_kv, query_group_count, head_dim)
    projected_key_rows = packed_qkv[:, q_width : q_width + kv_width].reshape(
        pack_len, local_kv, head_dim
    )
    projected_value_rows = packed_qkv[:, q_width + kv_width :].reshape(pack_len, local_kv, head_dim)

    own_lengths = seq_len[0]
    own_ends = jnp.cumsum(own_lengths).astype(jnp.int32)
    segment = jnp.sum((own_ends[None, :] <= slot_ids[:, None]).astype(jnp.int32), axis=1)

    score_scale = 1.0 / math.sqrt(head_dim)
    scores = (
        jnp.einsum(
            "qkgd,tkd->kgqt",
            query_matrix,
            projected_key_rows,
            preferred_element_type=jnp.float32,
        )
        * score_scale
    )
    allowed = (segment[:, None] == segment[None, :]) & (slot_ids[None, :] <= slot_ids[:, None])
    scores = jnp.where(allowed[None, None], scores, -1e30)
    row_max = jnp.max(scores, axis=-1, keepdims=True)
    weights = jnp.exp(scores - row_max)
    row_total = jnp.sum(weights, axis=-1, keepdims=True)
    probability = (weights / row_total).astype(jnp.bfloat16)
    mixed_heads = jnp.einsum(
        "kgqt,tkd->qkgd", probability, projected_value_rows, preferred_element_type=jnp.float32
    )
    mixed_heads = mixed_heads.astype(jnp.bfloat16).reshape(pack_len, local_heads * head_dim)
    partial_out = jnp.dot(mixed_heads, w_out, preferred_element_type=jnp.float32)
    return halving_scatter(partial_out, "head", head_count).astype(jnp.bfloat16)


def halving_scatter(partial, axis_name, count):
    bits = count.bit_length() - 1
    if count != 1 << bits or bits == 0:
        return lax.psum_scatter(partial, axis_name, scatter_dimension=1, tiled=True)
    block = partial.shape[1] // count
    me = lax.axis_index(axis_name)
    pieces = [(b, partial[:, b * block : (b + 1) * block]) for b in range(count)]
    for stage in range(bits):
        bit = (me >> stage) & 1
        lows = [(b, x) for b, x in pieces if not (b >> stage) & 1]
        highs = [x for b, x in pieces if (b >> stage) & 1]
        keep = [jnp.where(bit == 0, lo, hi) for (_, lo), hi in zip(lows, highs)]
        send = jnp.stack([jnp.where(bit == 0, hi, lo) for (_, lo), hi in zip(lows, highs)])
        pairs = [(i, i ^ (1 << stage)) for i in range(count)]
        got = lax.ppermute(send, axis_name, pairs)
        pieces = [(b, k + got[i]) for i, ((b, _), k) in enumerate(zip(lows, keep))]
    return pieces[0][1]


def doubling_gather(part, axis_name, count):
    bits = count.bit_length() - 1
    if count != 1 << bits or bits == 0:
        return lax.all_gather(part, axis_name, tiled=True)
    me = lax.axis_index(axis_name)
    have = part[None]
    for stage in reversed(range(bits)):
        bit = (me >> stage) & 1
        pairs = [(i, i ^ (1 << stage)) for i in range(count)]
        got = lax.ppermute(have, axis_name, pairs)
        first = jnp.where(bit == 0, have, got)
        second = jnp.where(bit == 0, got, have)
        have = jnp.stack([first, second], axis=1).reshape((-1,) + part.shape)
    return have.reshape((count * part.shape[0],) + part.shape[1:])


def split_gather(part, axis_name, count):
    if count == 1:
        return part, part[:0], lambda v: v
    half = count // 2
    if count % 2 or half & (half - 1):
        gathered = lax.all_gather(part, axis_name, tiled=True)
        return gathered, gathered[:0], lambda v: v
    crossed = lax.ppermute(part, axis_name, [(i, (i + half) % count) for i in range(count)])
    if half == 1:
        return part, crossed, lambda v: v
    near = doubling_gather_within(part, axis_name, half)
    return near, crossed, lambda v: doubling_gather_within(v, axis_name, half)


def doubling_gather_within(part, axis_name, span):
    bits = span.bit_length() - 1
    me = lax.axis_index(axis_name)
    count = lax.axis_size(axis_name)
    have = part[None]
    for stage in reversed(range(bits)):
        bit = (me >> stage) & 1
        pairs = [(i, i ^ (1 << stage)) for i in range(count)]
        got = lax.ppermute(have, axis_name, pairs)
        first = jnp.where(bit == 0, have, got)
        second = jnp.where(bit == 0, got, have)
        have = jnp.stack([first, second], axis=1).reshape((-1,) + part.shape)
    return have.reshape((span * part.shape[0],) + part.shape[1:])


def solution(mesh):
    in_specs = (
        P(("ctx", "head"), None),
        P(),
        P("ctx", None),
        P(),
        P(None, "head"),
        P("head"),
        P(None, "head"),
        P("head"),
        P(None, "head"),
        P("head"),
        P("head", None),
    )
    out_specs = P("ctx", "head")
    return jax.shard_map(local, mesh=mesh, in_specs=in_specs, out_specs=out_specs, check_vma=False)
```

```python
import math

import jax
import jax.numpy as jnp
from jax import lax
from jax.sharding import PartitionSpec as P

HEAD_SIZE = 128
PACKED_SLOTS = 256


rope_base = 1000000.0
norm_eps = 1e-06


def send_places(targets, owner_count, capacity, pack_len):
    is_filled = targets >= 0
    owner_ids = jnp.where(is_filled, targets // pack_len, -1)
    membership = (owner_ids[:, None] == jnp.arange(owner_count, dtype=jnp.int32)[None, :]).astype(
        jnp.int32
    )
    earlier = jnp.cumsum(membership, axis=0) - membership
    rank_in = jnp.sum(earlier * membership, axis=1)
    return jnp.where(is_filled, owner_ids * capacity + rank_in, owner_count * capacity)


def one_hot_rows(index, count):
    return (index[:, None] == jnp.arange(count, dtype=jnp.int32)[None, :]).astype(jnp.bfloat16)


def select_rows(index, values):
    picked = jnp.dot(
        one_hot_rows(index, values.shape[0]), values, preferred_element_type=jnp.float32
    )
    return picked.astype(values.dtype)


def apply_rotary(values, sequence_starts, head_dim):
    half_dim = head_dim // 2
    frequency = jnp.exp(
        jnp.arange(half_dim, dtype=jnp.float32) * (-2.0 * math.log(rope_base) / head_dim)
    )
    angles = sequence_starts.astype(jnp.float32)[:, None] * frequency[None, :]
    cosine = jnp.cos(angles)[:, None, :]
    sine_table = jnp.sin(angles)[:, None, :]
    first_half = values[..., :half_dim]
    second_half = values[..., half_dim:]
    return jnp.concatenate(
        [
            first_half * cosine - second_half * sine_table,
            second_half * cosine + first_half * sine_table,
        ],
        axis=-1,
    )


def local(
    x_pool,
    pool_dest,
    seq_len,
    norm_gain,
    w_query,
    q_bias,
    key_projection_weight,
    key_bias_vector,
    value_projection_weight,
    value_bias_vector,
    w_out,
):
    ctx_count = lax.axis_size("ctx")
    head_count = lax.axis_size("head")
    pool_rows = x_pool.shape[0]
    capacity = pool_rows // ctx_count
    group_rows = pool_rows * head_count
    group_cap = capacity * head_count
    pack_len = PACKED_SLOTS
    head_dim = HEAD_SIZE
    ctx_index = lax.axis_index("ctx")

    all_lengths = doubling_gather(seq_len, "ctx", ctx_count)
    near_x, far_x = split_gather(x_pool, "head", head_count)
    half_rows = near_x.shape[0]

    dest_grid = pool_dest.reshape(ctx_count, group_rows)
    my_dest = lax.dynamic_index_in_dim(dest_grid, ctx_index, 0, keepdims=False)
    upper = lax.axis_index("head") >= head_count - head_count // 2
    if far_x.shape[0]:
        to_work_order = lambda v: jnp.where(upper, jnp.roll(v, -half_rows), v)
    else:
        to_work_order = lambda v: v
    work_dest = to_work_order(my_dest)
    is_filled = work_dest >= 0
    owner = jnp.where(is_filled, work_dest // pack_len, 0)
    slot = jnp.where(is_filled, work_dest % pack_len, 0)
    seq_ends = jnp.cumsum(all_lengths, axis=1).astype(jnp.int32)
    row_ends = jnp.take(seq_ends, owner, axis=0)
    row_lengths = jnp.take(all_lengths, owner, axis=0)
    finished = (row_ends <= slot[:, None]).astype(jnp.int32)
    sequence_starts = slot - jnp.sum(finished * row_lengths, axis=1)

    local_heads = w_query.shape[1] // head_dim
    local_kv = key_projection_weight.shape[1] // head_dim
    query_group_count = local_heads // local_kv

    def project(rows_x, starts):
        count = rows_x.shape[0]
        values_wide = rows_x.astype(jnp.float32)
        normalized_input = (
            values_wide
            * lax.rsqrt(jnp.mean(values_wide * values_wide, axis=-1, keepdims=True) + norm_eps)
            * norm_gain
        ).astype(jnp.bfloat16)
        query_matrix = (
            jnp.dot(normalized_input, w_query, preferred_element_type=jnp.float32) + q_bias
        )
        query_matrix = apply_rotary(
            query_matrix.reshape(count, local_heads, head_dim), starts, head_dim
        ).astype(jnp.bfloat16)
        key_rows = (
            jnp.dot(normalized_input, key_projection_weight, preferred_element_type=jnp.float32)
            + key_bias_vector
        )
        key_rows = apply_rotary(
            key_rows.reshape(count, local_kv, head_dim), starts, head_dim
        ).astype(jnp.bfloat16)
        value_rows = (
            jnp.dot(normalized_input, value_projection_weight, preferred_element_type=jnp.float32)
            + value_bias_vector
        ).astype(jnp.bfloat16)
        return jnp.concatenate(
            [
                query_matrix.reshape(count, local_heads * head_dim),
                key_rows.reshape(count, local_kv * head_dim),
                value_rows,
            ],
            axis=1,
        )

    parts = [project(near_x, sequence_starts[:half_rows])]
    if far_x.shape[0]:
        parts.append(project(far_x, sequence_starts[half_rows:]))
    qkv = jnp.concatenate(parts, axis=0)

    places = to_work_order(send_places(my_dest, ctx_count, group_cap, pack_len))
    send_hot = (
        places[None, :] == jnp.arange(ctx_count * group_cap, dtype=jnp.int32)[:, None]
    ).astype(jnp.bfloat16)
    outgoing = jnp.dot(send_hot, qkv, preferred_element_type=jnp.float32).astype(jnp.bfloat16)
    arrived = lax.all_to_all(outgoing, "ctx", split_axis=0, concat_axis=0, tiled=True)

    mine = (pool_dest >= 0) & (pool_dest // pack_len == ctx_index)
    mine_grid = mine.reshape(ctx_count, group_rows).astype(jnp.int32)
    rank_in = jnp.cumsum(mine_grid, axis=1) - mine_grid
    arrived_index = (
        jnp.arange(ctx_count, dtype=jnp.int32)[:, None] * group_cap + rank_in
    ).reshape(-1)
    my_slot_of_row = jnp.where(mine, pool_dest - ctx_index * pack_len, -1)
    slot_ids = jnp.arange(pack_len, dtype=jnp.int32)
    names_slot = my_slot_of_row[None, :] == slot_ids[:, None]
    source_of_slot = jnp.sum(jnp.where(names_slot, arrived_index[None, :], 0), axis=1)
    packed_qkv = select_rows(source_of_slot, arrived)

    q_width = local_heads * head_dim
    kv_width = local_kv * head_dim
    query_matrix = packed_qkv[:, :q_width].reshape(pack_len, local_kv, query_group_count, head_dim)
    projected_key_rows = packed_qkv[:, q_width : q_width + kv_width].reshape(
        pack_len, local_kv, head_dim
    )
    projected_value_rows = packed_qkv[:, q_width + kv_width :].reshape(pack_len, local_kv, head_dim)

    own_lengths = seq_len[0]
    own_ends = jnp.cumsum(own_lengths).astype(jnp.int32)
    segment = jnp.sum((own_ends[None, :] <= slot_ids[:, None]).astype(jnp.int32), axis=1)

    score_scale = 1.0 / math.sqrt(head_dim)
    chunk_count = 2 if pack_len % 16 == 0 else 1
    chunk_len = pack_len // chunk_count
    results = []
    for chunk in range(chunk_count):
        lo, hi = chunk * chunk_len, (chunk + 1) * chunk_len
        scores = (
            jnp.einsum(
                "qkgd,tkd->kgqt",
                query_matrix[lo:hi],
                projected_key_rows[:hi],
                preferred_element_type=jnp.float32,
            )
            * score_scale
        )
        allowed = (segment[lo:hi, None] == segment[None, :hi]) & (
            slot_ids[None, :hi] <= slot_ids[lo:hi, None]
        )
        scores = jnp.where(allowed[None, None], scores, -1e30)
        row_max = jnp.max(scores, axis=-1, keepdims=True)
        weights = jnp.exp(scores - row_max)
        row_total = jnp.sum(weights, axis=-1, keepdims=True)
        probability = (weights / row_total).astype(jnp.bfloat16)
        mixed_heads = jnp.einsum(
            "kgqt,tkd->qkgd",
            probability,
            projected_value_rows[:hi],
            preferred_element_type=jnp.float32,
        )
        mixed_heads = mixed_heads.astype(jnp.bfloat16).reshape(chunk_len, local_heads * head_dim)
        partial_out = jnp.dot(mixed_heads, w_out, preferred_element_type=jnp.float32)
        results.append(halving_scatter(partial_out, "head", head_count).astype(jnp.bfloat16))
    return jnp.concatenate(results, axis=0)


def halving_scatter(partial, axis_name, count):
    bits = count.bit_length() - 1
    if count != 1 << bits or bits == 0:
        return lax.psum_scatter(partial, axis_name, scatter_dimension=1, tiled=True)
    block = partial.shape[1] // count
    me = lax.axis_index(axis_name)
    pieces = [(b, partial[:, b * block : (b + 1) * block]) for b in range(count)]
    for stage in range(bits):
        bit = (me >> stage) & 1
        lows = [(b, x) for b, x in pieces if not (b >> stage) & 1]
        highs = [x for b, x in pieces if (b >> stage) & 1]
        keep = [jnp.where(bit == 0, lo, hi) for (_, lo), hi in zip(lows, highs)]
        send = jnp.stack([jnp.where(bit == 0, hi, lo) for (_, lo), hi in zip(lows, highs)])
        pairs = [(i, i ^ (1 << stage)) for i in range(count)]
        got = lax.ppermute(send, axis_name, pairs)
        pieces = [(b, k + got[i]) for i, ((b, _), k) in enumerate(zip(lows, keep))]
    return pieces[0][1]


def doubling_gather(part, axis_name, count):
    bits = count.bit_length() - 1
    if count != 1 << bits or bits == 0:
        return lax.all_gather(part, axis_name, tiled=True)
    me = lax.axis_index(axis_name)
    have = part[None]
    for stage in reversed(range(bits)):
        bit = (me >> stage) & 1
        pairs = [(i, i ^ (1 << stage)) for i in range(count)]
        got = lax.ppermute(have, axis_name, pairs)
        first = jnp.where(bit == 0, have, got)
        second = jnp.where(bit == 0, got, have)
        have = jnp.stack([first, second], axis=1).reshape((-1,) + part.shape)
    return have.reshape((count * part.shape[0],) + part.shape[1:])


def split_gather(part, axis_name, count):
    if count == 1:
        return part, part[:0]
    half = count // 2
    if count % 2 or half & (half - 1):
        gathered = lax.all_gather(part, axis_name, tiled=True)
        return gathered, gathered[:0]
    me = lax.axis_index(axis_name)
    crossed = lax.ppermute(part, axis_name, [(i, (i + half) % count) for i in range(count)])
    if half == 1:
        return part, crossed
    near = doubling_gather_within(part, axis_name, half)
    far = doubling_gather_within(crossed, axis_name, half)
    return near, far


def doubling_gather_within(part, axis_name, span):
    bits = span.bit_length() - 1
    me = lax.axis_index(axis_name)
    count = lax.axis_size(axis_name)
    have = part[None]
    for stage in reversed(range(bits)):
        bit = (me >> stage) & 1
        pairs = [(i, i ^ (1 << stage)) for i in range(count)]
        got = lax.ppermute(have, axis_name, pairs)
        first = jnp.where(bit == 0, have, got)
        second = jnp.where(bit == 0, got, have)
        have = jnp.stack([first, second], axis=1).reshape((-1,) + part.shape)
    return have.reshape((span * part.shape[0],) + part.shape[1:])


def solution(mesh):
    in_specs = (
        P(("ctx", "head"), None),
        P(),
        P("ctx", None),
        P(),
        P(None, "head"),
        P("head"),
        P(None, "head"),
        P("head"),
        P(None, "head"),
        P("head"),
        P("head", None),
    )
    out_specs = P("ctx", "head")
    return jax.shard_map(local, mesh=mesh, in_specs=in_specs, out_specs=out_specs, check_vma=False)
```

```python
import math

import jax
import jax.numpy as jnp
from jax import lax
from jax.sharding import PartitionSpec as P

HEAD_SIZE = 128
PACKED_SLOTS = 256


rope_base = 1000000.0
norm_eps = 1e-06


def send_places(targets, owner_count, capacity, pack_len):
    is_filled = targets >= 0
    owner_ids = jnp.where(is_filled, targets // pack_len, -1)
    membership = (owner_ids[:, None] == jnp.arange(owner_count, dtype=jnp.int32)[None, :]).astype(
        jnp.int32
    )
    earlier = jnp.cumsum(membership, axis=0) - membership
    rank_in = jnp.sum(earlier * membership, axis=1)
    return jnp.where(is_filled, owner_ids * capacity + rank_in, owner_count * capacity)


def one_hot_rows(index, count):
    return (index[:, None] == jnp.arange(count, dtype=jnp.int32)[None, :]).astype(jnp.bfloat16)


def select_rows(index, values):
    picked = jnp.dot(
        one_hot_rows(index, values.shape[0]), values, preferred_element_type=jnp.float32
    )
    return picked.astype(values.dtype)


def apply_rotary(values, sequence_starts, head_dim):
    half_dim = head_dim // 2
    frequency = jnp.exp(
        jnp.arange(half_dim, dtype=jnp.float32) * (-2.0 * math.log(rope_base) / head_dim)
    )
    angles = sequence_starts.astype(jnp.float32)[:, None] * frequency[None, :]
    cosine = jnp.cos(angles)[:, None, :]
    sine_table = jnp.sin(angles)[:, None, :]
    first_half = values[..., :half_dim]
    second_half = values[..., half_dim:]
    return jnp.concatenate(
        [
            first_half * cosine - second_half * sine_table,
            second_half * cosine + first_half * sine_table,
        ],
        axis=-1,
    )


def local(
    x_pool,
    pool_dest,
    seq_len,
    norm_gain,
    w_query,
    q_bias,
    key_projection_weight,
    key_bias_vector,
    value_projection_weight,
    value_bias_vector,
    w_out,
):
    ctx_count = lax.axis_size("ctx")
    head_count = lax.axis_size("head")
    pool_rows = x_pool.shape[0]
    capacity = pool_rows // ctx_count
    group_rows = pool_rows * head_count
    group_cap = capacity * head_count
    pack_len = PACKED_SLOTS
    head_dim = HEAD_SIZE
    ctx_index = lax.axis_index("ctx")

    all_lengths = doubling_gather(seq_len, "ctx", ctx_count)
    near_x, far_x = split_gather(x_pool, "head", head_count)
    half_rows = near_x.shape[0]

    dest_grid = pool_dest.reshape(ctx_count, group_rows)
    my_dest = lax.dynamic_index_in_dim(dest_grid, ctx_index, 0, keepdims=False)
    upper = lax.axis_index("head") >= head_count - head_count // 2
    if far_x.shape[0]:
        to_work_order = lambda v: jnp.where(upper, jnp.roll(v, -half_rows), v)
    else:
        to_work_order = lambda v: v
    work_dest = to_work_order(my_dest)
    is_filled = work_dest >= 0
    owner = jnp.where(is_filled, work_dest // pack_len, 0)
    slot = jnp.where(is_filled, work_dest % pack_len, 0)
    seq_ends = jnp.cumsum(all_lengths, axis=1).astype(jnp.int32)
    row_ends = jnp.take(seq_ends, owner, axis=0)
    row_lengths = jnp.take(all_lengths, owner, axis=0)
    finished = (row_ends <= slot[:, None]).astype(jnp.int32)
    sequence_starts = slot - jnp.sum(finished * row_lengths, axis=1)

    local_heads = w_query.shape[1] // head_dim
    local_kv = key_projection_weight.shape[1] // head_dim
    query_group_count = local_heads // local_kv

    def project(rows_x, starts):
        count = rows_x.shape[0]
        values_wide = rows_x.astype(jnp.float32)
        normalized_input = (
            values_wide
            * lax.rsqrt(jnp.mean(values_wide * values_wide, axis=-1, keepdims=True) + norm_eps)
            * norm_gain
        ).astype(jnp.bfloat16)
        query_matrix = (
            jnp.dot(normalized_input, w_query, preferred_element_type=jnp.float32) + q_bias
        )
        query_matrix = apply_rotary(
            query_matrix.reshape(count, local_heads, head_dim), starts, head_dim
        ).astype(jnp.bfloat16)
        key_rows = (
            jnp.dot(normalized_input, key_projection_weight, preferred_element_type=jnp.float32)
            + key_bias_vector
        )
        key_rows = apply_rotary(
            key_rows.reshape(count, local_kv, head_dim), starts, head_dim
        ).astype(jnp.bfloat16)
        value_rows = (
            jnp.dot(normalized_input, value_projection_weight, preferred_element_type=jnp.float32)
            + value_bias_vector
        ).astype(jnp.bfloat16)
        return jnp.concatenate(
            [
                query_matrix.reshape(count, local_heads * head_dim),
                key_rows.reshape(count, local_kv * head_dim),
                value_rows,
            ],
            axis=1,
        )

    parts = [project(near_x, sequence_starts[:half_rows])]
    if far_x.shape[0]:
        parts.append(project(far_x, sequence_starts[half_rows:]))
    qkv = jnp.concatenate(parts, axis=0)

    places = to_work_order(send_places(my_dest, ctx_count, group_cap, pack_len))
    send_hot = (
        places[None, :] == jnp.arange(ctx_count * group_cap, dtype=jnp.int32)[:, None]
    ).astype(jnp.bfloat16)
    outgoing = jnp.dot(send_hot, qkv, preferred_element_type=jnp.float32).astype(jnp.bfloat16)
    arrived = exchange(outgoing, "ctx", ctx_count)

    mine = (pool_dest >= 0) & (pool_dest // pack_len == ctx_index)
    mine_grid = mine.reshape(ctx_count, group_rows).astype(jnp.int32)
    rank_in = jnp.cumsum(mine_grid, axis=1) - mine_grid
    arrived_index = (
        jnp.arange(ctx_count, dtype=jnp.int32)[:, None] * group_cap + rank_in
    ).reshape(-1)
    my_slot_of_row = jnp.where(mine, pool_dest - ctx_index * pack_len, -1)
    slot_ids = jnp.arange(pack_len, dtype=jnp.int32)
    names_slot = my_slot_of_row[None, :] == slot_ids[:, None]
    source_of_slot = jnp.sum(jnp.where(names_slot, arrived_index[None, :], 0), axis=1)
    packed_qkv = select_rows(source_of_slot, arrived)

    q_width = local_heads * head_dim
    kv_width = local_kv * head_dim
    query_matrix = packed_qkv[:, :q_width].reshape(pack_len, local_kv, query_group_count, head_dim)
    projected_key_rows = packed_qkv[:, q_width : q_width + kv_width].reshape(
        pack_len, local_kv, head_dim
    )
    projected_value_rows = packed_qkv[:, q_width + kv_width :].reshape(pack_len, local_kv, head_dim)

    own_lengths = seq_len[0]
    own_ends = jnp.cumsum(own_lengths).astype(jnp.int32)
    segment = jnp.sum((own_ends[None, :] <= slot_ids[:, None]).astype(jnp.int32), axis=1)

    score_scale = 1.0 / math.sqrt(head_dim)
    chunk_count = 2 if pack_len % 16 == 0 else 1
    chunk_len = pack_len // chunk_count
    results = []
    for chunk in range(chunk_count):
        lo, hi = chunk * chunk_len, (chunk + 1) * chunk_len
        scores = (
            jnp.einsum(
                "qkgd,tkd->kgqt",
                query_matrix[lo:hi],
                projected_key_rows[:hi],
                preferred_element_type=jnp.float32,
            )
            * score_scale
        )
        allowed = (segment[lo:hi, None] == segment[None, :hi]) & (
            slot_ids[None, :hi] <= slot_ids[lo:hi, None]
        )
        scores = jnp.where(allowed[None, None], scores, -1e30)
        row_max = jnp.max(scores, axis=-1, keepdims=True)
        weights = jnp.exp(scores - row_max)
        row_total = jnp.sum(weights, axis=-1, keepdims=True)
        probability = (weights / row_total).astype(jnp.bfloat16)
        mixed_heads = jnp.einsum(
            "kgqt,tkd->qkgd",
            probability,
            projected_value_rows[:hi],
            preferred_element_type=jnp.float32,
        )
        mixed_heads = mixed_heads.astype(jnp.bfloat16).reshape(chunk_len, local_heads * head_dim)
        partial_out = jnp.dot(mixed_heads, w_out, preferred_element_type=jnp.float32)
        results.append(halving_scatter(partial_out, "head", head_count).astype(jnp.bfloat16))
    return jnp.concatenate(results, axis=0)


def exchange(outgoing, axis_name, count):
    if count > 8:
        return lax.all_to_all(outgoing, axis_name, split_axis=0, concat_axis=0, tiled=True)
    me = lax.axis_index(axis_name)
    chunks = outgoing.reshape((count, -1) + outgoing.shape[1:])
    by_shift = jnp.take(chunks, (me + jnp.arange(count)) % count, axis=0)
    from_shift = [by_shift[0]]
    for shift in range(1, count):
        pairs = [(i, (i + shift) % count) for i in range(count)]
        from_shift.append(lax.ppermute(by_shift[shift], axis_name, pairs))
    from_shift = jnp.stack(from_shift)
    arrived = jnp.take(from_shift, (me - jnp.arange(count)) % count, axis=0)
    return arrived.reshape(outgoing.shape)


def halving_scatter(partial, axis_name, count):
    bits = count.bit_length() - 1
    if count != 1 << bits or bits == 0:
        return lax.psum_scatter(partial, axis_name, scatter_dimension=1, tiled=True)
    block = partial.shape[1] // count
    me = lax.axis_index(axis_name)
    pieces = [(b, partial[:, b * block : (b + 1) * block]) for b in range(count)]
    for stage in range(bits):
        bit = (me >> stage) & 1
        lows = [(b, x) for b, x in pieces if not (b >> stage) & 1]
        highs = [x for b, x in pieces if (b >> stage) & 1]
        keep = [jnp.where(bit == 0, lo, hi) for (_, lo), hi in zip(lows, highs)]
        send = jnp.stack([jnp.where(bit == 0, hi, lo) for (_, lo), hi in zip(lows, highs)])
        pairs = [(i, i ^ (1 << stage)) for i in range(count)]
        got = lax.ppermute(send, axis_name, pairs)
        pieces = [(b, k + got[i]) for i, ((b, _), k) in enumerate(zip(lows, keep))]
    return pieces[0][1]


def doubling_gather(part, axis_name, count):
    bits = count.bit_length() - 1
    if count != 1 << bits or bits == 0:
        return lax.all_gather(part, axis_name, tiled=True)
    me = lax.axis_index(axis_name)
    have = part[None]
    for stage in reversed(range(bits)):
        bit = (me >> stage) & 1
        pairs = [(i, i ^ (1 << stage)) for i in range(count)]
        got = lax.ppermute(have, axis_name, pairs)
        first = jnp.where(bit == 0, have, got)
        second = jnp.where(bit == 0, got, have)
        have = jnp.stack([first, second], axis=1).reshape((-1,) + part.shape)
    return have.reshape((count * part.shape[0],) + part.shape[1:])


def split_gather(part, axis_name, count):
    if count == 1:
        return part, part[:0]
    half = count // 2
    if count % 2 or half & (half - 1):
        gathered = lax.all_gather(part, axis_name, tiled=True)
        return gathered, gathered[:0]
    me = lax.axis_index(axis_name)
    crossed = lax.ppermute(part, axis_name, [(i, (i + half) % count) for i in range(count)])
    if half == 1:
        return part, crossed
    near = doubling_gather_within(part, axis_name, half)
    far = doubling_gather_within(crossed, axis_name, half)
    return near, far


def doubling_gather_within(part, axis_name, span):
    bits = span.bit_length() - 1
    me = lax.axis_index(axis_name)
    count = lax.axis_size(axis_name)
    have = part[None]
    for stage in reversed(range(bits)):
        bit = (me >> stage) & 1
        pairs = [(i, i ^ (1 << stage)) for i in range(count)]
        got = lax.ppermute(have, axis_name, pairs)
        first = jnp.where(bit == 0, have, got)
        second = jnp.where(bit == 0, got, have)
        have = jnp.stack([first, second], axis=1).reshape((-1,) + part.shape)
    return have.reshape((span * part.shape[0],) + part.shape[1:])


def solution(mesh):
    in_specs = (
        P(("ctx", "head"), None),
        P(),
        P("ctx", None),
        P(),
        P(None, "head"),
        P("head"),
        P(None, "head"),
        P("head"),
        P(None, "head"),
        P("head"),
        P("head", None),
    )
    out_specs = P("ctx", "head")
    return jax.shard_map(local, mesh=mesh, in_specs=in_specs, out_specs=out_specs, check_vma=False)
```

```python
import math

import jax
import jax.numpy as jnp
from jax import lax
from jax.sharding import PartitionSpec as P

HEAD_SIZE = 128
PACKED_SLOTS = 256


rope_base = 1000000.0
norm_eps = 1e-06


def send_places(targets, owner_count, capacity, pack_len):
    is_filled = targets >= 0
    owner_ids = jnp.where(is_filled, targets // pack_len, -1)
    membership = (owner_ids[:, None] == jnp.arange(owner_count, dtype=jnp.int32)[None, :]).astype(
        jnp.int32
    )
    earlier = jnp.cumsum(membership, axis=0) - membership
    rank_in = jnp.sum(earlier * membership, axis=1)
    return jnp.where(is_filled, owner_ids * capacity + rank_in, owner_count * capacity)


def one_hot_rows(index, count):
    return (index[:, None] == jnp.arange(count, dtype=jnp.int32)[None, :]).astype(jnp.bfloat16)


def select_rows(index, values):
    picked = jnp.dot(
        one_hot_rows(index, values.shape[0]), values, preferred_element_type=jnp.float32
    )
    return picked.astype(values.dtype)


def apply_rotary(values, sequence_starts, head_dim):
    half_dim = head_dim // 2
    frequency = jnp.exp(
        jnp.arange(half_dim, dtype=jnp.float32) * (-2.0 * math.log(rope_base) / head_dim)
    )
    angles = sequence_starts.astype(jnp.float32)[:, None] * frequency[None, :]
    cosine = jnp.cos(angles)[:, None, :]
    sine_table = jnp.sin(angles)[:, None, :]
    first_half = values[..., :half_dim]
    second_half = values[..., half_dim:]
    return jnp.concatenate(
        [
            first_half * cosine - second_half * sine_table,
            second_half * cosine + first_half * sine_table,
        ],
        axis=-1,
    )


def local(
    x_pool,
    pool_dest,
    seq_len,
    norm_gain,
    w_query,
    q_bias,
    key_projection_weight,
    key_bias_vector,
    value_projection_weight,
    value_bias_vector,
    w_out,
):
    ctx_count = lax.axis_size("ctx")
    head_count = lax.axis_size("head")
    pool_rows = x_pool.shape[0]
    capacity = pool_rows // ctx_count
    group_rows = pool_rows * head_count
    group_cap = capacity * head_count
    pack_len = PACKED_SLOTS
    head_dim = HEAD_SIZE
    ctx_index = lax.axis_index("ctx")

    all_lengths = doubling_gather(seq_len, "ctx", ctx_count)
    pieces, work_heads = xor_gather(x_pool, "head", head_count)

    dest_grid = pool_dest.reshape(ctx_count, group_rows)
    my_dest = lax.dynamic_index_in_dim(dest_grid, ctx_index, 0, keepdims=False)
    to_work_order = lambda v: jnp.take(
        v.reshape(head_count, pool_rows), work_heads, axis=0
    ).reshape(-1)
    work_dest = to_work_order(my_dest)
    is_filled = work_dest >= 0
    owner = jnp.where(is_filled, work_dest // pack_len, 0)
    slot = jnp.where(is_filled, work_dest % pack_len, 0)
    seq_ends = jnp.cumsum(all_lengths, axis=1).astype(jnp.int32)
    row_ends = jnp.take(seq_ends, owner, axis=0)
    row_lengths = jnp.take(all_lengths, owner, axis=0)
    finished = (row_ends <= slot[:, None]).astype(jnp.int32)
    sequence_starts = slot - jnp.sum(finished * row_lengths, axis=1)

    local_heads = w_query.shape[1] // head_dim
    local_kv = key_projection_weight.shape[1] // head_dim
    query_group_count = local_heads // local_kv

    def project(rows_x, starts):
        count = rows_x.shape[0]
        values_wide = rows_x.astype(jnp.float32)
        normalized_input = (
            values_wide
            * lax.rsqrt(jnp.mean(values_wide * values_wide, axis=-1, keepdims=True) + norm_eps)
            * norm_gain
        ).astype(jnp.bfloat16)
        query_matrix = (
            jnp.dot(normalized_input, w_query, preferred_element_type=jnp.float32) + q_bias
        )
        query_matrix = apply_rotary(
            query_matrix.reshape(count, local_heads, head_dim), starts, head_dim
        ).astype(jnp.bfloat16)
        key_rows = (
            jnp.dot(normalized_input, key_projection_weight, preferred_element_type=jnp.float32)
            + key_bias_vector
        )
        key_rows = apply_rotary(
            key_rows.reshape(count, local_kv, head_dim), starts, head_dim
        ).astype(jnp.bfloat16)
        value_rows = (
            jnp.dot(normalized_input, value_projection_weight, preferred_element_type=jnp.float32)
            + value_bias_vector
        ).astype(jnp.bfloat16)
        return jnp.concatenate(
            [
                query_matrix.reshape(count, local_heads * head_dim),
                key_rows.reshape(count, local_kv * head_dim),
                value_rows,
            ],
            axis=1,
        )

    qkv = project(jnp.concatenate(pieces, axis=0), sequence_starts)

    places = to_work_order(send_places(my_dest, ctx_count, group_cap, pack_len))
    send_hot = (
        places[None, :] == jnp.arange(ctx_count * group_cap, dtype=jnp.int32)[:, None]
    ).astype(jnp.bfloat16)
    outgoing = jnp.dot(send_hot, qkv, preferred_element_type=jnp.float32).astype(jnp.bfloat16)
    arrived = exchange(outgoing, "ctx", ctx_count)

    mine = (pool_dest >= 0) & (pool_dest // pack_len == ctx_index)
    mine_grid = mine.reshape(ctx_count, group_rows).astype(jnp.int32)
    rank_in = jnp.cumsum(mine_grid, axis=1) - mine_grid
    arrived_index = (
        jnp.arange(ctx_count, dtype=jnp.int32)[:, None] * group_cap + rank_in
    ).reshape(-1)
    my_slot_of_row = jnp.where(mine, pool_dest - ctx_index * pack_len, -1)
    slot_ids = jnp.arange(pack_len, dtype=jnp.int32)
    names_slot = my_slot_of_row[None, :] == slot_ids[:, None]
    source_of_slot = jnp.sum(jnp.where(names_slot, arrived_index[None, :], 0), axis=1)
    packed_qkv = select_rows(source_of_slot, arrived)

    q_width = local_heads * head_dim
    kv_width = local_kv * head_dim
    query_matrix = packed_qkv[:, :q_width].reshape(pack_len, local_kv, query_group_count, head_dim)
    projected_key_rows = packed_qkv[:, q_width : q_width + kv_width].reshape(
        pack_len, local_kv, head_dim
    )
    projected_value_rows = packed_qkv[:, q_width + kv_width :].reshape(pack_len, local_kv, head_dim)

    own_lengths = seq_len[0]
    own_ends = jnp.cumsum(own_lengths).astype(jnp.int32)
    segment = jnp.sum((own_ends[None, :] <= slot_ids[:, None]).astype(jnp.int32), axis=1)

    score_scale = 1.0 / math.sqrt(head_dim)
    chunk_count = 2 if pack_len % 16 == 0 else 1
    chunk_len = pack_len // chunk_count
    results = []
    for chunk in range(chunk_count):
        lo, hi = chunk * chunk_len, (chunk + 1) * chunk_len
        scores = (
            jnp.einsum(
                "qkgd,tkd->kgqt",
                query_matrix[lo:hi],
                projected_key_rows[:hi],
                preferred_element_type=jnp.float32,
            )
            * score_scale
        )
        allowed = (segment[lo:hi, None] == segment[None, :hi]) & (
            slot_ids[None, :hi] <= slot_ids[lo:hi, None]
        )
        scores = jnp.where(allowed[None, None], scores, -1e30)
        row_max = jnp.max(scores, axis=-1, keepdims=True)
        weights = jnp.exp(scores - row_max)
        row_total = jnp.sum(weights, axis=-1, keepdims=True)
        probability = (weights / row_total).astype(jnp.bfloat16)
        mixed_heads = jnp.einsum(
            "kgqt,tkd->qkgd",
            probability,
            projected_value_rows[:hi],
            preferred_element_type=jnp.float32,
        )
        mixed_heads = mixed_heads.astype(jnp.bfloat16).reshape(chunk_len, local_heads * head_dim)
        partial_out = jnp.dot(mixed_heads, w_out, preferred_element_type=jnp.float32)
        results.append(halving_scatter(partial_out, "head", head_count).astype(jnp.bfloat16))
    return jnp.concatenate(results, axis=0)


def exchange(outgoing, axis_name, count):
    if count > 8:
        return lax.all_to_all(outgoing, axis_name, split_axis=0, concat_axis=0, tiled=True)
    me = lax.axis_index(axis_name)
    chunks = outgoing.reshape((count, -1) + outgoing.shape[1:])
    by_shift = jnp.take(chunks, (me + jnp.arange(count)) % count, axis=0)
    from_shift = [by_shift[0]]
    for shift in range(1, count):
        pairs = [(i, (i + shift) % count) for i in range(count)]
        from_shift.append(lax.ppermute(by_shift[shift], axis_name, pairs))
    from_shift = jnp.stack(from_shift)
    arrived = jnp.take(from_shift, (me - jnp.arange(count)) % count, axis=0)
    return arrived.reshape(outgoing.shape)


def halving_scatter(partial, axis_name, count):
    bits = count.bit_length() - 1
    if count != 1 << bits or bits == 0:
        return lax.psum_scatter(partial, axis_name, scatter_dimension=1, tiled=True)
    block = partial.shape[1] // count
    me = lax.axis_index(axis_name)
    pieces = [(b, partial[:, b * block : (b + 1) * block]) for b in range(count)]
    for stage in range(bits):
        bit = (me >> stage) & 1
        lows = [(b, x) for b, x in pieces if not (b >> stage) & 1]
        highs = [x for b, x in pieces if (b >> stage) & 1]
        keep = [jnp.where(bit == 0, lo, hi) for (_, lo), hi in zip(lows, highs)]
        send = jnp.stack([jnp.where(bit == 0, hi, lo) for (_, lo), hi in zip(lows, highs)])
        pairs = [(i, i ^ (1 << stage)) for i in range(count)]
        got = lax.ppermute(send, axis_name, pairs)
        pieces = [(b, k + got[i]) for i, ((b, _), k) in enumerate(zip(lows, keep))]
    return pieces[0][1]


def doubling_gather(part, axis_name, count):
    bits = count.bit_length() - 1
    if count != 1 << bits or bits == 0:
        return lax.all_gather(part, axis_name, tiled=True)
    me = lax.axis_index(axis_name)
    have = part[None]
    for stage in reversed(range(bits)):
        bit = (me >> stage) & 1
        pairs = [(i, i ^ (1 << stage)) for i in range(count)]
        got = lax.ppermute(have, axis_name, pairs)
        first = jnp.where(bit == 0, have, got)
        second = jnp.where(bit == 0, got, have)
        have = jnp.stack([first, second], axis=1).reshape((-1,) + part.shape)
    return have.reshape((count * part.shape[0],) + part.shape[1:])


def xor_gather(part, axis_name, count):
    me = lax.axis_index(axis_name)
    bits = count.bit_length() - 1
    if count != 1 << bits:
        return [lax.all_gather(part, axis_name, tiled=True)], jnp.arange(count, dtype=jnp.int32)
    pieces, masks = [part], [0]
    for stage in reversed(range(bits)):
        pairs = [(i, i ^ (1 << stage)) for i in range(count)]
        pieces = pieces + [lax.ppermute(p, axis_name, pairs) for p in pieces]
        masks = masks + [m ^ (1 << stage) for m in masks]
    return pieces, me ^ jnp.asarray(masks, dtype=jnp.int32)


def solution(mesh):
    in_specs = (
        P(("ctx", "head"), None),
        P(),
        P("ctx", None),
        P(),
        P(None, "head"),
        P("head"),
        P(None, "head"),
        P("head"),
        P(None, "head"),
        P("head"),
        P("head", None),
    )
    out_specs = P("ctx", "head")
    return jax.shard_map(local, mesh=mesh, in_specs=in_specs, out_specs=out_specs, check_vma=False)
```

```python
import math

import jax
import jax.numpy as jnp
from jax import lax
from jax.sharding import PartitionSpec as P

HEAD_SIZE = 128
PACKED_SLOTS = 256


rope_base = 1000000.0
norm_eps = 1e-06


def send_places(targets, owner_count, capacity, pack_len):
    is_filled = targets >= 0
    owner_ids = jnp.where(is_filled, targets // pack_len, -1)
    membership = (owner_ids[:, None] == jnp.arange(owner_count, dtype=jnp.int32)[None, :]).astype(
        jnp.int32
    )
    earlier = jnp.cumsum(membership, axis=0) - membership
    rank_in = jnp.sum(earlier * membership, axis=1)
    return jnp.where(is_filled, owner_ids * capacity + rank_in, owner_count * capacity)


def one_hot_rows(index, count):
    return (index[:, None] == jnp.arange(count, dtype=jnp.int32)[None, :]).astype(jnp.bfloat16)


def select_rows(index, values):
    picked = jnp.dot(
        one_hot_rows(index, values.shape[0]), values, preferred_element_type=jnp.float32
    )
    return picked.astype(values.dtype)


def apply_rotary(values, sequence_starts, head_dim):
    half_dim = head_dim // 2
    frequency = jnp.exp(
        jnp.arange(half_dim, dtype=jnp.float32) * (-2.0 * math.log(rope_base) / head_dim)
    )
    angles = sequence_starts.astype(jnp.float32)[:, None] * frequency[None, :]
    cosine = jnp.cos(angles)[:, None, :]
    sine_table = jnp.sin(angles)[:, None, :]
    first_half = values[..., :half_dim]
    second_half = values[..., half_dim:]
    return jnp.concatenate(
        [
            first_half * cosine - second_half * sine_table,
            second_half * cosine + first_half * sine_table,
        ],
        axis=-1,
    )


def local(
    x_pool,
    pool_dest,
    seq_len,
    norm_gain,
    w_query,
    q_bias,
    key_projection_weight,
    key_bias_vector,
    value_projection_weight,
    value_bias_vector,
    w_out,
):
    ctx_count = lax.axis_size("ctx")
    head_count = lax.axis_size("head")
    pool_rows = x_pool.shape[0]
    capacity = pool_rows // ctx_count
    group_rows = pool_rows * head_count
    group_cap = capacity * head_count
    pack_len = PACKED_SLOTS
    head_dim = HEAD_SIZE
    ctx_index = lax.axis_index("ctx")

    all_lengths = doubling_gather(seq_len, "ctx", ctx_count)
    pieces, work_heads = xor_gather(x_pool, "head", head_count)

    dest_grid = pool_dest.reshape(ctx_count, group_rows)
    my_dest = lax.dynamic_index_in_dim(dest_grid, ctx_index, 0, keepdims=False)
    to_work_order = lambda v: jnp.take(
        v.reshape(head_count, pool_rows), work_heads, axis=0
    ).reshape(-1)
    work_dest = to_work_order(my_dest)
    is_filled = work_dest >= 0
    owner = jnp.where(is_filled, work_dest // pack_len, 0)
    slot = jnp.where(is_filled, work_dest % pack_len, 0)
    seq_ends = jnp.cumsum(all_lengths, axis=1).astype(jnp.int32)
    row_ends = jnp.take(seq_ends, owner, axis=0)
    row_lengths = jnp.take(all_lengths, owner, axis=0)
    finished = (row_ends <= slot[:, None]).astype(jnp.int32)
    sequence_starts = slot - jnp.sum(finished * row_lengths, axis=1)

    local_heads = w_query.shape[1] // head_dim
    local_kv = key_projection_weight.shape[1] // head_dim
    query_group_count = local_heads // local_kv

    def project(rows_x, starts):
        count = rows_x.shape[0]
        values_wide = rows_x.astype(jnp.float32)
        normalized_input = (
            values_wide
            * lax.rsqrt(jnp.mean(values_wide * values_wide, axis=-1, keepdims=True) + norm_eps)
            * norm_gain
        ).astype(jnp.bfloat16)
        query_matrix = (
            jnp.dot(normalized_input, w_query, preferred_element_type=jnp.float32) + q_bias
        )
        key_rows = (
            jnp.dot(normalized_input, key_projection_weight, preferred_element_type=jnp.float32)
            + key_bias_vector
        )
        query_matrix, key_rows = lax.optimization_barrier((query_matrix, key_rows))
        query_matrix = apply_rotary(
            query_matrix.reshape(count, local_heads, head_dim), starts, head_dim
        ).astype(jnp.bfloat16)
        key_rows = apply_rotary(
            key_rows.reshape(count, local_kv, head_dim), starts, head_dim
        ).astype(jnp.bfloat16)
        value_rows = (
            jnp.dot(normalized_input, value_projection_weight, preferred_element_type=jnp.float32)
            + value_bias_vector
        ).astype(jnp.bfloat16)
        return jnp.concatenate(
            [
                query_matrix.reshape(count, local_heads * head_dim),
                key_rows.reshape(count, local_kv * head_dim),
                value_rows,
            ],
            axis=1,
        )

    qkv = project(jnp.concatenate(pieces, axis=0), sequence_starts)

    shift_order = ctx_count <= 8
    if shift_order:
        shifted_dest = jnp.where(
            my_dest >= 0,
            ((my_dest // pack_len - ctx_index) % ctx_count) * pack_len + my_dest % pack_len,
            -1,
        )
    else:
        shifted_dest = my_dest
    places = to_work_order(send_places(shifted_dest, ctx_count, group_cap, pack_len))
    send_hot = (
        places[None, :] == jnp.arange(ctx_count * group_cap, dtype=jnp.int32)[:, None]
    ).astype(jnp.bfloat16)
    outgoing = jnp.dot(send_hot, qkv, preferred_element_type=jnp.float32).astype(jnp.bfloat16)
    arrived = exchange(outgoing, "ctx", ctx_count)

    mine = (pool_dest >= 0) & (pool_dest // pack_len == ctx_index)
    mine_grid = mine.reshape(ctx_count, group_rows).astype(jnp.int32)
    rank_in = jnp.cumsum(mine_grid, axis=1) - mine_grid
    source_ctx = jnp.arange(ctx_count, dtype=jnp.int32)[:, None]
    if shift_order:
        source_ctx = (ctx_index - source_ctx) % ctx_count
    arrived_index = (
        source_ctx * group_cap + rank_in
    ).reshape(-1)
    my_slot_of_row = jnp.where(mine, pool_dest - ctx_index * pack_len, -1)
    slot_ids = jnp.arange(pack_len, dtype=jnp.int32)
    names_slot = my_slot_of_row[None, :] == slot_ids[:, None]
    source_of_slot = jnp.sum(jnp.where(names_slot, arrived_index[None, :], 0), axis=1)
    packed_qkv = select_rows(source_of_slot, arrived)

    q_width = local_heads * head_dim
    kv_width = local_kv * head_dim
    query_matrix = packed_qkv[:, :q_width].reshape(pack_len, local_kv, query_group_count, head_dim)
    projected_key_rows = packed_qkv[:, q_width : q_width + kv_width].reshape(
        pack_len, local_kv, head_dim
    )
    projected_value_rows = packed_qkv[:, q_width + kv_width :].reshape(pack_len, local_kv, head_dim)

    own_lengths = seq_len[0]
    own_ends = jnp.cumsum(own_lengths).astype(jnp.int32)
    segment = jnp.sum((own_ends[None, :] <= slot_ids[:, None]).astype(jnp.int32), axis=1)

    score_scale = 1.0 / math.sqrt(head_dim)
    chunk_count = 4 if pack_len % 32 == 0 else 1
    chunk_len = pack_len // chunk_count
    results = []
    for chunk in range(chunk_count):
        lo, hi = chunk * chunk_len, (chunk + 1) * chunk_len
        scores = (
            jnp.einsum(
                "qkgd,tkd->kgqt",
                query_matrix[lo:hi],
                projected_key_rows[:hi],
                preferred_element_type=jnp.float32,
            )
            * score_scale
        )
        allowed = (segment[lo:hi, None] == segment[None, :hi]) & (
            slot_ids[None, :hi] <= slot_ids[lo:hi, None]
        )
        scores = jnp.where(allowed[None, None], scores, -1e30)
        row_max = jnp.max(scores, axis=-1, keepdims=True)
        weights = jnp.exp(scores - row_max)
        row_total = jnp.sum(weights, axis=-1, keepdims=True)
        probability = (weights / row_total).astype(jnp.bfloat16)
        mixed_heads = jnp.einsum(
            "kgqt,tkd->qkgd",
            probability,
            projected_value_rows[:hi],
            preferred_element_type=jnp.float32,
        )
        mixed_heads = mixed_heads.astype(jnp.bfloat16).reshape(chunk_len, local_heads * head_dim)
        partial_out = jnp.dot(mixed_heads, w_out, preferred_element_type=jnp.float32)
        results.append(halving_scatter(partial_out, "head", head_count).astype(jnp.bfloat16))
    return jnp.concatenate(results, axis=0)


def exchange(outgoing, axis_name, count):
    if count > 8:
        return lax.all_to_all(outgoing, axis_name, split_axis=0, concat_axis=0, tiled=True)
    chunks = outgoing.reshape((count, -1) + outgoing.shape[1:])
    arrived = [chunks[0]]
    for shift in range(1, count):
        pairs = [(i, (i + shift) % count) for i in range(count)]
        arrived.append(lax.ppermute(chunks[shift], axis_name, pairs))
    return jnp.concatenate(arrived, axis=0)


def halving_scatter(partial, axis_name, count):
    bits = count.bit_length() - 1
    if count != 1 << bits or bits == 0:
        return lax.psum_scatter(partial, axis_name, scatter_dimension=1, tiled=True)
    block = partial.shape[1] // count
    me = lax.axis_index(axis_name)
    pieces = [(b, partial[:, b * block : (b + 1) * block]) for b in range(count)]
    for stage in range(bits):
        bit = (me >> stage) & 1
        lows = [(b, x) for b, x in pieces if not (b >> stage) & 1]
        highs = [x for b, x in pieces if (b >> stage) & 1]
        keep = [jnp.where(bit == 0, lo, hi) for (_, lo), hi in zip(lows, highs)]
        send = jnp.stack([jnp.where(bit == 0, hi, lo) for (_, lo), hi in zip(lows, highs)])
        pairs = [(i, i ^ (1 << stage)) for i in range(count)]
        got = lax.ppermute(send, axis_name, pairs)
        pieces = [(b, k + got[i]) for i, ((b, _), k) in enumerate(zip(lows, keep))]
    return pieces[0][1]


def doubling_gather(part, axis_name, count):
    bits = count.bit_length() - 1
    if count != 1 << bits or bits == 0:
        return lax.all_gather(part, axis_name, tiled=True)
    me = lax.axis_index(axis_name)
    have = part[None]
    for stage in reversed(range(bits)):
        bit = (me >> stage) & 1
        pairs = [(i, i ^ (1 << stage)) for i in range(count)]
        got = lax.ppermute(have, axis_name, pairs)
        first = jnp.where(bit == 0, have, got)
        second = jnp.where(bit == 0, got, have)
        have = jnp.stack([first, second], axis=1).reshape((-1,) + part.shape)
    return have.reshape((count * part.shape[0],) + part.shape[1:])


def xor_gather(part, axis_name, count):
    me = lax.axis_index(axis_name)
    bits = count.bit_length() - 1
    if count != 1 << bits:
        return [lax.all_gather(part, axis_name, tiled=True)], jnp.arange(count, dtype=jnp.int32)
    pieces, masks = [part], [0]
    for stage in reversed(range(bits)):
        pairs = [(i, i ^ (1 << stage)) for i in range(count)]
        pieces = pieces + [lax.ppermute(p, axis_name, pairs) for p in pieces]
        masks = masks + [m ^ (1 << stage) for m in masks]
    return pieces, me ^ jnp.asarray(masks, dtype=jnp.int32)


def solution(mesh):
    in_specs = (
        P(("ctx", "head"), None),
        P(),
        P("ctx", None),
        P(),
        P(None, "head"),
        P("head"),
        P(None, "head"),
        P("head"),
        P(None, "head"),
        P("head"),
        P("head", None),
    )
    out_specs = P("ctx", "head")
    return jax.shard_map(local, mesh=mesh, in_specs=in_specs, out_specs=out_specs, check_vma=False)
```

```python
import math

import jax
import jax.numpy as jnp
from jax import lax
from jax.sharding import PartitionSpec as P

HEAD_SIZE = 128
PACKED_SLOTS = 256


rope_base = 1000000.0
norm_eps = 1e-06


def send_places(targets, owner_count, capacity, pack_len):
    is_filled = targets >= 0
    owner_ids = jnp.where(is_filled, targets // pack_len, -1)
    membership = (owner_ids[:, None] == jnp.arange(owner_count, dtype=jnp.int32)[None, :]).astype(
        jnp.int32
    )
    earlier = jnp.cumsum(membership, axis=0) - membership
    rank_in = jnp.sum(earlier * membership, axis=1)
    return jnp.where(is_filled, owner_ids * capacity + rank_in, owner_count * capacity)


def one_hot_rows(index, count):
    return (index[:, None] == jnp.arange(count, dtype=jnp.int32)[None, :]).astype(jnp.bfloat16)


def select_rows(index, values):
    picked = jnp.dot(
        one_hot_rows(index, values.shape[0]), values, preferred_element_type=jnp.float32
    )
    return picked.astype(values.dtype)


def apply_rotary(values, sequence_starts, head_dim):
    half_dim = head_dim // 2
    frequency = jnp.exp(
        jnp.arange(half_dim, dtype=jnp.float32) * (-2.0 * math.log(rope_base) / head_dim)
    )
    angles = sequence_starts.astype(jnp.float32)[:, None] * frequency[None, :]
    cosine = jnp.cos(angles)[:, None, :]
    sine_table = jnp.sin(angles)[:, None, :]
    first_half = values[..., :half_dim]
    second_half = values[..., half_dim:]
    return jnp.concatenate(
        [
            first_half * cosine - second_half * sine_table,
            second_half * cosine + first_half * sine_table,
        ],
        axis=-1,
    )


def local(
    x_pool,
    pool_dest,
    seq_len,
    norm_gain,
    w_query,
    q_bias,
    key_projection_weight,
    key_bias_vector,
    value_projection_weight,
    value_bias_vector,
    w_out,
):
    ctx_count = lax.axis_size("ctx")
    head_count = lax.axis_size("head")
    pool_rows = x_pool.shape[0]
    capacity = pool_rows // ctx_count
    group_rows = pool_rows * head_count
    group_cap = capacity * head_count
    pack_len = PACKED_SLOTS
    head_dim = HEAD_SIZE
    ctx_index = lax.axis_index("ctx")

    all_lengths = shift_gather(seq_len, "ctx", ctx_count)
    pieces, work_heads = xor_gather(x_pool, "head", head_count)

    dest_grid = pool_dest.reshape(ctx_count, group_rows)
    my_dest = lax.dynamic_index_in_dim(dest_grid, ctx_index, 0, keepdims=False)
    to_work_order = lambda v: jnp.take(
        v.reshape(head_count, pool_rows), work_heads, axis=0
    ).reshape(-1)
    work_dest = to_work_order(my_dest)
    is_filled = work_dest >= 0
    owner = jnp.where(is_filled, work_dest // pack_len, 0)
    slot = jnp.where(is_filled, work_dest % pack_len, 0)
    seq_ends = jnp.cumsum(all_lengths, axis=1).astype(jnp.int32)
    owner_hot = owner[:, None, None] == jnp.arange(ctx_count, dtype=jnp.int32)[None, :, None]
    row_ends = jnp.sum(jnp.where(owner_hot, seq_ends[None], 0), axis=1)
    row_lengths = jnp.sum(jnp.where(owner_hot, all_lengths[None], 0), axis=1)
    finished = (row_ends <= slot[:, None]).astype(jnp.int32)
    sequence_starts = slot - jnp.sum(finished * row_lengths, axis=1)

    local_heads = w_query.shape[1] // head_dim
    local_kv = key_projection_weight.shape[1] // head_dim
    query_group_count = local_heads // local_kv

    def project(rows_x, starts):
        count = rows_x.shape[0]
        values_wide = rows_x.astype(jnp.float32)
        normalized_input = (
            values_wide
            * lax.rsqrt(jnp.mean(values_wide * values_wide, axis=-1, keepdims=True) + norm_eps)
            * norm_gain
        ).astype(jnp.bfloat16)
        query_matrix = (
            jnp.dot(normalized_input, w_query, preferred_element_type=jnp.float32) + q_bias
        )
        key_rows = (
            jnp.dot(normalized_input, key_projection_weight, preferred_element_type=jnp.float32)
            + key_bias_vector
        )
        query_matrix, key_rows = lax.optimization_barrier((query_matrix, key_rows))
        query_matrix = apply_rotary(
            query_matrix.reshape(count, local_heads, head_dim), starts, head_dim
        ).astype(jnp.bfloat16)
        key_rows = apply_rotary(
            key_rows.reshape(count, local_kv, head_dim), starts, head_dim
        ).astype(jnp.bfloat16)
        value_rows = (
            jnp.dot(normalized_input, value_projection_weight, preferred_element_type=jnp.float32)
            + value_bias_vector
        ).astype(jnp.bfloat16)
        return jnp.concatenate(
            [
                query_matrix.reshape(count, local_heads * head_dim),
                key_rows.reshape(count, local_kv * head_dim),
                value_rows,
            ],
            axis=1,
        )

    qkv = project(jnp.concatenate(pieces, axis=0), sequence_starts)

    shift_order = ctx_count <= 8
    if shift_order:
        shifted_dest = jnp.where(
            my_dest >= 0,
            ((my_dest // pack_len - ctx_index) % ctx_count) * pack_len + my_dest % pack_len,
            -1,
        )
    else:
        shifted_dest = my_dest
    places = to_work_order(send_places(shifted_dest, ctx_count, group_cap, pack_len))
    send_hot = (
        places[None, :] == jnp.arange(ctx_count * group_cap, dtype=jnp.int32)[:, None]
    ).astype(jnp.bfloat16)
    outgoing = jnp.dot(send_hot, qkv, preferred_element_type=jnp.float32).astype(jnp.bfloat16)
    arrived = exchange(outgoing, "ctx", ctx_count)

    mine = (pool_dest >= 0) & (pool_dest // pack_len == ctx_index)
    mine_grid = mine.reshape(ctx_count, group_rows).astype(jnp.int32)
    rank_in = jnp.cumsum(mine_grid, axis=1) - mine_grid
    source_ctx = jnp.arange(ctx_count, dtype=jnp.int32)[:, None]
    if shift_order:
        source_ctx = (ctx_index - source_ctx) % ctx_count
    arrived_index = (
        source_ctx * group_cap + rank_in
    ).reshape(-1)
    my_slot_of_row = jnp.where(mine, pool_dest - ctx_index * pack_len, -1)
    slot_ids = jnp.arange(pack_len, dtype=jnp.int32)
    names_slot = my_slot_of_row[None, :] == slot_ids[:, None]
    source_of_slot = jnp.sum(jnp.where(names_slot, arrived_index[None, :], 0), axis=1)
    packed_qkv = select_rows(source_of_slot, arrived)

    q_width = local_heads * head_dim
    kv_width = local_kv * head_dim
    query_matrix = packed_qkv[:, :q_width].reshape(pack_len, local_kv, query_group_count, head_dim)
    projected_key_rows = packed_qkv[:, q_width : q_width + kv_width].reshape(
        pack_len, local_kv, head_dim
    )
    projected_value_rows = packed_qkv[:, q_width + kv_width :].reshape(pack_len, local_kv, head_dim)

    own_lengths = seq_len[0]
    own_ends = jnp.cumsum(own_lengths).astype(jnp.int32)
    segment = jnp.sum((own_ends[None, :] <= slot_ids[:, None]).astype(jnp.int32), axis=1)

    score_scale = 1.0 / math.sqrt(head_dim)
    chunk_count = 4 if pack_len % 32 == 0 else 1
    chunk_len = pack_len // chunk_count
    results = []
    for chunk in range(chunk_count):
        lo, hi = chunk * chunk_len, (chunk + 1) * chunk_len
        scores = (
            jnp.einsum(
                "qkgd,tkd->kgqt",
                query_matrix[lo:hi],
                projected_key_rows[:hi],
                preferred_element_type=jnp.float32,
            )
            * score_scale
        )
        allowed = (segment[lo:hi, None] == segment[None, :hi]) & (
            slot_ids[None, :hi] <= slot_ids[lo:hi, None]
        )
        scores = jnp.where(allowed[None, None], scores, -1e30)
        row_max = jnp.max(scores, axis=-1, keepdims=True)
        weights = jnp.exp(scores - row_max)
        row_total = jnp.sum(weights, axis=-1, keepdims=True)
        probability = (weights / row_total).astype(jnp.bfloat16)
        mixed_heads = jnp.einsum(
            "kgqt,tkd->qkgd",
            probability,
            projected_value_rows[:hi],
            preferred_element_type=jnp.float32,
        )
        mixed_heads = mixed_heads.astype(jnp.bfloat16).reshape(chunk_len, local_heads * head_dim)
        partial_out = jnp.dot(mixed_heads, w_out, preferred_element_type=jnp.float32)
        results.append(halving_scatter(partial_out, "head", head_count).astype(jnp.bfloat16))
    return jnp.concatenate(results, axis=0)


def shift_gather(part, axis_name, count):
    if count > 8:
        return doubling_gather(part, axis_name, count)
    me = lax.axis_index(axis_name)
    by_shift = [part] + [
        lax.ppermute(part, axis_name, [(i, (i + shift) % count) for i in range(count)])
        for shift in range(1, count)
    ]
    stacked = jnp.stack(by_shift)
    return jnp.take(stacked, (me - jnp.arange(count)) % count, axis=0).reshape(
        (count * part.shape[0],) + part.shape[1:]
    )


def exchange(outgoing, axis_name, count):
    if count > 8:
        return lax.all_to_all(outgoing, axis_name, split_axis=0, concat_axis=0, tiled=True)
    chunks = outgoing.reshape((count, -1) + outgoing.shape[1:])
    arrived = [chunks[0]]
    for shift in range(1, count):
        pairs = [(i, (i + shift) % count) for i in range(count)]
        arrived.append(lax.ppermute(chunks[shift], axis_name, pairs))
    return jnp.concatenate(arrived, axis=0)


def halving_scatter(partial, axis_name, count):
    bits = count.bit_length() - 1
    if count != 1 << bits or bits == 0:
        return lax.psum_scatter(partial, axis_name, scatter_dimension=1, tiled=True)
    block = partial.shape[1] // count
    me = lax.axis_index(axis_name)
    pieces = [(b, partial[:, b * block : (b + 1) * block]) for b in range(count)]
    for stage in range(bits):
        bit = (me >> stage) & 1
        lows = [(b, x) for b, x in pieces if not (b >> stage) & 1]
        highs = [x for b, x in pieces if (b >> stage) & 1]
        keep = [jnp.where(bit == 0, lo, hi) for (_, lo), hi in zip(lows, highs)]
        send = jnp.stack([jnp.where(bit == 0, hi, lo) for (_, lo), hi in zip(lows, highs)])
        pairs = [(i, i ^ (1 << stage)) for i in range(count)]
        got = lax.ppermute(send, axis_name, pairs)
        pieces = [(b, k + got[i]) for i, ((b, _), k) in enumerate(zip(lows, keep))]
    return pieces[0][1]


def doubling_gather(part, axis_name, count):
    bits = count.bit_length() - 1
    if count != 1 << bits or bits == 0:
        return lax.all_gather(part, axis_name, tiled=True)
    me = lax.axis_index(axis_name)
    have = part[None]
    for stage in reversed(range(bits)):
        bit = (me >> stage) & 1
        pairs = [(i, i ^ (1 << stage)) for i in range(count)]
        got = lax.ppermute(have, axis_name, pairs)
        first = jnp.where(bit == 0, have, got)
        second = jnp.where(bit == 0, got, have)
        have = jnp.stack([first, second], axis=1).reshape((-1,) + part.shape)
    return have.reshape((count * part.shape[0],) + part.shape[1:])


def xor_gather(part, axis_name, count):
    me = lax.axis_index(axis_name)
    bits = count.bit_length() - 1
    if count != 1 << bits:
        return [lax.all_gather(part, axis_name, tiled=True)], jnp.arange(count, dtype=jnp.int32)
    pieces, masks = [part], [0]
    for stage in reversed(range(bits)):
        pairs = [(i, i ^ (1 << stage)) for i in range(count)]
        pieces = pieces + [lax.ppermute(p, axis_name, pairs) for p in pieces]
        masks = masks + [m ^ (1 << stage) for m in masks]
    return pieces, me ^ jnp.asarray(masks, dtype=jnp.int32)


def solution(mesh):
    in_specs = (
        P(("ctx", "head"), None),
        P(),
        P("ctx", None),
        P(),
        P(None, "head"),
        P("head"),
        P(None, "head"),
        P("head"),
        P(None, "head"),
        P("head"),
        P("head", None),
    )
    out_specs = P("ctx", "head")
    return jax.shard_map(local, mesh=mesh, in_specs=in_specs, out_specs=out_specs, check_vma=False)
```

```python
import math

import jax
import jax.numpy as jnp
from jax import lax
from jax.sharding import PartitionSpec as P

HEAD_SIZE = 128
PACKED_SLOTS = 256


rope_base = 1000000.0
norm_eps = 1e-06


def send_places(targets, owner_count, capacity, pack_len):
    is_filled = targets >= 0
    owner_ids = jnp.where(is_filled, targets // pack_len, -1)
    membership = (owner_ids[:, None] == jnp.arange(owner_count, dtype=jnp.int32)[None, :]).astype(
        jnp.int32
    )
    earlier = jnp.cumsum(membership, axis=0) - membership
    rank_in = jnp.sum(earlier * membership, axis=1)
    return jnp.where(is_filled, owner_ids * capacity + rank_in, owner_count * capacity)


def one_hot_rows(index, count):
    return (index[:, None] == jnp.arange(count, dtype=jnp.int32)[None, :]).astype(jnp.bfloat16)


def select_rows(index, values):
    picked = jnp.dot(
        one_hot_rows(index, values.shape[0]), values, preferred_element_type=jnp.float32
    )
    return picked.astype(values.dtype)


def apply_rotary(values, sequence_starts, head_dim):
    half_dim = head_dim // 2
    frequency = jnp.exp(
        jnp.arange(half_dim, dtype=jnp.float32) * (-2.0 * math.log(rope_base) / head_dim)
    )
    angles = sequence_starts.astype(jnp.float32)[:, None] * frequency[None, :]
    cosine = jnp.cos(angles)[:, None, :]
    sine_table = jnp.sin(angles)[:, None, :]
    first_half = values[..., :half_dim]
    second_half = values[..., half_dim:]
    return jnp.concatenate(
        [
            first_half * cosine - second_half * sine_table,
            second_half * cosine + first_half * sine_table,
        ],
        axis=-1,
    )


def local(
    x_pool,
    pool_dest,
    seq_len,
    norm_gain,
    w_query,
    q_bias,
    key_projection_weight,
    key_bias_vector,
    value_projection_weight,
    value_bias_vector,
    w_out,
):
    ctx_count = lax.axis_size("ctx")
    head_count = lax.axis_size("head")
    pool_rows = x_pool.shape[0]
    capacity = pool_rows // ctx_count
    group_rows = pool_rows * head_count
    group_cap = capacity * head_count
    pack_len = PACKED_SLOTS
    head_dim = HEAD_SIZE
    ctx_index = lax.axis_index("ctx")

    all_lengths = shift_gather(seq_len, "ctx", ctx_count)
    pieces, work_heads = xor_gather(x_pool, "head", head_count)

    dest_grid = pool_dest.reshape(ctx_count, group_rows)
    my_dest = lax.dynamic_index_in_dim(dest_grid, ctx_index, 0, keepdims=False)
    to_work_order = lambda v: jnp.take(
        v.reshape(head_count, pool_rows), work_heads, axis=0
    ).reshape(-1)
    work_dest = to_work_order(my_dest)
    is_filled = work_dest >= 0
    owner = jnp.where(is_filled, work_dest // pack_len, 0)
    slot = jnp.where(is_filled, work_dest % pack_len, 0)
    seq_ends = jnp.cumsum(all_lengths, axis=1).astype(jnp.int32)
    owner_hot = owner[:, None, None] == jnp.arange(ctx_count, dtype=jnp.int32)[None, :, None]
    row_ends = jnp.sum(jnp.where(owner_hot, seq_ends[None], 0), axis=1)
    row_lengths = jnp.sum(jnp.where(owner_hot, all_lengths[None], 0), axis=1)
    finished = (row_ends <= slot[:, None]).astype(jnp.int32)
    sequence_starts = slot - jnp.sum(finished * row_lengths, axis=1)

    local_heads = w_query.shape[1] // head_dim
    local_kv = key_projection_weight.shape[1] // head_dim
    query_group_count = local_heads // local_kv

    def project(rows_x, starts):
        count = rows_x.shape[0]
        values_wide = rows_x.astype(jnp.float32)
        normalized_input = (
            values_wide
            * lax.rsqrt(jnp.mean(values_wide * values_wide, axis=-1, keepdims=True) + norm_eps)
            * norm_gain
        ).astype(jnp.bfloat16)
        query_matrix = (
            jnp.dot(normalized_input, w_query, preferred_element_type=jnp.float32) + q_bias
        )
        key_rows = (
            jnp.dot(normalized_input, key_projection_weight, preferred_element_type=jnp.float32)
            + key_bias_vector
        )
        query_matrix, key_rows = lax.optimization_barrier((query_matrix, key_rows))
        query_matrix = apply_rotary(
            query_matrix.reshape(count, local_heads, head_dim), starts, head_dim
        ).astype(jnp.bfloat16)
        key_rows = apply_rotary(
            key_rows.reshape(count, local_kv, head_dim), starts, head_dim
        ).astype(jnp.bfloat16)
        value_rows = (
            jnp.dot(normalized_input, value_projection_weight, preferred_element_type=jnp.float32)
            + value_bias_vector
        ).astype(jnp.bfloat16)
        return jnp.concatenate(
            [
                query_matrix.reshape(count, local_heads * head_dim),
                key_rows.reshape(count, local_kv * head_dim),
                value_rows,
            ],
            axis=1,
        )

    qkv = project(jnp.concatenate(pieces, axis=0), sequence_starts)

    shift_order = ctx_count <= 8
    if shift_order:
        shifted_dest = jnp.where(
            my_dest >= 0,
            ((my_dest // pack_len - ctx_index) % ctx_count) * pack_len + my_dest % pack_len,
            -1,
        )
    else:
        shifted_dest = my_dest
    places = to_work_order(send_places(shifted_dest, ctx_count, group_cap, pack_len))
    send_hot = (
        places[None, :] == jnp.arange(ctx_count * group_cap, dtype=jnp.int32)[:, None]
    ).astype(jnp.bfloat16)
    outgoing = jnp.dot(send_hot, qkv, preferred_element_type=jnp.float32).astype(jnp.bfloat16)
    arrived = exchange(outgoing, "ctx", ctx_count)

    mine = (pool_dest >= 0) & (pool_dest // pack_len == ctx_index)
    mine_grid = mine.reshape(ctx_count, group_rows).astype(jnp.int32)
    rank_in = jnp.cumsum(mine_grid, axis=1) - mine_grid
    source_ctx = jnp.arange(ctx_count, dtype=jnp.int32)[:, None]
    if shift_order:
        source_ctx = (ctx_index - source_ctx) % ctx_count
    arrived_index = (
        source_ctx * group_cap + rank_in
    ).reshape(-1)
    my_slot_of_row = jnp.where(mine, pool_dest - ctx_index * pack_len, -1)
    slot_ids = jnp.arange(pack_len, dtype=jnp.int32)
    names_slot = my_slot_of_row[None, :] == slot_ids[:, None]
    source_of_slot = jnp.sum(jnp.where(names_slot, arrived_index[None, :], 0), axis=1)
    q_width = local_heads * head_dim
    kv_width = local_kv * head_dim

    own_lengths = seq_len[0]
    own_ends = jnp.cumsum(own_lengths).astype(jnp.int32)
    segment = jnp.sum((own_ends[None, :] <= slot_ids[:, None]).astype(jnp.int32), axis=1)

    score_scale = 1.0 / math.sqrt(head_dim)
    chunk_count = 4 if pack_len % 32 == 0 else 1
    chunk_len = pack_len // chunk_count
    results = []
    key_parts, value_parts = [], []
    pending = None
    for chunk in range(chunk_count):
        lo, hi = chunk * chunk_len, (chunk + 1) * chunk_len
        chunk_qkv = select_rows(source_of_slot[lo:hi], arrived)
        if pending is not None:
            chunk_qkv, held = lax.optimization_barrier((chunk_qkv, [x for _, x in pending]))
            pending = [(b, x) for (b, _), x in zip(pending, held)]
            results.append(finish_scatter(pending, "head", head_count).astype(jnp.bfloat16))
        query_matrix = chunk_qkv[:, :q_width].reshape(
            chunk_len, local_kv, query_group_count, head_dim
        )
        key_parts.append(chunk_qkv[:, q_width : q_width + kv_width])
        value_parts.append(chunk_qkv[:, q_width + kv_width :])
        projected_key_rows = jnp.concatenate(key_parts, axis=0).reshape(hi, local_kv, head_dim)
        projected_value_rows = jnp.concatenate(value_parts, axis=0).reshape(
            hi, local_kv, head_dim
        )
        scores = (
            jnp.einsum(
                "qkgd,tkd->kgqt",
                query_matrix,
                projected_key_rows,
                preferred_element_type=jnp.float32,
            )
            * score_scale
        )
        allowed = (segment[lo:hi, None] == segment[None, :hi]) & (
            slot_ids[None, :hi] <= slot_ids[lo:hi, None]
        )
        scores = jnp.where(allowed[None, None], scores, -1e30)
        row_max = jnp.max(scores, axis=-1, keepdims=True)
        weights = jnp.exp(scores - row_max)
        row_total = jnp.sum(weights, axis=-1, keepdims=True)
        probability = (weights / row_total).astype(jnp.bfloat16)
        mixed_heads = jnp.einsum(
            "kgqt,tkd->qkgd",
            probability,
            projected_value_rows,
            preferred_element_type=jnp.float32,
        )
        mixed_heads = mixed_heads.astype(jnp.bfloat16).reshape(chunk_len, local_heads * head_dim)
        partial_out = jnp.dot(mixed_heads, w_out, preferred_element_type=jnp.float32)
        pending = start_scatter(partial_out, "head", head_count)
    results.append(finish_scatter(pending, "head", head_count).astype(jnp.bfloat16))
    return jnp.concatenate(results, axis=0)


def shift_gather(part, axis_name, count):
    if count > 8:
        return doubling_gather(part, axis_name, count)
    me = lax.axis_index(axis_name)
    by_shift = [part] + [
        lax.ppermute(part, axis_name, [(i, (i + shift) % count) for i in range(count)])
        for shift in range(1, count)
    ]
    stacked = jnp.stack(by_shift)
    return jnp.take(stacked, (me - jnp.arange(count)) % count, axis=0).reshape(
        (count * part.shape[0],) + part.shape[1:]
    )


def exchange(outgoing, axis_name, count):
    if count > 8:
        return lax.all_to_all(outgoing, axis_name, split_axis=0, concat_axis=0, tiled=True)
    chunks = outgoing.reshape((count, -1) + outgoing.shape[1:])
    arrived = [chunks[0]]
    for shift in range(1, count):
        pairs = [(i, (i + shift) % count) for i in range(count)]
        arrived.append(lax.ppermute(chunks[shift], axis_name, pairs))
    return jnp.concatenate(arrived, axis=0)


def scatter_bits(count):
    bits = count.bit_length() - 1
    return bits if count == 1 << bits else 0


def halving_stage(pieces, stage, axis_name, count):
    me = lax.axis_index(axis_name)
    bit = (me >> stage) & 1
    lows = [(b, x) for b, x in pieces if not (b >> stage) & 1]
    highs = [x for b, x in pieces if (b >> stage) & 1]
    keep = [jnp.where(bit == 0, lo, hi) for (_, lo), hi in zip(lows, highs)]
    send = jnp.stack([jnp.where(bit == 0, hi, lo) for (_, lo), hi in zip(lows, highs)])
    pairs = [(i, i ^ (1 << stage)) for i in range(count)]
    got = lax.ppermute(send, axis_name, pairs)
    return [(b, k + got[i]) for i, ((b, _), k) in enumerate(zip(lows, keep))]


def start_scatter(partial, axis_name, count):
    bits = scatter_bits(count)
    if bits == 0:
        return [(0, partial)]
    block = partial.shape[1] // count
    pieces = [(b, partial[:, b * block : (b + 1) * block]) for b in range(count)]
    return halving_stage(pieces, 0, axis_name, count)


def finish_scatter(pieces, axis_name, count):
    bits = scatter_bits(count)
    if bits == 0:
        return lax.psum_scatter(pieces[0][1], axis_name, scatter_dimension=1, tiled=True)
    for stage in range(1, bits):
        pieces = halving_stage(pieces, stage, axis_name, count)
    return pieces[0][1]


def doubling_gather(part, axis_name, count):
    bits = count.bit_length() - 1
    if count != 1 << bits or bits == 0:
        return lax.all_gather(part, axis_name, tiled=True)
    me = lax.axis_index(axis_name)
    have = part[None]
    for stage in reversed(range(bits)):
        bit = (me >> stage) & 1
        pairs = [(i, i ^ (1 << stage)) for i in range(count)]
        got = lax.ppermute(have, axis_name, pairs)
        first = jnp.where(bit == 0, have, got)
        second = jnp.where(bit == 0, got, have)
        have = jnp.stack([first, second], axis=1).reshape((-1,) + part.shape)
    return have.reshape((count * part.shape[0],) + part.shape[1:])


def xor_gather(part, axis_name, count):
    me = lax.axis_index(axis_name)
    bits = count.bit_length() - 1
    if count != 1 << bits:
        return [lax.all_gather(part, axis_name, tiled=True)], jnp.arange(count, dtype=jnp.int32)
    pieces, masks = [part], [0]
    for stage in reversed(range(bits)):
        pairs = [(i, i ^ (1 << stage)) for i in range(count)]
        pieces = pieces + [lax.ppermute(p, axis_name, pairs) for p in pieces]
        masks = masks + [m ^ (1 << stage) for m in masks]
    return pieces, me ^ jnp.asarray(masks, dtype=jnp.int32)


def solution(mesh):
    in_specs = (
        P(("ctx", "head"), None),
        P(),
        P("ctx", None),
        P(),
        P(None, "head"),
        P("head"),
        P(None, "head"),
        P("head"),
        P(None, "head"),
        P("head"),
        P("head", None),
    )
    out_specs = P("ctx", "head")
    return jax.shard_map(local, mesh=mesh, in_specs=in_specs, out_specs=out_specs, check_vma=False)
```

```python
import math

import jax
import jax.numpy as jnp
from jax import lax
from jax.sharding import PartitionSpec as P

HEAD_SIZE = 128
PACKED_SLOTS = 256


rope_base = 1000000.0
norm_eps = 1e-06


def send_places(targets, owner_count, capacity, pack_len):
    is_filled = targets >= 0
    owner_ids = jnp.where(is_filled, targets // pack_len, -1)
    membership = (owner_ids[:, None] == jnp.arange(owner_count, dtype=jnp.int32)[None, :]).astype(
        jnp.int32
    )
    earlier = jnp.cumsum(membership, axis=0) - membership
    rank_in = jnp.sum(earlier * membership, axis=1)
    return jnp.where(is_filled, owner_ids * capacity + rank_in, owner_count * capacity)


def one_hot_rows(index, count):
    return (index[:, None] == jnp.arange(count, dtype=jnp.int32)[None, :]).astype(jnp.bfloat16)


def select_rows(index, values):
    picked = jnp.dot(
        one_hot_rows(index, values.shape[0]), values, preferred_element_type=jnp.float32
    )
    return picked.astype(values.dtype)


def apply_rotary(values, sequence_starts, head_dim):
    half_dim = head_dim // 2
    frequency = jnp.exp(
        jnp.arange(half_dim, dtype=jnp.float32) * (-2.0 * math.log(rope_base) / head_dim)
    )
    angles = sequence_starts.astype(jnp.float32)[:, None] * frequency[None, :]
    cosine = jnp.cos(angles)[:, None, :]
    sine_table = jnp.sin(angles)[:, None, :]
    first_half = values[..., :half_dim]
    second_half = values[..., half_dim:]
    return jnp.concatenate(
        [
            first_half * cosine - second_half * sine_table,
            second_half * cosine + first_half * sine_table,
        ],
        axis=-1,
    )


def local(
    x_pool,
    pool_dest,
    seq_len,
    norm_gain,
    w_query,
    q_bias,
    key_projection_weight,
    key_bias_vector,
    value_projection_weight,
    value_bias_vector,
    w_out,
):
    ctx_count = lax.axis_size("ctx")
    head_count = lax.axis_size("head")
    pool_rows = x_pool.shape[0]
    capacity = pool_rows // ctx_count
    group_rows = pool_rows * head_count
    group_cap = capacity * head_count
    pack_len = PACKED_SLOTS
    head_dim = HEAD_SIZE
    ctx_index = lax.axis_index("ctx")

    all_lengths = shift_gather(seq_len, "ctx", ctx_count)
    pieces, work_heads = xor_gather(x_pool, "head", head_count)

    dest_grid = pool_dest.reshape(ctx_count, group_rows)
    my_dest = lax.dynamic_index_in_dim(dest_grid, ctx_index, 0, keepdims=False)
    to_work_order = lambda v: jnp.take(
        v.reshape(head_count, pool_rows), work_heads, axis=0
    ).reshape(-1)
    work_dest = to_work_order(my_dest)
    is_filled = work_dest >= 0
    owner = jnp.where(is_filled, work_dest // pack_len, 0)
    slot = jnp.where(is_filled, work_dest % pack_len, 0)
    seq_ends = jnp.cumsum(all_lengths, axis=1).astype(jnp.int32)
    owner_hot = owner[:, None, None] == jnp.arange(ctx_count, dtype=jnp.int32)[None, :, None]
    row_ends = jnp.sum(jnp.where(owner_hot, seq_ends[None], 0), axis=1)
    row_lengths = jnp.sum(jnp.where(owner_hot, all_lengths[None], 0), axis=1)
    finished = (row_ends <= slot[:, None]).astype(jnp.int32)
    sequence_starts = slot - jnp.sum(finished * row_lengths, axis=1)

    local_heads = w_query.shape[1] // head_dim
    local_kv = key_projection_weight.shape[1] // head_dim
    query_group_count = local_heads // local_kv

    def project(rows_x, starts):
        count = rows_x.shape[0]
        values_wide = rows_x.astype(jnp.float32)
        normalized_input = (
            values_wide
            * lax.rsqrt(jnp.mean(values_wide * values_wide, axis=-1, keepdims=True) + norm_eps)
            * norm_gain
        ).astype(jnp.bfloat16)
        query_matrix = (
            jnp.dot(normalized_input, w_query, preferred_element_type=jnp.float32) + q_bias
        )
        key_rows = (
            jnp.dot(normalized_input, key_projection_weight, preferred_element_type=jnp.float32)
            + key_bias_vector
        )
        query_matrix, key_rows = lax.optimization_barrier((query_matrix, key_rows))
        query_matrix = apply_rotary(
            query_matrix.reshape(count, local_heads, head_dim), starts, head_dim
        ).astype(jnp.bfloat16)
        key_rows = apply_rotary(
            key_rows.reshape(count, local_kv, head_dim), starts, head_dim
        ).astype(jnp.bfloat16)
        value_rows = (
            jnp.dot(normalized_input, value_projection_weight, preferred_element_type=jnp.float32)
            + value_bias_vector
        ).astype(jnp.bfloat16)
        return jnp.concatenate(
            [
                query_matrix.reshape(count, local_heads * head_dim),
                key_rows.reshape(count, local_kv * head_dim),
                value_rows,
            ],
            axis=1,
        )

    own_rows = pieces[0].shape[0]
    qkv_parts = [project(pieces[0], sequence_starts[:own_rows])]
    if len(pieces) > 1:
        qkv_parts.append(project(jnp.concatenate(pieces[1:], axis=0), sequence_starts[own_rows:]))
    qkv = jnp.concatenate(qkv_parts, axis=0)

    shift_order = ctx_count <= 8
    if shift_order:
        shifted_dest = jnp.where(
            my_dest >= 0,
            ((my_dest // pack_len - ctx_index) % ctx_count) * pack_len + my_dest % pack_len,
            -1,
        )
    else:
        shifted_dest = my_dest
    places = to_work_order(send_places(shifted_dest, ctx_count, group_cap, pack_len))
    send_hot = (
        places[None, :] == jnp.arange(ctx_count * group_cap, dtype=jnp.int32)[:, None]
    ).astype(jnp.bfloat16)
    outgoing = jnp.dot(send_hot, qkv, preferred_element_type=jnp.float32).astype(jnp.bfloat16)
    arrived = exchange(outgoing, "ctx", ctx_count)

    mine = (pool_dest >= 0) & (pool_dest // pack_len == ctx_index)
    mine_grid = mine.reshape(ctx_count, group_rows).astype(jnp.int32)
    rank_in = jnp.cumsum(mine_grid, axis=1) - mine_grid
    source_ctx = jnp.arange(ctx_count, dtype=jnp.int32)[:, None]
    if shift_order:
        source_ctx = (ctx_index - source_ctx) % ctx_count
    arrived_index = (
        source_ctx * group_cap + rank_in
    ).reshape(-1)
    my_slot_of_row = jnp.where(mine, pool_dest - ctx_index * pack_len, -1)
    slot_ids = jnp.arange(pack_len, dtype=jnp.int32)
    names_slot = my_slot_of_row[None, :] == slot_ids[:, None]
    source_of_slot = jnp.sum(jnp.where(names_slot, arrived_index[None, :], 0), axis=1)
    q_width = local_heads * head_dim
    kv_width = local_kv * head_dim

    own_lengths = seq_len[0]
    own_ends = jnp.cumsum(own_lengths).astype(jnp.int32)
    segment = jnp.sum((own_ends[None, :] <= slot_ids[:, None]).astype(jnp.int32), axis=1)

    score_scale = 1.0 / math.sqrt(head_dim)
    chunk_count = 4 if pack_len % 32 == 0 else 1
    chunk_len = pack_len // chunk_count
    results = []
    key_parts, value_parts = [], []
    for chunk in range(chunk_count):
        lo, hi = chunk * chunk_len, (chunk + 1) * chunk_len
        chunk_qkv = select_rows(source_of_slot[lo:hi], arrived)
        query_matrix = chunk_qkv[:, :q_width].reshape(
            chunk_len, local_kv, query_group_count, head_dim
        )
        key_parts.append(chunk_qkv[:, q_width : q_width + kv_width])
        value_parts.append(chunk_qkv[:, q_width + kv_width :])
        projected_key_rows = jnp.concatenate(key_parts, axis=0).reshape(hi, local_kv, head_dim)
        projected_value_rows = jnp.concatenate(value_parts, axis=0).reshape(
            hi, local_kv, head_dim
        )
        scores = (
            jnp.einsum(
                "qkgd,tkd->kgqt",
                query_matrix,
                projected_key_rows,
                preferred_element_type=jnp.float32,
            )
            * score_scale
        )
        allowed = (segment[lo:hi, None] == segment[None, :hi]) & (
            slot_ids[None, :hi] <= slot_ids[lo:hi, None]
        )
        scores = jnp.where(allowed[None, None], scores, -1e30)
        row_max = jnp.max(scores, axis=-1, keepdims=True)
        weights = jnp.exp(scores - row_max)
        row_total = jnp.sum(weights, axis=-1, keepdims=True)
        probability = (weights / row_total).astype(jnp.bfloat16)
        mixed_heads = jnp.einsum(
            "kgqt,tkd->qkgd",
            probability,
            projected_value_rows,
            preferred_element_type=jnp.float32,
        )
        mixed_heads = mixed_heads.astype(jnp.bfloat16).reshape(chunk_len, local_heads * head_dim)
        partial_out = jnp.dot(mixed_heads, w_out, preferred_element_type=jnp.float32)
        results.append(halving_scatter(partial_out, "head", head_count).astype(jnp.bfloat16))
    return jnp.concatenate(results, axis=0)


def shift_gather(part, axis_name, count):
    if count > 8:
        return doubling_gather(part, axis_name, count)
    me = lax.axis_index(axis_name)
    by_shift = [part] + [
        lax.ppermute(part, axis_name, [(i, (i + shift) % count) for i in range(count)])
        for shift in range(1, count)
    ]
    stacked = jnp.stack(by_shift)
    return jnp.take(stacked, (me - jnp.arange(count)) % count, axis=0).reshape(
        (count * part.shape[0],) + part.shape[1:]
    )


def exchange(outgoing, axis_name, count):
    if count > 8:
        return lax.all_to_all(outgoing, axis_name, split_axis=0, concat_axis=0, tiled=True)
    chunks = outgoing.reshape((count, -1) + outgoing.shape[1:])
    arrived = [chunks[0]]
    for shift in range(1, count):
        pairs = [(i, (i + shift) % count) for i in range(count)]
        arrived.append(lax.ppermute(chunks[shift], axis_name, pairs))
    return jnp.concatenate(arrived, axis=0)


def halving_scatter(partial, axis_name, count):
    bits = count.bit_length() - 1
    if count != 1 << bits or bits == 0:
        return lax.psum_scatter(partial, axis_name, scatter_dimension=1, tiled=True)
    block = partial.shape[1] // count
    me = lax.axis_index(axis_name)
    pieces = [(b, partial[:, b * block : (b + 1) * block]) for b in range(count)]
    for stage in range(bits):
        bit = (me >> stage) & 1
        lows = [(b, x) for b, x in pieces if not (b >> stage) & 1]
        highs = [x for b, x in pieces if (b >> stage) & 1]
        keep = [jnp.where(bit == 0, lo, hi) for (_, lo), hi in zip(lows, highs)]
        send = jnp.stack([jnp.where(bit == 0, hi, lo) for (_, lo), hi in zip(lows, highs)])
        pairs = [(i, i ^ (1 << stage)) for i in range(count)]
        got = lax.ppermute(send, axis_name, pairs)
        pieces = [(b, k + got[i]) for i, ((b, _), k) in enumerate(zip(lows, keep))]
    return pieces[0][1]


def doubling_gather(part, axis_name, count):
    bits = count.bit_length() - 1
    if count != 1 << bits or bits == 0:
        return lax.all_gather(part, axis_name, tiled=True)
    me = lax.axis_index(axis_name)
    have = part[None]
    for stage in reversed(range(bits)):
        bit = (me >> stage) & 1
        pairs = [(i, i ^ (1 << stage)) for i in range(count)]
        got = lax.ppermute(have, axis_name, pairs)
        first = jnp.where(bit == 0, have, got)
        second = jnp.where(bit == 0, got, have)
        have = jnp.stack([first, second], axis=1).reshape((-1,) + part.shape)
    return have.reshape((count * part.shape[0],) + part.shape[1:])


def xor_gather(part, axis_name, count):
    me = lax.axis_index(axis_name)
    bits = count.bit_length() - 1
    if count != 1 << bits:
        return [lax.all_gather(part, axis_name, tiled=True)], jnp.arange(count, dtype=jnp.int32)
    pieces, masks = [part], [0]
    for stage in reversed(range(bits)):
        pairs = [(i, i ^ (1 << stage)) for i in range(count)]
        pieces = pieces + [lax.ppermute(p, axis_name, pairs) for p in pieces]
        masks = masks + [m ^ (1 << stage) for m in masks]
    return pieces, me ^ jnp.asarray(masks, dtype=jnp.int32)


def solution(mesh):
    in_specs = (
        P(("ctx", "head"), None),
        P(),
        P("ctx", None),
        P(),
        P(None, "head"),
        P("head"),
        P(None, "head"),
        P("head"),
        P(None, "head"),
        P("head"),
        P("head", None),
    )
    out_specs = P("ctx", "head")
    return jax.shard_map(local, mesh=mesh, in_specs=in_specs, out_specs=out_specs, check_vma=False)
```

```python
import math

import jax
import jax.numpy as jnp
from jax import lax
from jax.sharding import PartitionSpec as P

HEAD_SIZE = 128
PACKED_SLOTS = 256


rope_base = 1000000.0
norm_eps = 1e-06


def send_places(targets, owner_count, capacity, pack_len):
    is_filled = targets >= 0
    owner_ids = jnp.where(is_filled, targets // pack_len, -1)
    membership = (owner_ids[:, None] == jnp.arange(owner_count, dtype=jnp.int32)[None, :]).astype(
        jnp.int32
    )
    earlier = jnp.cumsum(membership, axis=0) - membership
    rank_in = jnp.sum(earlier * membership, axis=1)
    return jnp.where(is_filled, owner_ids * capacity + rank_in, owner_count * capacity)


def one_hot_rows(index, count):
    return (index[:, None] == jnp.arange(count, dtype=jnp.int32)[None, :]).astype(jnp.bfloat16)


def select_rows(index, values):
    picked = jnp.dot(
        one_hot_rows(index, values.shape[0]), values, preferred_element_type=jnp.float32
    )
    return picked.astype(values.dtype)


def apply_rotary(values, sequence_starts, head_dim):
    half_dim = head_dim // 2
    frequency = jnp.exp(
        jnp.arange(half_dim, dtype=jnp.float32) * (-2.0 * math.log(rope_base) / head_dim)
    )
    angles = sequence_starts.astype(jnp.float32)[:, None] * frequency[None, :]
    cosine = jnp.cos(angles)[:, None, :]
    sine_table = jnp.sin(angles)[:, None, :]
    first_half = values[..., :half_dim]
    second_half = values[..., half_dim:]
    return jnp.concatenate(
        [
            first_half * cosine - second_half * sine_table,
            second_half * cosine + first_half * sine_table,
        ],
        axis=-1,
    )


def local(
    x_pool,
    pool_dest,
    seq_len,
    norm_gain,
    w_query,
    q_bias,
    key_projection_weight,
    key_bias_vector,
    value_projection_weight,
    value_bias_vector,
    w_out,
):
    ctx_count = lax.axis_size("ctx")
    head_count = lax.axis_size("head")
    pool_rows = x_pool.shape[0]
    capacity = pool_rows // ctx_count
    group_rows = pool_rows * head_count
    group_cap = capacity * head_count
    pack_len = PACKED_SLOTS
    head_dim = HEAD_SIZE
    ctx_index = lax.axis_index("ctx")

    all_lengths = shift_gather(seq_len, "ctx", ctx_count)
    pieces, work_heads = xor_gather(x_pool, "head", head_count)

    dest_grid = pool_dest.reshape(ctx_count, group_rows)
    my_dest = lax.dynamic_index_in_dim(dest_grid, ctx_index, 0, keepdims=False)
    to_work_order = lambda v: jnp.take(
        v.reshape(head_count, pool_rows), work_heads, axis=0
    ).reshape(-1)
    work_dest = to_work_order(my_dest)
    is_filled = work_dest >= 0
    owner = jnp.where(is_filled, work_dest // pack_len, 0)
    slot = jnp.where(is_filled, work_dest % pack_len, 0)
    seq_ends = jnp.cumsum(all_lengths, axis=1).astype(jnp.int32)
    owner_hot = owner[:, None, None] == jnp.arange(ctx_count, dtype=jnp.int32)[None, :, None]
    row_ends = jnp.sum(jnp.where(owner_hot, seq_ends[None], 0), axis=1)
    row_lengths = jnp.sum(jnp.where(owner_hot, all_lengths[None], 0), axis=1)
    finished = (row_ends <= slot[:, None]).astype(jnp.int32)
    sequence_starts = slot - jnp.sum(finished * row_lengths, axis=1)

    local_heads = w_query.shape[1] // head_dim
    local_kv = key_projection_weight.shape[1] // head_dim
    query_group_count = local_heads // local_kv

    def project(rows_x, starts):
        count = rows_x.shape[0]
        values_wide = rows_x.astype(jnp.float32)
        normalized_input = (
            values_wide
            * lax.rsqrt(jnp.mean(values_wide * values_wide, axis=-1, keepdims=True) + norm_eps)
            * norm_gain
        ).astype(jnp.bfloat16)
        query_matrix = (
            jnp.dot(normalized_input, w_query, preferred_element_type=jnp.float32) + q_bias
        )
        key_rows = (
            jnp.dot(normalized_input, key_projection_weight, preferred_element_type=jnp.float32)
            + key_bias_vector
        )
        query_matrix, key_rows = lax.optimization_barrier((query_matrix, key_rows))
        query_matrix = apply_rotary(
            query_matrix.reshape(count, local_heads, head_dim), starts, head_dim
        ).astype(jnp.bfloat16)
        key_rows = apply_rotary(
            key_rows.reshape(count, local_kv, head_dim), starts, head_dim
        ).astype(jnp.bfloat16)
        value_rows = (
            jnp.dot(normalized_input, value_projection_weight, preferred_element_type=jnp.float32)
            + value_bias_vector
        ).astype(jnp.bfloat16)
        return jnp.concatenate(
            [
                query_matrix.reshape(count, local_heads * head_dim),
                key_rows.reshape(count, local_kv * head_dim),
                value_rows,
            ],
            axis=1,
        )

    qkv = project(jnp.concatenate(pieces, axis=0), sequence_starts)

    shift_order = ctx_count <= 8
    if shift_order:
        shifted_dest = jnp.where(
            my_dest >= 0,
            ((my_dest // pack_len - ctx_index) % ctx_count) * pack_len + my_dest % pack_len,
            -1,
        )
    else:
        shifted_dest = my_dest
    places = to_work_order(send_places(shifted_dest, ctx_count, group_cap, pack_len))
    send_hot = (
        places[None, :] == jnp.arange(ctx_count * group_cap, dtype=jnp.int32)[:, None]
    ).astype(jnp.bfloat16)
    outgoing = jnp.dot(send_hot, qkv, preferred_element_type=jnp.float32).astype(jnp.bfloat16)
    arrived = exchange(outgoing, "ctx", ctx_count)

    mine = (pool_dest >= 0) & (pool_dest // pack_len == ctx_index)
    mine_grid = mine.reshape(ctx_count, group_rows).astype(jnp.int32)
    rank_in = jnp.cumsum(mine_grid, axis=1) - mine_grid
    source_ctx = jnp.arange(ctx_count, dtype=jnp.int32)[:, None]
    if shift_order:
        source_ctx = (ctx_index - source_ctx) % ctx_count
    arrived_index = (
        source_ctx * group_cap + rank_in
    ).reshape(-1)
    my_slot_of_row = jnp.where(mine, pool_dest - ctx_index * pack_len, -1)
    slot_ids = jnp.arange(pack_len, dtype=jnp.int32)
    names_slot = my_slot_of_row[None, :] == slot_ids[:, None]
    source_of_slot = jnp.sum(jnp.where(names_slot, arrived_index[None, :], 0), axis=1)
    q_width = local_heads * head_dim
    kv_width = local_kv * head_dim

    own_lengths = seq_len[0]
    own_ends = jnp.cumsum(own_lengths).astype(jnp.int32)
    segment = jnp.sum((own_ends[None, :] <= slot_ids[:, None]).astype(jnp.int32), axis=1)

    score_scale = 1.0 / math.sqrt(head_dim)
    chunk_count = 4 if pack_len % 32 == 0 else 1
    chunk_len = pack_len // chunk_count
    results = []
    key_parts, value_parts = [], []
    for chunk in range(chunk_count):
        lo, hi = chunk * chunk_len, (chunk + 1) * chunk_len
        chunk_qkv = select_rows(source_of_slot[lo:hi], arrived)
        query_matrix = chunk_qkv[:, :q_width].reshape(
            chunk_len, local_kv, query_group_count, head_dim
        )
        key_parts.append(chunk_qkv[:, q_width : q_width + kv_width])
        value_parts.append(chunk_qkv[:, q_width + kv_width :])
        projected_key_rows = jnp.concatenate(key_parts, axis=0).reshape(hi, local_kv, head_dim)
        projected_value_rows = jnp.concatenate(value_parts, axis=0).reshape(
            hi, local_kv, head_dim
        )
        scores = (
            jnp.einsum(
                "qkgd,tkd->kgqt",
                query_matrix,
                projected_key_rows,
                preferred_element_type=jnp.float32,
            )
            * score_scale
        )
        allowed = (segment[lo:hi, None] == segment[None, :hi]) & (
            slot_ids[None, :hi] <= slot_ids[lo:hi, None]
        )
        scores = jnp.where(allowed[None, None], scores, -1e30)
        row_max = jnp.max(scores, axis=-1, keepdims=True)
        weights = jnp.exp(scores - row_max)
        row_total = jnp.sum(weights, axis=-1, keepdims=True)
        probability = (weights / row_total).astype(jnp.bfloat16)
        mixed_heads = jnp.einsum(
            "kgqt,tkd->qkgd",
            probability,
            projected_value_rows,
            preferred_element_type=jnp.float32,
        )
        mixed_heads = mixed_heads.astype(jnp.bfloat16).reshape(chunk_len, local_heads * head_dim)
        partial_out = jnp.dot(mixed_heads, w_out, preferred_element_type=jnp.float32)
        results.append(halving_scatter(partial_out, "head", head_count).astype(jnp.bfloat16))
    return jnp.concatenate(results, axis=0)


def shift_gather(part, axis_name, count):
    if count > 8:
        return doubling_gather(part, axis_name, count)
    me = lax.axis_index(axis_name)
    by_shift = [part] + [
        lax.ppermute(part, axis_name, [(i, (i + shift) % count) for i in range(count)])
        for shift in range(1, count)
    ]
    stacked = jnp.stack(by_shift)
    return jnp.take(stacked, (me - jnp.arange(count)) % count, axis=0).reshape(
        (count * part.shape[0],) + part.shape[1:]
    )


def exchange(outgoing, axis_name, count):
    if count > 8:
        return lax.all_to_all(outgoing, axis_name, split_axis=0, concat_axis=0, tiled=True)
    chunks = outgoing.reshape((count, -1) + outgoing.shape[1:])
    arrived = [chunks[0]]
    for shift in range(1, count):
        pairs = [(i, (i + shift) % count) for i in range(count)]
        arrived.append(lax.ppermute(chunks[shift], axis_name, pairs))
    return jnp.concatenate(arrived, axis=0)


def halving_scatter(partial, axis_name, count):
    bits = count.bit_length() - 1
    if count != 1 << bits or bits == 0:
        return lax.psum_scatter(partial, axis_name, scatter_dimension=1, tiled=True)
    block = partial.shape[1] // count
    me = lax.axis_index(axis_name)
    pieces = [(b, partial[:, b * block : (b + 1) * block]) for b in range(count)]
    for stage in range(bits):
        bit = (me >> stage) & 1
        lows = [(b, x) for b, x in pieces if not (b >> stage) & 1]
        highs = [x for b, x in pieces if (b >> stage) & 1]
        keep = [jnp.where(bit == 0, lo, hi) for (_, lo), hi in zip(lows, highs)]
        send = jnp.stack([jnp.where(bit == 0, hi, lo) for (_, lo), hi in zip(lows, highs)])
        pairs = [(i, i ^ (1 << stage)) for i in range(count)]
        got = lax.ppermute(send, axis_name, pairs)
        pieces = [(b, k + got[i]) for i, ((b, _), k) in enumerate(zip(lows, keep))]
    return pieces[0][1]


def doubling_gather(part, axis_name, count):
    bits = count.bit_length() - 1
    if count != 1 << bits or bits == 0:
        return lax.all_gather(part, axis_name, tiled=True)
    me = lax.axis_index(axis_name)
    have = part[None]
    for stage in reversed(range(bits)):
        bit = (me >> stage) & 1
        pairs = [(i, i ^ (1 << stage)) for i in range(count)]
        got = lax.ppermute(have, axis_name, pairs)
        first = jnp.where(bit == 0, have, got)
        second = jnp.where(bit == 0, got, have)
        have = jnp.stack([first, second], axis=1).reshape((-1,) + part.shape)
    return have.reshape((count * part.shape[0],) + part.shape[1:])


def xor_gather(part, axis_name, count):
    me = lax.axis_index(axis_name)
    bits = count.bit_length() - 1
    if count != 1 << bits:
        return [lax.all_gather(part, axis_name, tiled=True)], jnp.arange(count, dtype=jnp.int32)
    pieces, masks = [part], [0]
    for stage in reversed(range(bits)):
        pairs = [(i, i ^ (1 << stage)) for i in range(count)]
        pieces = pieces + [lax.ppermute(p, axis_name, pairs) for p in pieces]
        masks = masks + [m ^ (1 << stage) for m in masks]
    return pieces, me ^ jnp.asarray(masks, dtype=jnp.int32)


def solution(mesh):
    in_specs = (
        P(("ctx", "head"), None),
        P(),
        P("ctx", None),
        P(),
        P(None, "head"),
        P("head"),
        P(None, "head"),
        P("head"),
        P(None, "head"),
        P("head"),
        P("head", None),
    )
    out_specs = P("ctx", "head")
    return jax.shard_map(local, mesh=mesh, in_specs=in_specs, out_specs=out_specs, check_vma=False)
```

```python
import math

import jax
import jax.numpy as jnp
from jax import lax
from jax.sharding import PartitionSpec as P

HEAD_SIZE = 128
PACKED_SLOTS = 256


rope_base = 1000000.0
norm_eps = 1e-06


def send_places(targets, owner_count, capacity, pack_len):
    is_filled = targets >= 0
    owner_ids = jnp.where(is_filled, targets // pack_len, -1)
    membership = (owner_ids[:, None] == jnp.arange(owner_count, dtype=jnp.int32)[None, :]).astype(
        jnp.int32
    )
    earlier = jnp.cumsum(membership, axis=0) - membership
    rank_in = jnp.sum(earlier * membership, axis=1)
    return jnp.where(is_filled, owner_ids * capacity + rank_in, owner_count * capacity)


def one_hot_rows(index, count):
    return (index[:, None] == jnp.arange(count, dtype=jnp.int32)[None, :]).astype(jnp.bfloat16)


def select_rows(index, values):
    picked = jnp.dot(
        one_hot_rows(index, values.shape[0]), values, preferred_element_type=jnp.float32
    )
    return picked.astype(values.dtype)


def apply_rotary(values, sequence_starts, head_dim):
    half_dim = head_dim // 2
    frequency = jnp.exp(
        jnp.arange(half_dim, dtype=jnp.float32) * (-2.0 * math.log(rope_base) / head_dim)
    )
    angles = sequence_starts.astype(jnp.float32)[:, None] * frequency[None, :]
    cosine = jnp.cos(angles)[:, None, :]
    sine_table = jnp.sin(angles)[:, None, :]
    first_half = values[..., :half_dim]
    second_half = values[..., half_dim:]
    return jnp.concatenate(
        [
            first_half * cosine - second_half * sine_table,
            second_half * cosine + first_half * sine_table,
        ],
        axis=-1,
    )


def local(
    x_pool,
    pool_dest,
    seq_len,
    norm_gain,
    w_query,
    q_bias,
    key_projection_weight,
    key_bias_vector,
    value_projection_weight,
    value_bias_vector,
    w_out,
):
    ctx_count = lax.axis_size("ctx")
    head_count = lax.axis_size("head")
    pool_rows = x_pool.shape[0]
    capacity = pool_rows // ctx_count
    group_rows = pool_rows * head_count
    group_cap = capacity * head_count
    pack_len = PACKED_SLOTS
    head_dim = HEAD_SIZE
    ctx_index = lax.axis_index("ctx")

    all_lengths = shift_gather(seq_len, "ctx", ctx_count)
    pieces, work_heads = xor_gather(x_pool, "head", head_count)

    dest_grid = pool_dest.reshape(ctx_count, group_rows)
    my_dest = lax.dynamic_index_in_dim(dest_grid, ctx_index, 0, keepdims=False)
    to_work_order = lambda v: jnp.take(
        v.reshape(head_count, pool_rows), work_heads, axis=0
    ).reshape(-1)
    work_dest = to_work_order(my_dest)
    is_filled = work_dest >= 0
    owner = jnp.where(is_filled, work_dest // pack_len, 0)
    slot = jnp.where(is_filled, work_dest % pack_len, 0)
    seq_ends = jnp.cumsum(all_lengths, axis=1).astype(jnp.int32)
    owner_hot = owner[:, None, None] == jnp.arange(ctx_count, dtype=jnp.int32)[None, :, None]
    row_ends = jnp.sum(jnp.where(owner_hot, seq_ends[None], 0), axis=1)
    row_lengths = jnp.sum(jnp.where(owner_hot, all_lengths[None], 0), axis=1)
    finished = (row_ends <= slot[:, None]).astype(jnp.int32)
    sequence_starts = slot - jnp.sum(finished * row_lengths, axis=1)

    local_heads = w_query.shape[1] // head_dim
    local_kv = key_projection_weight.shape[1] // head_dim
    query_group_count = local_heads // local_kv

    def project(rows_x, starts):
        count = rows_x.shape[0]
        values_wide = rows_x.astype(jnp.float32)
        normalized_input = (
            values_wide
            * lax.rsqrt(jnp.mean(values_wide * values_wide, axis=-1, keepdims=True) + norm_eps)
            * norm_gain
        ).astype(jnp.bfloat16)
        query_matrix = (
            jnp.dot(normalized_input, w_query, preferred_element_type=jnp.float32) + q_bias
        )
        key_rows = (
            jnp.dot(normalized_input, key_projection_weight, preferred_element_type=jnp.float32)
            + key_bias_vector
        )
        query_matrix, key_rows = lax.optimization_barrier((query_matrix, key_rows))
        query_matrix = apply_rotary(
            query_matrix.reshape(count, local_heads, head_dim), starts, head_dim
        ).astype(jnp.bfloat16)
        key_rows = apply_rotary(
            key_rows.reshape(count, local_kv, head_dim), starts, head_dim
        ).astype(jnp.bfloat16)
        value_rows = (
            jnp.dot(normalized_input, value_projection_weight, preferred_element_type=jnp.float32)
            + value_bias_vector
        ).astype(jnp.bfloat16)
        return jnp.concatenate(
            [
                query_matrix.reshape(count, local_heads * head_dim),
                key_rows.reshape(count, local_kv * head_dim),
                value_rows,
            ],
            axis=1,
        )

    qkv = project(jnp.concatenate(pieces, axis=0), sequence_starts)

    shift_order = ctx_count <= 8
    if shift_order:
        shifted_dest = jnp.where(
            my_dest >= 0,
            ((my_dest // pack_len - ctx_index) % ctx_count) * pack_len + my_dest % pack_len,
            -1,
        )
    else:
        shifted_dest = my_dest
    places = to_work_order(send_places(shifted_dest, ctx_count, group_cap, pack_len))
    send_hit = places[None, :] == jnp.arange(ctx_count * group_cap, dtype=jnp.int32)[:, None]
    work_rows = jnp.arange(group_rows, dtype=jnp.int32)
    source_rows = jnp.where(
        jnp.any(send_hit, axis=1),
        jnp.sum(jnp.where(send_hit, work_rows[None, :], 0), axis=1),
        group_rows,
    )
    padded_qkv = jnp.concatenate([qkv, jnp.zeros((1, qkv.shape[1]), qkv.dtype)], axis=0)
    outgoing = jnp.take(padded_qkv, source_rows, axis=0)
    arrived = exchange(outgoing, "ctx", ctx_count)

    mine = (pool_dest >= 0) & (pool_dest // pack_len == ctx_index)
    mine_grid = mine.reshape(ctx_count, group_rows).astype(jnp.int32)
    rank_in = jnp.cumsum(mine_grid, axis=1) - mine_grid
    source_ctx = jnp.arange(ctx_count, dtype=jnp.int32)[:, None]
    if shift_order:
        source_ctx = (ctx_index - source_ctx) % ctx_count
    arrived_index = (
        source_ctx * group_cap + rank_in
    ).reshape(-1)
    my_slot_of_row = jnp.where(mine, pool_dest - ctx_index * pack_len, -1)
    slot_ids = jnp.arange(pack_len, dtype=jnp.int32)
    names_slot = my_slot_of_row[None, :] == slot_ids[:, None]
    source_of_slot = jnp.sum(jnp.where(names_slot, arrived_index[None, :], 0), axis=1)
    packed_qkv = select_rows(source_of_slot, arrived)

    q_width = local_heads * head_dim
    kv_width = local_kv * head_dim
    query_matrix = packed_qkv[:, :q_width].reshape(pack_len, local_kv, query_group_count, head_dim)
    projected_key_rows = packed_qkv[:, q_width : q_width + kv_width].reshape(
        pack_len, local_kv, head_dim
    )
    projected_value_rows = packed_qkv[:, q_width + kv_width :].reshape(pack_len, local_kv, head_dim)

    own_lengths = seq_len[0]
    own_ends = jnp.cumsum(own_lengths).astype(jnp.int32)
    segment = jnp.sum((own_ends[None, :] <= slot_ids[:, None]).astype(jnp.int32), axis=1)

    score_scale = 1.0 / math.sqrt(head_dim)
    chunk_count = 4 if pack_len % 32 == 0 else 1
    chunk_len = pack_len // chunk_count
    results = []
    for chunk in range(chunk_count):
        lo, hi = chunk * chunk_len, (chunk + 1) * chunk_len
        scores = (
            jnp.einsum(
                "qkgd,tkd->kgqt",
                query_matrix[lo:hi],
                projected_key_rows[:hi],
                preferred_element_type=jnp.float32,
            )
            * score_scale
        )
        allowed = (segment[lo:hi, None] == segment[None, :hi]) & (
            slot_ids[None, :hi] <= slot_ids[lo:hi, None]
        )
        scores = jnp.where(allowed[None, None], scores, -1e30)
        row_max = jnp.max(scores, axis=-1, keepdims=True)
        weights = jnp.exp(scores - row_max)
        row_total = jnp.sum(weights, axis=-1, keepdims=True)
        probability = (weights / row_total).astype(jnp.bfloat16)
        mixed_heads = jnp.einsum(
            "kgqt,tkd->qkgd",
            probability,
            projected_value_rows[:hi],
            preferred_element_type=jnp.float32,
        )
        mixed_heads = mixed_heads.astype(jnp.bfloat16).reshape(chunk_len, local_heads * head_dim)
        partial_out = jnp.dot(mixed_heads, w_out, preferred_element_type=jnp.float32)
        results.append(halving_scatter(partial_out, "head", head_count).astype(jnp.bfloat16))
    return jnp.concatenate(results, axis=0)


def shift_gather(part, axis_name, count):
    if count > 8:
        return doubling_gather(part, axis_name, count)
    me = lax.axis_index(axis_name)
    by_shift = [part] + [
        lax.ppermute(part, axis_name, [(i, (i + shift) % count) for i in range(count)])
        for shift in range(1, count)
    ]
    stacked = jnp.stack(by_shift)
    return jnp.take(stacked, (me - jnp.arange(count)) % count, axis=0).reshape(
        (count * part.shape[0],) + part.shape[1:]
    )


def exchange(outgoing, axis_name, count):
    if count > 8:
        return lax.all_to_all(outgoing, axis_name, split_axis=0, concat_axis=0, tiled=True)
    chunks = outgoing.reshape((count, -1) + outgoing.shape[1:])
    arrived = [chunks[0]]
    for shift in range(1, count):
        pairs = [(i, (i + shift) % count) for i in range(count)]
        arrived.append(lax.ppermute(chunks[shift], axis_name, pairs))
    return jnp.concatenate(arrived, axis=0)


def halving_scatter(partial, axis_name, count):
    bits = count.bit_length() - 1
    if count != 1 << bits or bits == 0:
        return lax.psum_scatter(partial, axis_name, scatter_dimension=1, tiled=True)
    block = partial.shape[1] // count
    me = lax.axis_index(axis_name)
    pieces = [(b, partial[:, b * block : (b + 1) * block]) for b in range(count)]
    for stage in range(bits):
        bit = (me >> stage) & 1
        lows = [(b, x) for b, x in pieces if not (b >> stage) & 1]
        highs = [x for b, x in pieces if (b >> stage) & 1]
        keep = [jnp.where(bit == 0, lo, hi) for (_, lo), hi in zip(lows, highs)]
        send = jnp.stack([jnp.where(bit == 0, hi, lo) for (_, lo), hi in zip(lows, highs)])
        pairs = [(i, i ^ (1 << stage)) for i in range(count)]
        got = lax.ppermute(send, axis_name, pairs)
        pieces = [(b, k + got[i]) for i, ((b, _), k) in enumerate(zip(lows, keep))]
    return pieces[0][1]


def doubling_gather(part, axis_name, count):
    bits = count.bit_length() - 1
    if count != 1 << bits or bits == 0:
        return lax.all_gather(part, axis_name, tiled=True)
    me = lax.axis_index(axis_name)
    have = part[None]
    for stage in reversed(range(bits)):
        bit = (me >> stage) & 1
        pairs = [(i, i ^ (1 << stage)) for i in range(count)]
        got = lax.ppermute(have, axis_name, pairs)
        first = jnp.where(bit == 0, have, got)
        second = jnp.where(bit == 0, got, have)
        have = jnp.stack([first, second], axis=1).reshape((-1,) + part.shape)
    return have.reshape((count * part.shape[0],) + part.shape[1:])


def xor_gather(part, axis_name, count):
    me = lax.axis_index(axis_name)
    bits = count.bit_length() - 1
    if count != 1 << bits:
        return [lax.all_gather(part, axis_name, tiled=True)], jnp.arange(count, dtype=jnp.int32)
    pieces, masks = [part], [0]
    for stage in reversed(range(bits)):
        pairs = [(i, i ^ (1 << stage)) for i in range(count)]
        pieces = pieces + [lax.ppermute(p, axis_name, pairs) for p in pieces]
        masks = masks + [m ^ (1 << stage) for m in masks]
    return pieces, me ^ jnp.asarray(masks, dtype=jnp.int32)


def solution(mesh):
    in_specs = (
        P(("ctx", "head"), None),
        P(),
        P("ctx", None),
        P(),
        P(None, "head"),
        P("head"),
        P(None, "head"),
        P("head"),
        P(None, "head"),
        P("head"),
        P("head", None),
    )
    out_specs = P("ctx", "head")
    return jax.shard_map(local, mesh=mesh, in_specs=in_specs, out_specs=out_specs, check_vma=False)
```

```python
import math

import jax
import jax.numpy as jnp
from jax import lax
from jax.sharding import PartitionSpec as P

HEAD_SIZE = 128
PACKED_SLOTS = 256


rope_base = 1000000.0
norm_eps = 1e-06


def send_places(targets, owner_count, capacity, pack_len):
    is_filled = targets >= 0
    owner_ids = jnp.where(is_filled, targets // pack_len, -1)
    membership = (owner_ids[:, None] == jnp.arange(owner_count, dtype=jnp.int32)[None, :]).astype(
        jnp.int32
    )
    earlier = jnp.cumsum(membership, axis=0) - membership
    rank_in = jnp.sum(earlier * membership, axis=1)
    return jnp.where(is_filled, owner_ids * capacity + rank_in, owner_count * capacity)


def one_hot_rows(index, count):
    return (index[:, None] == jnp.arange(count, dtype=jnp.int32)[None, :]).astype(jnp.bfloat16)


def select_rows(index, values):
    picked = jnp.dot(
        one_hot_rows(index, values.shape[0]), values, preferred_element_type=jnp.float32
    )
    return picked.astype(values.dtype)


def apply_rotary(values, sequence_starts, head_dim):
    half_dim = head_dim // 2
    frequency = jnp.exp(
        jnp.arange(half_dim, dtype=jnp.float32) * (-2.0 * math.log(rope_base) / head_dim)
    )
    angles = sequence_starts.astype(jnp.float32)[:, None] * frequency[None, :]
    cosine = jnp.cos(angles)[:, None, :]
    sine_table = jnp.sin(angles)[:, None, :]
    first_half = values[..., :half_dim]
    second_half = values[..., half_dim:]
    return jnp.concatenate(
        [
            first_half * cosine - second_half * sine_table,
            second_half * cosine + first_half * sine_table,
        ],
        axis=-1,
    )


def local(
    x_pool,
    pool_dest,
    seq_len,
    norm_gain,
    w_query,
    q_bias,
    key_projection_weight,
    key_bias_vector,
    value_projection_weight,
    value_bias_vector,
    w_out,
):
    ctx_count = lax.axis_size("ctx")
    head_count = lax.axis_size("head")
    pool_rows = x_pool.shape[0]
    capacity = pool_rows // ctx_count
    group_rows = pool_rows * head_count
    group_cap = capacity * head_count
    pack_len = PACKED_SLOTS
    head_dim = HEAD_SIZE
    ctx_index = lax.axis_index("ctx")

    all_lengths = shift_gather(seq_len, "ctx", ctx_count)
    pieces, work_heads = xor_gather(x_pool, "head", head_count)

    dest_grid = pool_dest.reshape(ctx_count, group_rows)
    my_dest = lax.dynamic_index_in_dim(dest_grid, ctx_index, 0, keepdims=False)
    to_work_order = lambda v: jnp.take(
        v.reshape(head_count, pool_rows), work_heads, axis=0
    ).reshape(-1)
    work_dest = to_work_order(my_dest)
    is_filled = work_dest >= 0
    owner = jnp.where(is_filled, work_dest // pack_len, 0)
    slot = jnp.where(is_filled, work_dest % pack_len, 0)
    seq_ends = jnp.cumsum(all_lengths, axis=1).astype(jnp.int32)
    owner_hot = owner[:, None, None] == jnp.arange(ctx_count, dtype=jnp.int32)[None, :, None]
    row_ends = jnp.sum(jnp.where(owner_hot, seq_ends[None], 0), axis=1)
    row_lengths = jnp.sum(jnp.where(owner_hot, all_lengths[None], 0), axis=1)
    finished = (row_ends <= slot[:, None]).astype(jnp.int32)
    sequence_starts = slot - jnp.sum(finished * row_lengths, axis=1)

    local_heads = w_query.shape[1] // head_dim
    local_kv = key_projection_weight.shape[1] // head_dim
    query_group_count = local_heads // local_kv

    def project(rows_x, starts):
        count = rows_x.shape[0]
        values_wide = rows_x.astype(jnp.float32)
        normalized_input = (
            values_wide
            * lax.rsqrt(jnp.mean(values_wide * values_wide, axis=-1, keepdims=True) + norm_eps)
            * norm_gain
        ).astype(jnp.bfloat16)
        query_matrix = (
            jnp.dot(normalized_input, w_query, preferred_element_type=jnp.float32) + q_bias
        )
        key_value = jnp.dot(
            normalized_input,
            jnp.concatenate([key_projection_weight, value_projection_weight], axis=1),
            preferred_element_type=jnp.float32,
        ) + jnp.concatenate([key_bias_vector, value_bias_vector])
        kv_cols = key_projection_weight.shape[1]
        query_matrix, key_value = lax.optimization_barrier((query_matrix, key_value))
        key_rows = key_value[:, :kv_cols]
        query_matrix = apply_rotary(
            query_matrix.reshape(count, local_heads, head_dim), starts, head_dim
        ).astype(jnp.bfloat16)
        key_rows = apply_rotary(
            key_rows.reshape(count, local_kv, head_dim), starts, head_dim
        ).astype(jnp.bfloat16)
        value_rows = key_value[:, kv_cols:].astype(jnp.bfloat16)
        return jnp.concatenate(
            [
                query_matrix.reshape(count, local_heads * head_dim),
                key_rows.reshape(count, local_kv * head_dim),
                value_rows,
            ],
            axis=1,
        )

    qkv = project(jnp.concatenate(pieces, axis=0), sequence_starts)

    shift_order = ctx_count <= 8
    if shift_order:
        shifted_dest = jnp.where(
            my_dest >= 0,
            ((my_dest // pack_len - ctx_index) % ctx_count) * pack_len + my_dest % pack_len,
            -1,
        )
    else:
        shifted_dest = my_dest
    places = to_work_order(send_places(shifted_dest, ctx_count, group_cap, pack_len))
    send_hot = (
        places[None, :] == jnp.arange(ctx_count * group_cap, dtype=jnp.int32)[:, None]
    ).astype(jnp.bfloat16)
    outgoing = jnp.dot(send_hot, qkv, preferred_element_type=jnp.float32).astype(jnp.bfloat16)
    arrived = exchange(outgoing, "ctx", ctx_count)

    mine = (pool_dest >= 0) & (pool_dest // pack_len == ctx_index)
    mine_grid = mine.reshape(ctx_count, group_rows).astype(jnp.int32)
    rank_in = jnp.cumsum(mine_grid, axis=1) - mine_grid
    source_ctx = jnp.arange(ctx_count, dtype=jnp.int32)[:, None]
    if shift_order:
        source_ctx = (ctx_index - source_ctx) % ctx_count
    arrived_index = (
        source_ctx * group_cap + rank_in
    ).reshape(-1)
    my_slot_of_row = jnp.where(mine, pool_dest - ctx_index * pack_len, -1)
    slot_ids = jnp.arange(pack_len, dtype=jnp.int32)
    names_slot = my_slot_of_row[None, :] == slot_ids[:, None]
    source_of_slot = jnp.sum(jnp.where(names_slot, arrived_index[None, :], 0), axis=1)
    packed_qkv = select_rows(source_of_slot, arrived)

    q_width = local_heads * head_dim
    kv_width = local_kv * head_dim
    query_matrix = packed_qkv[:, :q_width].reshape(pack_len, local_kv, query_group_count, head_dim)
    projected_key_rows = packed_qkv[:, q_width : q_width + kv_width].reshape(
        pack_len, local_kv, head_dim
    )
    projected_value_rows = packed_qkv[:, q_width + kv_width :].reshape(pack_len, local_kv, head_dim)

    own_lengths = seq_len[0]
    own_ends = jnp.cumsum(own_lengths).astype(jnp.int32)
    segment = jnp.sum((own_ends[None, :] <= slot_ids[:, None]).astype(jnp.int32), axis=1)

    score_scale = 1.0 / math.sqrt(head_dim)
    chunk_count = 4 if pack_len % 32 == 0 else 1
    chunk_len = pack_len // chunk_count
    results = []
    for chunk in range(chunk_count):
        lo, hi = chunk * chunk_len, (chunk + 1) * chunk_len
        scores = (
            jnp.einsum(
                "qkgd,tkd->kgqt",
                query_matrix[lo:hi],
                projected_key_rows[:hi],
                preferred_element_type=jnp.float32,
            )
            * score_scale
        )
        allowed = (segment[lo:hi, None] == segment[None, :hi]) & (
            slot_ids[None, :hi] <= slot_ids[lo:hi, None]
        )
        scores = jnp.where(allowed[None, None], scores, -1e30)
        row_max = jnp.max(scores, axis=-1, keepdims=True)
        weights = jnp.exp(scores - row_max)
        row_total = jnp.sum(weights, axis=-1, keepdims=True)
        probability = (weights / row_total).astype(jnp.bfloat16)
        mixed_heads = jnp.einsum(
            "kgqt,tkd->qkgd",
            probability,
            projected_value_rows[:hi],
            preferred_element_type=jnp.float32,
        )
        mixed_heads = mixed_heads.astype(jnp.bfloat16).reshape(chunk_len, local_heads * head_dim)
        partial_out = jnp.dot(mixed_heads, w_out, preferred_element_type=jnp.float32)
        results.append(halving_scatter(partial_out, "head", head_count).astype(jnp.bfloat16))
    return jnp.concatenate(results, axis=0)


def shift_gather(part, axis_name, count):
    if count > 8:
        return doubling_gather(part, axis_name, count)
    me = lax.axis_index(axis_name)
    by_shift = [part] + [
        lax.ppermute(part, axis_name, [(i, (i + shift) % count) for i in range(count)])
        for shift in range(1, count)
    ]
    stacked = jnp.stack(by_shift)
    return jnp.take(stacked, (me - jnp.arange(count)) % count, axis=0).reshape(
        (count * part.shape[0],) + part.shape[1:]
    )


def exchange(outgoing, axis_name, count):
    if count > 8:
        return lax.all_to_all(outgoing, axis_name, split_axis=0, concat_axis=0, tiled=True)
    chunks = outgoing.reshape((count, -1) + outgoing.shape[1:])
    arrived = [chunks[0]]
    for shift in range(1, count):
        pairs = [(i, (i + shift) % count) for i in range(count)]
        arrived.append(lax.ppermute(chunks[shift], axis_name, pairs))
    return jnp.concatenate(arrived, axis=0)


def halving_scatter(partial, axis_name, count):
    bits = count.bit_length() - 1
    if count != 1 << bits or bits == 0:
        return lax.psum_scatter(partial, axis_name, scatter_dimension=1, tiled=True)
    block = partial.shape[1] // count
    me = lax.axis_index(axis_name)
    pieces = [(b, partial[:, b * block : (b + 1) * block]) for b in range(count)]
    for stage in range(bits):
        bit = (me >> stage) & 1
        lows = [(b, x) for b, x in pieces if not (b >> stage) & 1]
        highs = [x for b, x in pieces if (b >> stage) & 1]
        keep = [jnp.where(bit == 0, lo, hi) for (_, lo), hi in zip(lows, highs)]
        send = jnp.stack([jnp.where(bit == 0, hi, lo) for (_, lo), hi in zip(lows, highs)])
        pairs = [(i, i ^ (1 << stage)) for i in range(count)]
        got = lax.ppermute(send, axis_name, pairs)
        pieces = [(b, k + got[i]) for i, ((b, _), k) in enumerate(zip(lows, keep))]
    return pieces[0][1]


def doubling_gather(part, axis_name, count):
    bits = count.bit_length() - 1
    if count != 1 << bits or bits == 0:
        return lax.all_gather(part, axis_name, tiled=True)
    me = lax.axis_index(axis_name)
    have = part[None]
    for stage in reversed(range(bits)):
        bit = (me >> stage) & 1
        pairs = [(i, i ^ (1 << stage)) for i in range(count)]
        got = lax.ppermute(have, axis_name, pairs)
        first = jnp.where(bit == 0, have, got)
        second = jnp.where(bit == 0, got, have)
        have = jnp.stack([first, second], axis=1).reshape((-1,) + part.shape)
    return have.reshape((count * part.shape[0],) + part.shape[1:])


def xor_gather(part, axis_name, count):
    me = lax.axis_index(axis_name)
    bits = count.bit_length() - 1
    if count != 1 << bits:
        return [lax.all_gather(part, axis_name, tiled=True)], jnp.arange(count, dtype=jnp.int32)
    pieces, masks = [part], [0]
    for stage in reversed(range(bits)):
        pairs = [(i, i ^ (1 << stage)) for i in range(count)]
        pieces = pieces + [lax.ppermute(p, axis_name, pairs) for p in pieces]
        masks = masks + [m ^ (1 << stage) for m in masks]
    return pieces, me ^ jnp.asarray(masks, dtype=jnp.int32)


def solution(mesh):
    in_specs = (
        P(("ctx", "head"), None),
        P(),
        P("ctx", None),
        P(),
        P(None, "head"),
        P("head"),
        P(None, "head"),
        P("head"),
        P(None, "head"),
        P("head"),
        P("head", None),
    )
    out_specs = P("ctx", "head")
    return jax.shard_map(local, mesh=mesh, in_specs=in_specs, out_specs=out_specs, check_vma=False)
```

```python
import math

import jax
import jax.numpy as jnp
from jax import lax
from jax.sharding import PartitionSpec as P

HEAD_SIZE = 128
PACKED_SLOTS = 256


rope_base = 1000000.0
norm_eps = 1e-06


def send_places(targets, owner_count, capacity, pack_len):
    is_filled = targets >= 0
    owner_ids = jnp.where(is_filled, targets // pack_len, -1)
    membership = (owner_ids[:, None] == jnp.arange(owner_count, dtype=jnp.int32)[None, :]).astype(
        jnp.int32
    )
    earlier = jnp.cumsum(membership, axis=0) - membership
    rank_in = jnp.sum(earlier * membership, axis=1)
    return jnp.where(is_filled, owner_ids * capacity + rank_in, owner_count * capacity)


def one_hot_rows(index, count):
    return (index[:, None] == jnp.arange(count, dtype=jnp.int32)[None, :]).astype(jnp.bfloat16)


def select_rows(index, values):
    picked = jnp.dot(
        one_hot_rows(index, values.shape[0]), values, preferred_element_type=jnp.float32
    )
    return picked.astype(values.dtype)


def apply_rotary(values, sequence_starts, head_dim):
    half_dim = head_dim // 2
    frequency = jnp.exp(
        jnp.arange(half_dim, dtype=jnp.float32) * (-2.0 * math.log(rope_base) / head_dim)
    )
    angles = sequence_starts.astype(jnp.float32)[:, None] * frequency[None, :]
    cosine = jnp.cos(angles)[:, None, :]
    sine_table = jnp.sin(angles)[:, None, :]
    first_half = values[..., :half_dim]
    second_half = values[..., half_dim:]
    return jnp.concatenate(
        [
            first_half * cosine - second_half * sine_table,
            second_half * cosine + first_half * sine_table,
        ],
        axis=-1,
    )


def local(
    x_pool,
    pool_dest,
    seq_len,
    norm_gain,
    w_query,
    q_bias,
    key_projection_weight,
    key_bias_vector,
    value_projection_weight,
    value_bias_vector,
    w_out,
):
    ctx_count = lax.axis_size("ctx")
    head_count = lax.axis_size("head")
    pool_rows = x_pool.shape[0]
    capacity = pool_rows // ctx_count
    group_rows = pool_rows * head_count
    group_cap = capacity * head_count
    pack_len = PACKED_SLOTS
    head_dim = HEAD_SIZE
    ctx_index = lax.axis_index("ctx")

    all_lengths = shift_gather(seq_len, "ctx", ctx_count)
    pieces, work_heads = xor_gather(x_pool, "head", head_count)

    dest_grid = pool_dest.reshape(ctx_count, group_rows)
    my_dest = lax.dynamic_index_in_dim(dest_grid, ctx_index, 0, keepdims=False)
    to_work_order = lambda v: jnp.take(
        v.reshape(head_count, pool_rows), work_heads, axis=0
    ).reshape(-1)
    work_dest = to_work_order(my_dest)
    is_filled = work_dest >= 0
    owner = jnp.where(is_filled, work_dest // pack_len, 0)
    slot = jnp.where(is_filled, work_dest % pack_len, 0)
    seq_ends = jnp.cumsum(all_lengths, axis=1).astype(jnp.int32)
    owner_hot = owner[:, None, None] == jnp.arange(ctx_count, dtype=jnp.int32)[None, :, None]
    row_ends = jnp.sum(jnp.where(owner_hot, seq_ends[None], 0), axis=1)
    row_lengths = jnp.sum(jnp.where(owner_hot, all_lengths[None], 0), axis=1)
    finished = (row_ends <= slot[:, None]).astype(jnp.int32)
    sequence_starts = slot - jnp.sum(finished * row_lengths, axis=1)

    local_heads = w_query.shape[1] // head_dim
    local_kv = key_projection_weight.shape[1] // head_dim
    query_group_count = local_heads // local_kv

    def project(rows_x, starts):
        count = rows_x.shape[0]
        values_wide = rows_x.astype(jnp.float32)
        normalized_input = (
            values_wide
            * lax.rsqrt(jnp.mean(values_wide * values_wide, axis=-1, keepdims=True) + norm_eps)
            * norm_gain
        ).astype(jnp.bfloat16)
        query_matrix = (
            jnp.dot(normalized_input, w_query, preferred_element_type=jnp.float32) + q_bias
        )
        key_value = jnp.dot(
            normalized_input,
            jnp.concatenate([key_projection_weight, value_projection_weight], axis=1),
            preferred_element_type=jnp.float32,
        ) + jnp.concatenate([key_bias_vector, value_bias_vector])
        kv_cols = key_projection_weight.shape[1]
        query_matrix, key_value = lax.optimization_barrier((query_matrix, key_value))
        key_rows = key_value[:, :kv_cols]
        query_matrix = apply_rotary(
            query_matrix.reshape(count, local_heads, head_dim), starts, head_dim
        ).astype(jnp.bfloat16)
        key_rows = apply_rotary(
            key_rows.reshape(count, local_kv, head_dim), starts, head_dim
        ).astype(jnp.bfloat16)
        value_rows = key_value[:, kv_cols:].astype(jnp.bfloat16)
        return jnp.concatenate(
            [
                query_matrix.reshape(count, local_heads * head_dim),
                key_rows.reshape(count, local_kv * head_dim),
                value_rows,
            ],
            axis=1,
        )

    qkv = project(jnp.concatenate(pieces, axis=0), sequence_starts)

    shift_order = ctx_count <= 8
    if shift_order:
        shifted_dest = jnp.where(
            my_dest >= 0,
            ((my_dest // pack_len - ctx_index) % ctx_count) * pack_len + my_dest % pack_len,
            -1,
        )
    else:
        shifted_dest = my_dest
    places = to_work_order(send_places(shifted_dest, ctx_count, group_cap, pack_len))
    send_hot = (
        places[None, :] == jnp.arange(ctx_count * group_cap, dtype=jnp.int32)[:, None]
    ).astype(jnp.bfloat16)
    outgoing = jnp.dot(send_hot, qkv, preferred_element_type=jnp.float32).astype(jnp.bfloat16)
    arrived = exchange(outgoing, "ctx", ctx_count)

    mine = (pool_dest >= 0) & (pool_dest // pack_len == ctx_index)
    mine_grid = mine.reshape(ctx_count, group_rows).astype(jnp.int32)
    rank_in = jnp.cumsum(mine_grid, axis=1) - mine_grid
    source_ctx = jnp.arange(ctx_count, dtype=jnp.int32)[:, None]
    if shift_order:
        source_ctx = (ctx_index - source_ctx) % ctx_count
    arrived_index = (
        source_ctx * group_cap + rank_in
    ).reshape(-1)
    my_slot_of_row = jnp.where(mine, pool_dest - ctx_index * pack_len, -1)
    slot_ids = jnp.arange(pack_len, dtype=jnp.int32)
    names_slot = my_slot_of_row[None, :] == slot_ids[:, None]
    source_of_slot = jnp.sum(jnp.where(names_slot, arrived_index[None, :], 0), axis=1)
    packed_qkv = select_rows(source_of_slot, arrived)

    q_width = local_heads * head_dim
    kv_width = local_kv * head_dim
    query_matrix = packed_qkv[:, :q_width].reshape(pack_len, local_kv, query_group_count, head_dim)
    projected_key_rows = packed_qkv[:, q_width : q_width + kv_width].reshape(
        pack_len, local_kv, head_dim
    )
    projected_value_rows = packed_qkv[:, q_width + kv_width :].reshape(pack_len, local_kv, head_dim)

    own_lengths = seq_len[0]
    own_ends = jnp.cumsum(own_lengths).astype(jnp.int32)
    segment = jnp.sum((own_ends[None, :] <= slot_ids[:, None]).astype(jnp.int32), axis=1)

    score_scale = 1.0 / math.sqrt(head_dim)
    chunk_count = 8 if pack_len % 64 == 0 else 1
    chunk_len = pack_len // chunk_count
    results = []
    for chunk in range(chunk_count):
        lo, hi = chunk * chunk_len, (chunk + 1) * chunk_len
        scores = (
            jnp.einsum(
                "qkgd,tkd->kgqt",
                query_matrix[lo:hi],
                projected_key_rows[:hi],
                preferred_element_type=jnp.float32,
            )
            * score_scale
        )
        allowed = (segment[lo:hi, None] == segment[None, :hi]) & (
            slot_ids[None, :hi] <= slot_ids[lo:hi, None]
        )
        scores = jnp.where(allowed[None, None], scores, -1e30)
        row_max = jnp.max(scores, axis=-1, keepdims=True)
        weights = jnp.exp(scores - row_max)
        row_total = jnp.sum(weights, axis=-1, keepdims=True)
        probability = (weights / row_total).astype(jnp.bfloat16)
        mixed_heads = jnp.einsum(
            "kgqt,tkd->qkgd",
            probability,
            projected_value_rows[:hi],
            preferred_element_type=jnp.float32,
        )
        mixed_heads = mixed_heads.astype(jnp.bfloat16).reshape(chunk_len, local_heads * head_dim)
        partial_out = jnp.dot(mixed_heads, w_out, preferred_element_type=jnp.float32)
        results.append(halving_scatter(partial_out, "head", head_count).astype(jnp.bfloat16))
    return jnp.concatenate(results, axis=0)


def shift_gather(part, axis_name, count):
    if count > 8:
        return doubling_gather(part, axis_name, count)
    me = lax.axis_index(axis_name)
    by_shift = [part] + [
        lax.ppermute(part, axis_name, [(i, (i + shift) % count) for i in range(count)])
        for shift in range(1, count)
    ]
    stacked = jnp.stack(by_shift)
    return jnp.take(stacked, (me - jnp.arange(count)) % count, axis=0).reshape(
        (count * part.shape[0],) + part.shape[1:]
    )


def exchange(outgoing, axis_name, count):
    if count > 8:
        return lax.all_to_all(outgoing, axis_name, split_axis=0, concat_axis=0, tiled=True)
    chunks = outgoing.reshape((count, -1) + outgoing.shape[1:])
    arrived = [chunks[0]]
    for shift in range(1, count):
        pairs = [(i, (i + shift) % count) for i in range(count)]
        arrived.append(lax.ppermute(chunks[shift], axis_name, pairs))
    return jnp.concatenate(arrived, axis=0)


def halving_scatter(partial, axis_name, count):
    bits = count.bit_length() - 1
    if count != 1 << bits or bits == 0:
        return lax.psum_scatter(partial, axis_name, scatter_dimension=1, tiled=True)
    block = partial.shape[1] // count
    me = lax.axis_index(axis_name)
    pieces = [(b, partial[:, b * block : (b + 1) * block]) for b in range(count)]
    for stage in range(bits):
        bit = (me >> stage) & 1
        lows = [(b, x) for b, x in pieces if not (b >> stage) & 1]
        highs = [x for b, x in pieces if (b >> stage) & 1]
        keep = [jnp.where(bit == 0, lo, hi) for (_, lo), hi in zip(lows, highs)]
        send = jnp.stack([jnp.where(bit == 0, hi, lo) for (_, lo), hi in zip(lows, highs)])
        pairs = [(i, i ^ (1 << stage)) for i in range(count)]
        got = lax.ppermute(send, axis_name, pairs)
        pieces = [(b, k + got[i]) for i, ((b, _), k) in enumerate(zip(lows, keep))]
    return pieces[0][1]


def doubling_gather(part, axis_name, count):
    bits = count.bit_length() - 1
    if count != 1 << bits or bits == 0:
        return lax.all_gather(part, axis_name, tiled=True)
    me = lax.axis_index(axis_name)
    have = part[None]
    for stage in reversed(range(bits)):
        bit = (me >> stage) & 1
        pairs = [(i, i ^ (1 << stage)) for i in range(count)]
        got = lax.ppermute(have, axis_name, pairs)
        first = jnp.where(bit == 0, have, got)
        second = jnp.where(bit == 0, got, have)
        have = jnp.stack([first, second], axis=1).reshape((-1,) + part.shape)
    return have.reshape((count * part.shape[0],) + part.shape[1:])


def xor_gather(part, axis_name, count):
    me = lax.axis_index(axis_name)
    bits = count.bit_length() - 1
    if count != 1 << bits:
        return [lax.all_gather(part, axis_name, tiled=True)], jnp.arange(count, dtype=jnp.int32)
    pieces, masks = [part], [0]
    for stage in reversed(range(bits)):
        pairs = [(i, i ^ (1 << stage)) for i in range(count)]
        pieces = pieces + [lax.ppermute(p, axis_name, pairs) for p in pieces]
        masks = masks + [m ^ (1 << stage) for m in masks]
    return pieces, me ^ jnp.asarray(masks, dtype=jnp.int32)


def solution(mesh):
    in_specs = (
        P(("ctx", "head"), None),
        P(),
        P("ctx", None),
        P(),
        P(None, "head"),
        P("head"),
        P(None, "head"),
        P("head"),
        P(None, "head"),
        P("head"),
        P("head", None),
    )
    out_specs = P("ctx", "head")
    return jax.shard_map(local, mesh=mesh, in_specs=in_specs, out_specs=out_specs, check_vma=False)
```

```python
import math

import jax
import jax.numpy as jnp
from jax import lax
from jax.sharding import PartitionSpec as P

HEAD_SIZE = 128
PACKED_SLOTS = 256


rope_base = 1000000.0
norm_eps = 1e-06


def send_places(targets, owner_count, capacity, pack_len):
    is_filled = targets >= 0
    owner_ids = jnp.where(is_filled, targets // pack_len, -1)
    membership = (owner_ids[:, None] == jnp.arange(owner_count, dtype=jnp.int32)[None, :]).astype(
        jnp.int32
    )
    earlier = jnp.cumsum(membership, axis=0) - membership
    rank_in = jnp.sum(earlier * membership, axis=1)
    return jnp.where(is_filled, owner_ids * capacity + rank_in, owner_count * capacity)


def one_hot_rows(index, count):
    return (index[:, None] == jnp.arange(count, dtype=jnp.int32)[None, :]).astype(jnp.bfloat16)


def select_rows(index, values):
    picked = jnp.dot(
        one_hot_rows(index, values.shape[0]), values, preferred_element_type=jnp.float32
    )
    return picked.astype(values.dtype)


def apply_rotary(values, sequence_starts, head_dim):
    half_dim = head_dim // 2
    frequency = jnp.exp(
        jnp.arange(half_dim, dtype=jnp.float32) * (-2.0 * math.log(rope_base) / head_dim)
    )
    angles = sequence_starts.astype(jnp.float32)[:, None] * frequency[None, :]
    cosine = jnp.cos(angles)[:, None, :]
    sine_table = jnp.sin(angles)[:, None, :]
    first_half = values[..., :half_dim]
    second_half = values[..., half_dim:]
    return jnp.concatenate(
        [
            first_half * cosine - second_half * sine_table,
            second_half * cosine + first_half * sine_table,
        ],
        axis=-1,
    )


def local(
    x_pool,
    pool_dest,
    seq_len,
    norm_gain,
    w_query,
    q_bias,
    key_projection_weight,
    key_bias_vector,
    value_projection_weight,
    value_bias_vector,
    w_out,
):
    ctx_count = lax.axis_size("ctx")
    head_count = lax.axis_size("head")
    pool_rows = x_pool.shape[0]
    capacity = pool_rows // ctx_count
    group_rows = pool_rows * head_count
    group_cap = capacity * head_count
    pack_len = PACKED_SLOTS
    head_dim = HEAD_SIZE
    ctx_index = lax.axis_index("ctx")

    all_lengths = shift_gather(seq_len, "ctx", ctx_count)
    pieces, work_heads = xor_gather(x_pool, "head", head_count)

    dest_grid = pool_dest.reshape(ctx_count, group_rows)
    my_dest = lax.dynamic_index_in_dim(dest_grid, ctx_index, 0, keepdims=False)
    to_work_order = lambda v: jnp.take(
        v.reshape(head_count, pool_rows), work_heads, axis=0
    ).reshape(-1)
    work_dest = to_work_order(my_dest)
    is_filled = work_dest >= 0
    owner = jnp.where(is_filled, work_dest // pack_len, 0)
    slot = jnp.where(is_filled, work_dest % pack_len, 0)
    seq_ends = jnp.cumsum(all_lengths, axis=1).astype(jnp.int32)
    owner_hot = owner[:, None, None] == jnp.arange(ctx_count, dtype=jnp.int32)[None, :, None]
    row_ends = jnp.sum(jnp.where(owner_hot, seq_ends[None], 0), axis=1)
    row_lengths = jnp.sum(jnp.where(owner_hot, all_lengths[None], 0), axis=1)
    finished = (row_ends <= slot[:, None]).astype(jnp.int32)
    sequence_starts = slot - jnp.sum(finished * row_lengths, axis=1)

    local_heads = w_query.shape[1] // head_dim
    local_kv = key_projection_weight.shape[1] // head_dim
    query_group_count = local_heads // local_kv

    def project(rows_x, starts):
        count = rows_x.shape[0]
        values_wide = rows_x.astype(jnp.float32)
        normalized_input = (
            values_wide
            * lax.rsqrt(jnp.mean(values_wide * values_wide, axis=-1, keepdims=True) + norm_eps)
            * norm_gain
        ).astype(jnp.bfloat16)
        query_matrix = (
            jnp.dot(normalized_input, w_query, preferred_element_type=jnp.float32) + q_bias
        )
        key_value = jnp.dot(
            normalized_input,
            jnp.concatenate([key_projection_weight, value_projection_weight], axis=1),
            preferred_element_type=jnp.float32,
        ) + jnp.concatenate([key_bias_vector, value_bias_vector])
        kv_cols = key_projection_weight.shape[1]
        query_matrix, key_value = lax.optimization_barrier((query_matrix, key_value))
        key_rows = key_value[:, :kv_cols]
        query_matrix = apply_rotary(
            query_matrix.reshape(count, local_heads, head_dim), starts, head_dim
        ).astype(jnp.bfloat16)
        key_rows = apply_rotary(
            key_rows.reshape(count, local_kv, head_dim), starts, head_dim
        ).astype(jnp.bfloat16)
        value_rows = key_value[:, kv_cols:].astype(jnp.bfloat16)
        return jnp.concatenate(
            [
                query_matrix.reshape(count, local_heads * head_dim),
                key_rows.reshape(count, local_kv * head_dim),
                value_rows,
            ],
            axis=1,
        )

    qkv = project(jnp.concatenate(pieces, axis=0), sequence_starts)

    shift_order = ctx_count <= 8
    if shift_order:
        shifted_dest = jnp.where(
            my_dest >= 0,
            ((my_dest // pack_len - ctx_index) % ctx_count) * pack_len + my_dest % pack_len,
            -1,
        )
    else:
        shifted_dest = my_dest
    places = to_work_order(send_places(shifted_dest, ctx_count, group_cap, pack_len))
    send_hot = (
        places[None, :] == jnp.arange(ctx_count * group_cap, dtype=jnp.int32)[:, None]
    ).astype(jnp.bfloat16)
    outgoing = jnp.dot(send_hot, qkv, preferred_element_type=jnp.float32).astype(jnp.bfloat16)
    arrived = exchange(outgoing, "ctx", ctx_count)

    mine = (pool_dest >= 0) & (pool_dest // pack_len == ctx_index)
    mine_grid = mine.reshape(ctx_count, group_rows).astype(jnp.int32)
    rank_in = jnp.cumsum(mine_grid, axis=1) - mine_grid
    source_ctx = jnp.arange(ctx_count, dtype=jnp.int32)[:, None]
    if shift_order:
        source_ctx = (ctx_index - source_ctx) % ctx_count
    arrived_index = (
        source_ctx * group_cap + rank_in
    ).reshape(-1)
    my_slot_of_row = jnp.where(mine, pool_dest - ctx_index * pack_len, -1)
    slot_ids = jnp.arange(pack_len, dtype=jnp.int32)
    names_slot = my_slot_of_row[None, :] == slot_ids[:, None]
    source_of_slot = jnp.sum(jnp.where(names_slot, arrived_index[None, :], 0), axis=1)
    packed_qkv = select_rows(source_of_slot, arrived)

    q_width = local_heads * head_dim
    kv_width = local_kv * head_dim
    query_matrix = packed_qkv[:, :q_width].reshape(pack_len, local_kv, query_group_count, head_dim)
    projected_key_rows = packed_qkv[:, q_width : q_width + kv_width].reshape(
        pack_len, local_kv, head_dim
    )
    projected_value_rows = packed_qkv[:, q_width + kv_width :].reshape(pack_len, local_kv, head_dim)

    own_lengths = seq_len[0]
    own_ends = jnp.cumsum(own_lengths).astype(jnp.int32)
    segment = jnp.sum((own_ends[None, :] <= slot_ids[:, None]).astype(jnp.int32), axis=1)

    score_scale = 1.0 / math.sqrt(head_dim)
    chunk_count = 2 if pack_len % 16 == 0 else 1
    chunk_len = pack_len // chunk_count
    results = []
    for chunk in range(chunk_count):
        lo, hi = chunk * chunk_len, (chunk + 1) * chunk_len
        scores = (
            jnp.einsum(
                "qkgd,tkd->kgqt",
                query_matrix[lo:hi],
                projected_key_rows[:hi],
                preferred_element_type=jnp.float32,
            )
            * score_scale
        )
        allowed = (segment[lo:hi, None] == segment[None, :hi]) & (
            slot_ids[None, :hi] <= slot_ids[lo:hi, None]
        )
        scores = jnp.where(allowed[None, None], scores, -1e30)
        row_max = jnp.max(scores, axis=-1, keepdims=True)
        weights = jnp.exp(scores - row_max)
        row_total = jnp.sum(weights, axis=-1, keepdims=True)
        probability = (weights / row_total).astype(jnp.bfloat16)
        mixed_heads = jnp.einsum(
            "kgqt,tkd->qkgd",
            probability,
            projected_value_rows[:hi],
            preferred_element_type=jnp.float32,
        )
        mixed_heads = mixed_heads.astype(jnp.bfloat16).reshape(chunk_len, local_heads * head_dim)
        partial_out = jnp.dot(mixed_heads, w_out, preferred_element_type=jnp.float32)
        results.append(halving_scatter(partial_out, "head", head_count).astype(jnp.bfloat16))
    return jnp.concatenate(results, axis=0)


def shift_gather(part, axis_name, count):
    if count > 8:
        return doubling_gather(part, axis_name, count)
    me = lax.axis_index(axis_name)
    by_shift = [part] + [
        lax.ppermute(part, axis_name, [(i, (i + shift) % count) for i in range(count)])
        for shift in range(1, count)
    ]
    stacked = jnp.stack(by_shift)
    return jnp.take(stacked, (me - jnp.arange(count)) % count, axis=0).reshape(
        (count * part.shape[0],) + part.shape[1:]
    )


def exchange(outgoing, axis_name, count):
    if count > 8:
        return lax.all_to_all(outgoing, axis_name, split_axis=0, concat_axis=0, tiled=True)
    chunks = outgoing.reshape((count, -1) + outgoing.shape[1:])
    arrived = [chunks[0]]
    for shift in range(1, count):
        pairs = [(i, (i + shift) % count) for i in range(count)]
        arrived.append(lax.ppermute(chunks[shift], axis_name, pairs))
    return jnp.concatenate(arrived, axis=0)


def halving_scatter(partial, axis_name, count):
    bits = count.bit_length() - 1
    if count != 1 << bits or bits == 0:
        return lax.psum_scatter(partial, axis_name, scatter_dimension=1, tiled=True)
    block = partial.shape[1] // count
    me = lax.axis_index(axis_name)
    pieces = [(b, partial[:, b * block : (b + 1) * block]) for b in range(count)]
    for stage in range(bits):
        bit = (me >> stage) & 1
        lows = [(b, x) for b, x in pieces if not (b >> stage) & 1]
        highs = [x for b, x in pieces if (b >> stage) & 1]
        keep = [jnp.where(bit == 0, lo, hi) for (_, lo), hi in zip(lows, highs)]
        send = jnp.stack([jnp.where(bit == 0, hi, lo) for (_, lo), hi in zip(lows, highs)])
        pairs = [(i, i ^ (1 << stage)) for i in range(count)]
        got = lax.ppermute(send, axis_name, pairs)
        pieces = [(b, k + got[i]) for i, ((b, _), k) in enumerate(zip(lows, keep))]
    return pieces[0][1]


def doubling_gather(part, axis_name, count):
    bits = count.bit_length() - 1
    if count != 1 << bits or bits == 0:
        return lax.all_gather(part, axis_name, tiled=True)
    me = lax.axis_index(axis_name)
    have = part[None]
    for stage in reversed(range(bits)):
        bit = (me >> stage) & 1
        pairs = [(i, i ^ (1 << stage)) for i in range(count)]
        got = lax.ppermute(have, axis_name, pairs)
        first = jnp.where(bit == 0, have, got)
        second = jnp.where(bit == 0, got, have)
        have = jnp.stack([first, second], axis=1).reshape((-1,) + part.shape)
    return have.reshape((count * part.shape[0],) + part.shape[1:])


def xor_gather(part, axis_name, count):
    me = lax.axis_index(axis_name)
    bits = count.bit_length() - 1
    if count != 1 << bits:
        return [lax.all_gather(part, axis_name, tiled=True)], jnp.arange(count, dtype=jnp.int32)
    pieces, masks = [part], [0]
    for stage in reversed(range(bits)):
        pairs = [(i, i ^ (1 << stage)) for i in range(count)]
        pieces = pieces + [lax.ppermute(p, axis_name, pairs) for p in pieces]
        masks = masks + [m ^ (1 << stage) for m in masks]
    return pieces, me ^ jnp.asarray(masks, dtype=jnp.int32)


def solution(mesh):
    in_specs = (
        P(("ctx", "head"), None),
        P(),
        P("ctx", None),
        P(),
        P(None, "head"),
        P("head"),
        P(None, "head"),
        P("head"),
        P(None, "head"),
        P("head"),
        P("head", None),
    )
    out_specs = P("ctx", "head")
    return jax.shard_map(local, mesh=mesh, in_specs=in_specs, out_specs=out_specs, check_vma=False)
```

```python
import math

import jax
import jax.numpy as jnp
from jax import lax
from jax.sharding import PartitionSpec as P

HEAD_SIZE = 128
PACKED_SLOTS = 256


rope_base = 1000000.0
norm_eps = 1e-06


def send_places(targets, owner_count, capacity, pack_len):
    is_filled = targets >= 0
    owner_ids = jnp.where(is_filled, targets // pack_len, -1)
    membership = (owner_ids[:, None] == jnp.arange(owner_count, dtype=jnp.int32)[None, :]).astype(
        jnp.int32
    )
    earlier = jnp.cumsum(membership, axis=0) - membership
    rank_in = jnp.sum(earlier * membership, axis=1)
    return jnp.where(is_filled, owner_ids * capacity + rank_in, owner_count * capacity)


def one_hot_rows(index, count):
    return (index[:, None] == jnp.arange(count, dtype=jnp.int32)[None, :]).astype(jnp.bfloat16)


def select_rows(index, values):
    picked = jnp.dot(
        one_hot_rows(index, values.shape[0]), values, preferred_element_type=jnp.float32
    )
    return picked.astype(values.dtype)


def apply_rotary(values, sequence_starts, head_dim):
    half_dim = head_dim // 2
    frequency = jnp.exp(
        jnp.arange(half_dim, dtype=jnp.float32) * (-2.0 * math.log(rope_base) / head_dim)
    )
    angles = sequence_starts.astype(jnp.float32)[:, None] * frequency[None, :]
    cosine = jnp.cos(angles)[:, None, :]
    sine_table = jnp.sin(angles)[:, None, :]
    first_half = values[..., :half_dim]
    second_half = values[..., half_dim:]
    return jnp.concatenate(
        [
            first_half * cosine - second_half * sine_table,
            second_half * cosine + first_half * sine_table,
        ],
        axis=-1,
    )


def local(
    x_pool,
    pool_dest,
    seq_len,
    norm_gain,
    w_query,
    q_bias,
    key_projection_weight,
    key_bias_vector,
    value_projection_weight,
    value_bias_vector,
    w_out,
):
    ctx_count = lax.axis_size("ctx")
    head_count = lax.axis_size("head")
    pool_rows = x_pool.shape[0]
    capacity = pool_rows // ctx_count
    group_rows = pool_rows * head_count
    group_cap = capacity * head_count
    pack_len = PACKED_SLOTS
    head_dim = HEAD_SIZE
    ctx_index = lax.axis_index("ctx")

    all_lengths = shift_gather(seq_len, "ctx", ctx_count)
    pieces, work_heads = xor_gather(x_pool, "head", head_count)

    dest_grid = pool_dest.reshape(ctx_count, group_rows)
    my_dest = lax.dynamic_index_in_dim(dest_grid, ctx_index, 0, keepdims=False)
    to_work_order = lambda v: jnp.take(
        v.reshape(head_count, pool_rows), work_heads, axis=0
    ).reshape(-1)
    work_dest = to_work_order(my_dest)
    is_filled = work_dest >= 0
    owner = jnp.where(is_filled, work_dest // pack_len, 0)
    slot = jnp.where(is_filled, work_dest % pack_len, 0)
    seq_ends = jnp.cumsum(all_lengths, axis=1).astype(jnp.int32)
    owner_hot = owner[:, None, None] == jnp.arange(ctx_count, dtype=jnp.int32)[None, :, None]
    row_ends = jnp.sum(jnp.where(owner_hot, seq_ends[None], 0), axis=1)
    row_lengths = jnp.sum(jnp.where(owner_hot, all_lengths[None], 0), axis=1)
    finished = (row_ends <= slot[:, None]).astype(jnp.int32)
    sequence_starts = slot - jnp.sum(finished * row_lengths, axis=1)

    local_heads = w_query.shape[1] // head_dim
    local_kv = key_projection_weight.shape[1] // head_dim
    query_group_count = local_heads // local_kv

    def project(rows_x, starts):
        count = rows_x.shape[0]
        values_wide = rows_x.astype(jnp.float32)
        normalized_input = (
            values_wide
            * lax.rsqrt(jnp.mean(values_wide * values_wide, axis=-1, keepdims=True) + norm_eps)
            * norm_gain
        ).astype(jnp.bfloat16)
        query_matrix = (
            jnp.dot(normalized_input, w_query, preferred_element_type=jnp.float32) + q_bias
        )
        key_value = jnp.dot(
            normalized_input,
            jnp.concatenate([key_projection_weight, value_projection_weight], axis=1),
            preferred_element_type=jnp.float32,
        ) + jnp.concatenate([key_bias_vector, value_bias_vector])
        kv_cols = key_projection_weight.shape[1]
        query_matrix, key_value = lax.optimization_barrier((query_matrix, key_value))
        key_rows = key_value[:, :kv_cols]
        query_matrix = apply_rotary(
            query_matrix.reshape(count, local_heads, head_dim), starts, head_dim
        ).astype(jnp.bfloat16)
        key_rows = apply_rotary(
            key_rows.reshape(count, local_kv, head_dim), starts, head_dim
        ).astype(jnp.bfloat16)
        value_rows = key_value[:, kv_cols:].astype(jnp.bfloat16)
        return jnp.concatenate(
            [
                query_matrix.reshape(count, local_heads * head_dim),
                key_rows.reshape(count, local_kv * head_dim),
                value_rows,
            ],
            axis=1,
        )

    qkv = project(jnp.concatenate(pieces, axis=0), sequence_starts)

    shift_order = ctx_count <= 8
    if shift_order:
        shifted_dest = jnp.where(
            my_dest >= 0,
            ((my_dest // pack_len - ctx_index) % ctx_count) * pack_len + my_dest % pack_len,
            -1,
        )
    else:
        shifted_dest = my_dest
    places = to_work_order(send_places(shifted_dest, ctx_count, group_cap, pack_len))
    send_hot = (
        places[None, :] == jnp.arange(ctx_count * group_cap, dtype=jnp.int32)[:, None]
    ).astype(jnp.bfloat16)
    outgoing = jnp.dot(send_hot, qkv, preferred_element_type=jnp.float32).astype(jnp.bfloat16)
    arrived = exchange(outgoing, "ctx", ctx_count)

    mine = (pool_dest >= 0) & (pool_dest // pack_len == ctx_index)
    mine_grid = mine.reshape(ctx_count, group_rows).astype(jnp.int32)
    rank_in = jnp.cumsum(mine_grid, axis=1) - mine_grid
    source_ctx = jnp.arange(ctx_count, dtype=jnp.int32)[:, None]
    if shift_order:
        source_ctx = (ctx_index - source_ctx) % ctx_count
    arrived_index = (
        source_ctx * group_cap + rank_in
    ).reshape(-1)
    my_slot_of_row = jnp.where(mine, pool_dest - ctx_index * pack_len, -1)
    slot_ids = jnp.arange(pack_len, dtype=jnp.int32)
    names_slot = my_slot_of_row[None, :] == slot_ids[:, None]
    source_of_slot = jnp.sum(jnp.where(names_slot, arrived_index[None, :], 0), axis=1)
    packed_qkv = select_rows(source_of_slot, arrived)

    q_width = local_heads * head_dim
    kv_width = local_kv * head_dim
    query_matrix = packed_qkv[:, :q_width].reshape(pack_len, local_kv, query_group_count, head_dim)
    projected_key_rows = packed_qkv[:, q_width : q_width + kv_width].reshape(
        pack_len, local_kv, head_dim
    )
    projected_value_rows = packed_qkv[:, q_width + kv_width :].reshape(pack_len, local_kv, head_dim)

    own_lengths = seq_len[0]
    own_ends = jnp.cumsum(own_lengths).astype(jnp.int32)
    segment = jnp.sum((own_ends[None, :] <= slot_ids[:, None]).astype(jnp.int32), axis=1)

    score_scale = 1.0 / math.sqrt(head_dim)
    chunk_count = 4 if pack_len % 32 == 0 else 1
    chunk_len = pack_len // chunk_count
    results = []
    for chunk in range(chunk_count):
        lo, hi = chunk * chunk_len, (chunk + 1) * chunk_len
        scores = (
            jnp.einsum(
                "qkgd,tkd->kgqt",
                query_matrix[lo:hi],
                projected_key_rows[:hi],
                preferred_element_type=jnp.float32,
            )
            * score_scale
        )
        allowed = (segment[lo:hi, None] == segment[None, :hi]) & (
            slot_ids[None, :hi] <= slot_ids[lo:hi, None]
        )
        scores = jnp.where(allowed[None, None], scores, -1e30)
        row_max = jnp.max(scores, axis=-1, keepdims=True)
        weights = jnp.exp(scores - row_max)
        row_total = jnp.sum(weights, axis=-1, keepdims=True)
        probability = (weights / row_total).astype(jnp.bfloat16)
        mixed_heads = jnp.einsum(
            "kgqt,tkd->qkgd",
            probability,
            projected_value_rows[:hi],
            preferred_element_type=jnp.float32,
        )
        mixed_heads = mixed_heads.astype(jnp.bfloat16).reshape(chunk_len, local_heads * head_dim)
        partial_out = jnp.dot(mixed_heads, w_out, preferred_element_type=jnp.float32)
        results.append(halving_scatter(partial_out, "head", head_count).astype(jnp.bfloat16))
    return jnp.concatenate(results, axis=0)


def shift_gather(part, axis_name, count):
    if count > 8:
        return doubling_gather(part, axis_name, count)
    me = lax.axis_index(axis_name)
    by_shift = [part] + [
        lax.ppermute(part, axis_name, [(i, (i + shift) % count) for i in range(count)])
        for shift in range(1, count)
    ]
    stacked = jnp.stack(by_shift)
    return jnp.take(stacked, (me - jnp.arange(count)) % count, axis=0).reshape(
        (count * part.shape[0],) + part.shape[1:]
    )


def exchange(outgoing, axis_name, count):
    if count > 8:
        return lax.all_to_all(outgoing, axis_name, split_axis=0, concat_axis=0, tiled=True)
    chunks = outgoing.reshape((count, -1) + outgoing.shape[1:])
    arrived = [chunks[0]]
    for shift in range(1, count):
        pairs = [(i, (i + shift) % count) for i in range(count)]
        arrived.append(lax.ppermute(chunks[shift], axis_name, pairs))
    return jnp.concatenate(arrived, axis=0)


def halving_scatter(partial, axis_name, count):
    bits = count.bit_length() - 1
    if count != 1 << bits or bits == 0:
        return lax.psum_scatter(partial, axis_name, scatter_dimension=1, tiled=True)
    block = partial.shape[1] // count
    me = lax.axis_index(axis_name)
    pieces = [(b, partial[:, b * block : (b + 1) * block]) for b in range(count)]
    for stage in range(bits):
        bit = (me >> stage) & 1
        lows = [(b, x) for b, x in pieces if not (b >> stage) & 1]
        highs = [x for b, x in pieces if (b >> stage) & 1]
        keep = [jnp.where(bit == 0, lo, hi) for (_, lo), hi in zip(lows, highs)]
        send = jnp.stack([jnp.where(bit == 0, hi, lo) for (_, lo), hi in zip(lows, highs)])
        pairs = [(i, i ^ (1 << stage)) for i in range(count)]
        got = lax.ppermute(send, axis_name, pairs)
        pieces = [(b, k + got[i]) for i, ((b, _), k) in enumerate(zip(lows, keep))]
    return pieces[0][1]


def doubling_gather(part, axis_name, count):
    bits = count.bit_length() - 1
    if count != 1 << bits or bits == 0:
        return lax.all_gather(part, axis_name, tiled=True)
    me = lax.axis_index(axis_name)
    have = part[None]
    for stage in reversed(range(bits)):
        bit = (me >> stage) & 1
        pairs = [(i, i ^ (1 << stage)) for i in range(count)]
        got = lax.ppermute(have, axis_name, pairs)
        first = jnp.where(bit == 0, have, got)
        second = jnp.where(bit == 0, got, have)
        have = jnp.stack([first, second], axis=1).reshape((-1,) + part.shape)
    return have.reshape((count * part.shape[0],) + part.shape[1:])


def xor_gather(part, axis_name, count):
    me = lax.axis_index(axis_name)
    bits = count.bit_length() - 1
    if count != 1 << bits:
        return [lax.all_gather(part, axis_name, tiled=True)], jnp.arange(count, dtype=jnp.int32)
    pieces, masks = [part], [0]
    for stage in reversed(range(bits)):
        pairs = [(i, i ^ (1 << stage)) for i in range(count)]
        sent = pieces
        if stage == bits - 1 and part.shape[0] % 16 == 0:
            half = part.shape[0] // 2
            sent = [part[:half], part[half:]]
        pieces = pieces + [lax.ppermute(p, axis_name, pairs) for p in sent]
        masks = masks + [m ^ (1 << stage) for m in masks]
    return pieces, me ^ jnp.asarray(masks, dtype=jnp.int32)


def solution(mesh):
    in_specs = (
        P(("ctx", "head"), None),
        P(),
        P("ctx", None),
        P(),
        P(None, "head"),
        P("head"),
        P(None, "head"),
        P("head"),
        P(None, "head"),
        P("head"),
        P("head", None),
    )
    out_specs = P("ctx", "head")
    return jax.shard_map(local, mesh=mesh, in_specs=in_specs, out_specs=out_specs, check_vma=False)
```

```python
import math

import jax
import jax.numpy as jnp
from jax import lax
from jax.sharding import PartitionSpec as P

HEAD_SIZE = 128
PACKED_SLOTS = 256


rope_base = 1000000.0
norm_eps = 1e-06


def send_places(targets, owner_count, capacity, pack_len):
    is_filled = targets >= 0
    owner_ids = jnp.where(is_filled, targets // pack_len, -1)
    membership = (owner_ids[:, None] == jnp.arange(owner_count, dtype=jnp.int32)[None, :]).astype(
        jnp.int32
    )
    earlier = jnp.cumsum(membership, axis=0) - membership
    rank_in = jnp.sum(earlier * membership, axis=1)
    return jnp.where(is_filled, owner_ids * capacity + rank_in, owner_count * capacity)


def one_hot_rows(index, count):
    return (index[:, None] == jnp.arange(count, dtype=jnp.int32)[None, :]).astype(jnp.bfloat16)


def select_rows(index, values):
    return jnp.dot(one_hot_rows(index, values.shape[0]), values, preferred_element_type=values.dtype)


def apply_rotary(values, sequence_starts, head_dim):
    half_dim = head_dim // 2
    frequency = jnp.exp(
        jnp.arange(half_dim, dtype=jnp.float32) * (-2.0 * math.log(rope_base) / head_dim)
    )
    angles = sequence_starts.astype(jnp.float32)[:, None] * frequency[None, :]
    cosine = jnp.cos(angles)[:, None, :]
    sine_table = jnp.sin(angles)[:, None, :]
    first_half = values[..., :half_dim]
    second_half = values[..., half_dim:]
    return jnp.concatenate(
        [
            first_half * cosine - second_half * sine_table,
            second_half * cosine + first_half * sine_table,
        ],
        axis=-1,
    )


def local(
    x_pool,
    pool_dest,
    seq_len,
    norm_gain,
    w_query,
    q_bias,
    key_projection_weight,
    key_bias_vector,
    value_projection_weight,
    value_bias_vector,
    w_out,
):
    ctx_count = lax.axis_size("ctx")
    head_count = lax.axis_size("head")
    pool_rows = x_pool.shape[0]
    capacity = pool_rows // ctx_count
    group_rows = pool_rows * head_count
    group_cap = capacity * head_count
    pack_len = PACKED_SLOTS
    head_dim = HEAD_SIZE
    ctx_index = lax.axis_index("ctx")

    all_lengths = shift_gather(seq_len, "ctx", ctx_count)
    pieces, work_heads = xor_gather(x_pool, "head", head_count)

    dest_grid = pool_dest.reshape(ctx_count, group_rows)
    my_dest = lax.dynamic_index_in_dim(dest_grid, ctx_index, 0, keepdims=False)
    to_work_order = lambda v: jnp.take(
        v.reshape(head_count, pool_rows), work_heads, axis=0
    ).reshape(-1)
    work_dest = to_work_order(my_dest)
    is_filled = work_dest >= 0
    owner = jnp.where(is_filled, work_dest // pack_len, 0)
    slot = jnp.where(is_filled, work_dest % pack_len, 0)
    seq_ends = jnp.cumsum(all_lengths, axis=1).astype(jnp.int32)
    owner_hot = owner[:, None, None] == jnp.arange(ctx_count, dtype=jnp.int32)[None, :, None]
    row_ends = jnp.sum(jnp.where(owner_hot, seq_ends[None], 0), axis=1)
    row_lengths = jnp.sum(jnp.where(owner_hot, all_lengths[None], 0), axis=1)
    finished = (row_ends <= slot[:, None]).astype(jnp.int32)
    sequence_starts = slot - jnp.sum(finished * row_lengths, axis=1)

    local_heads = w_query.shape[1] // head_dim
    local_kv = key_projection_weight.shape[1] // head_dim
    query_group_count = local_heads // local_kv

    def project(rows_x, starts):
        count = rows_x.shape[0]
        values_wide = rows_x.astype(jnp.float32)
        normalized_input = (
            values_wide
            * lax.rsqrt(jnp.mean(values_wide * values_wide, axis=-1, keepdims=True) + norm_eps)
            * norm_gain
        ).astype(jnp.bfloat16)
        query_matrix = (
            jnp.dot(normalized_input, w_query, preferred_element_type=jnp.float32) + q_bias
        )
        key_value = jnp.dot(
            normalized_input,
            jnp.concatenate([key_projection_weight, value_projection_weight], axis=1),
            preferred_element_type=jnp.float32,
        ) + jnp.concatenate([key_bias_vector, value_bias_vector])
        kv_cols = key_projection_weight.shape[1]
        query_matrix, key_value = lax.optimization_barrier((query_matrix, key_value))
        key_rows = key_value[:, :kv_cols]
        query_matrix = apply_rotary(
            query_matrix.reshape(count, local_heads, head_dim), starts, head_dim
        ).astype(jnp.bfloat16)
        key_rows = apply_rotary(
            key_rows.reshape(count, local_kv, head_dim), starts, head_dim
        ).astype(jnp.bfloat16)
        value_rows = key_value[:, kv_cols:].astype(jnp.bfloat16)
        return jnp.concatenate(
            [
                query_matrix.reshape(count, local_heads * head_dim),
                key_rows.reshape(count, local_kv * head_dim),
                value_rows,
            ],
            axis=1,
        )

    qkv = project(jnp.concatenate(pieces, axis=0), sequence_starts)

    shift_order = ctx_count <= 8
    if shift_order:
        shifted_dest = jnp.where(
            my_dest >= 0,
            ((my_dest // pack_len - ctx_index) % ctx_count) * pack_len + my_dest % pack_len,
            -1,
        )
    else:
        shifted_dest = my_dest
    places = to_work_order(send_places(shifted_dest, ctx_count, group_cap, pack_len))
    send_hot = (
        places[None, :] == jnp.arange(ctx_count * group_cap, dtype=jnp.int32)[:, None]
    ).astype(jnp.bfloat16)
    outgoing = jnp.dot(send_hot, qkv, preferred_element_type=jnp.bfloat16)
    arrived = exchange(outgoing, "ctx", ctx_count)

    mine = (pool_dest >= 0) & (pool_dest // pack_len == ctx_index)
    mine_grid = mine.reshape(ctx_count, group_rows).astype(jnp.int32)
    rank_in = jnp.cumsum(mine_grid, axis=1) - mine_grid
    source_ctx = jnp.arange(ctx_count, dtype=jnp.int32)[:, None]
    if shift_order:
        source_ctx = (ctx_index - source_ctx) % ctx_count
    arrived_index = (
        source_ctx * group_cap + rank_in
    ).reshape(-1)
    my_slot_of_row = jnp.where(mine, pool_dest - ctx_index * pack_len, -1)
    slot_ids = jnp.arange(pack_len, dtype=jnp.int32)
    names_slot = my_slot_of_row[None, :] == slot_ids[:, None]
    source_of_slot = jnp.sum(jnp.where(names_slot, arrived_index[None, :], 0), axis=1)
    packed_qkv = select_rows(source_of_slot, arrived)

    q_width = local_heads * head_dim
    kv_width = local_kv * head_dim
    query_matrix = packed_qkv[:, :q_width].reshape(pack_len, local_kv, query_group_count, head_dim)
    projected_key_rows = packed_qkv[:, q_width : q_width + kv_width].reshape(
        pack_len, local_kv, head_dim
    )
    projected_value_rows = packed_qkv[:, q_width + kv_width :].reshape(pack_len, local_kv, head_dim)

    own_lengths = seq_len[0]
    own_ends = jnp.cumsum(own_lengths).astype(jnp.int32)
    segment = jnp.sum((own_ends[None, :] <= slot_ids[:, None]).astype(jnp.int32), axis=1)

    score_scale = 1.0 / math.sqrt(head_dim)
    chunk_count = 4 if pack_len % 32 == 0 else 1
    chunk_len = pack_len // chunk_count
    results = []
    for chunk in range(chunk_count):
        lo, hi = chunk * chunk_len, (chunk + 1) * chunk_len
        scores = (
            jnp.einsum(
                "qkgd,tkd->kgqt",
                query_matrix[lo:hi],
                projected_key_rows[:hi],
                preferred_element_type=jnp.float32,
            )
            * score_scale
        )
        allowed = (segment[lo:hi, None] == segment[None, :hi]) & (
            slot_ids[None, :hi] <= slot_ids[lo:hi, None]
        )
        scores = jnp.where(allowed[None, None], scores, -1e30)
        row_max = jnp.max(scores, axis=-1, keepdims=True)
        weights = jnp.exp(scores - row_max)
        row_total = jnp.sum(weights, axis=-1, keepdims=True)
        probability = (weights / row_total).astype(jnp.bfloat16)
        mixed_heads = jnp.einsum(
            "kgqt,tkd->qkgd",
            probability,
            projected_value_rows[:hi],
            preferred_element_type=jnp.float32,
        )
        mixed_heads = mixed_heads.astype(jnp.bfloat16).reshape(chunk_len, local_heads * head_dim)
        partial_out = jnp.dot(mixed_heads, w_out, preferred_element_type=jnp.float32)
        results.append(halving_scatter(partial_out, "head", head_count).astype(jnp.bfloat16))
    return jnp.concatenate(results, axis=0)


def shift_gather(part, axis_name, count):
    if count > 8:
        return doubling_gather(part, axis_name, count)
    me = lax.axis_index(axis_name)
    by_shift = [part] + [
        lax.ppermute(part, axis_name, [(i, (i + shift) % count) for i in range(count)])
        for shift in range(1, count)
    ]
    stacked = jnp.stack(by_shift)
    return jnp.take(stacked, (me - jnp.arange(count)) % count, axis=0).reshape(
        (count * part.shape[0],) + part.shape[1:]
    )


def exchange(outgoing, axis_name, count):
    if count > 8:
        return lax.all_to_all(outgoing, axis_name, split_axis=0, concat_axis=0, tiled=True)
    chunks = outgoing.reshape((count, -1) + outgoing.shape[1:])
    arrived = [chunks[0]]
    for shift in range(1, count):
        pairs = [(i, (i + shift) % count) for i in range(count)]
        arrived.append(lax.ppermute(chunks[shift], axis_name, pairs))
    return jnp.concatenate(arrived, axis=0)


def halving_scatter(partial, axis_name, count):
    bits = count.bit_length() - 1
    if count != 1 << bits or bits == 0:
        return lax.psum_scatter(partial, axis_name, scatter_dimension=1, tiled=True)
    block = partial.shape[1] // count
    me = lax.axis_index(axis_name)
    pieces = [(b, partial[:, b * block : (b + 1) * block]) for b in range(count)]
    for stage in range(bits):
        bit = (me >> stage) & 1
        lows = [(b, x) for b, x in pieces if not (b >> stage) & 1]
        highs = [x for b, x in pieces if (b >> stage) & 1]
        keep = [jnp.where(bit == 0, lo, hi) for (_, lo), hi in zip(lows, highs)]
        send = jnp.stack([jnp.where(bit == 0, hi, lo) for (_, lo), hi in zip(lows, highs)])
        pairs = [(i, i ^ (1 << stage)) for i in range(count)]
        got = lax.ppermute(send, axis_name, pairs)
        pieces = [(b, k + got[i]) for i, ((b, _), k) in enumerate(zip(lows, keep))]
    return pieces[0][1]


def doubling_gather(part, axis_name, count):
    bits = count.bit_length() - 1
    if count != 1 << bits or bits == 0:
        return lax.all_gather(part, axis_name, tiled=True)
    me = lax.axis_index(axis_name)
    have = part[None]
    for stage in reversed(range(bits)):
        bit = (me >> stage) & 1
        pairs = [(i, i ^ (1 << stage)) for i in range(count)]
        got = lax.ppermute(have, axis_name, pairs)
        first = jnp.where(bit == 0, have, got)
        second = jnp.where(bit == 0, got, have)
        have = jnp.stack([first, second], axis=1).reshape((-1,) + part.shape)
    return have.reshape((count * part.shape[0],) + part.shape[1:])


def xor_gather(part, axis_name, count):
    me = lax.axis_index(axis_name)
    bits = count.bit_length() - 1
    if count != 1 << bits:
        return [lax.all_gather(part, axis_name, tiled=True)], jnp.arange(count, dtype=jnp.int32)
    pieces, masks = [part], [0]
    for stage in reversed(range(bits)):
        pairs = [(i, i ^ (1 << stage)) for i in range(count)]
        pieces = pieces + [lax.ppermute(p, axis_name, pairs) for p in pieces]
        masks = masks + [m ^ (1 << stage) for m in masks]
    return pieces, me ^ jnp.asarray(masks, dtype=jnp.int32)


def solution(mesh):
    in_specs = (
        P(("ctx", "head"), None),
        P(),
        P("ctx", None),
        P(),
        P(None, "head"),
        P("head"),
        P(None, "head"),
        P("head"),
        P(None, "head"),
        P("head"),
        P("head", None),
    )
    out_specs = P("ctx", "head")
    return jax.shard_map(local, mesh=mesh, in_specs=in_specs, out_specs=out_specs, check_vma=False)
```

```python
import math

import jax
import jax.numpy as jnp
from jax import lax
from jax.sharding import PartitionSpec as P

HEAD_SIZE = 128
PACKED_SLOTS = 256


rope_base = 1000000.0
norm_eps = 1e-06


def send_places(targets, owner_count, capacity, pack_len):
    is_filled = targets >= 0
    owner_ids = jnp.where(is_filled, targets // pack_len, -1)
    membership = (owner_ids[:, None] == jnp.arange(owner_count, dtype=jnp.int32)[None, :]).astype(
        jnp.int32
    )
    earlier = jnp.cumsum(membership, axis=0) - membership
    rank_in = jnp.sum(earlier * membership, axis=1)
    return jnp.where(is_filled, owner_ids * capacity + rank_in, owner_count * capacity)


def one_hot_rows(index, count):
    return (index[:, None] == jnp.arange(count, dtype=jnp.int32)[None, :]).astype(jnp.bfloat16)


def select_rows(index, values):
    picked = jnp.dot(
        one_hot_rows(index, values.shape[0]), values, preferred_element_type=jnp.float32
    )
    return picked.astype(values.dtype)


def apply_rotary(values, sequence_starts, head_dim):
    half_dim = head_dim // 2
    frequency = jnp.exp(
        jnp.arange(half_dim, dtype=jnp.float32) * (-2.0 * math.log(rope_base) / head_dim)
    )
    angles = sequence_starts.astype(jnp.float32)[:, None] * frequency[None, :]
    cosine = jnp.cos(angles)[:, None, :]
    sine_table = jnp.sin(angles)[:, None, :]
    first_half = values[..., :half_dim]
    second_half = values[..., half_dim:]
    return jnp.concatenate(
        [
            first_half * cosine - second_half * sine_table,
            second_half * cosine + first_half * sine_table,
        ],
        axis=-1,
    )


def local(
    x_pool,
    pool_dest,
    seq_len,
    norm_gain,
    w_query,
    q_bias,
    key_projection_weight,
    key_bias_vector,
    value_projection_weight,
    value_bias_vector,
    w_out,
):
    ctx_count = lax.axis_size("ctx")
    head_count = lax.axis_size("head")
    pool_rows = x_pool.shape[0]
    capacity = pool_rows // ctx_count
    group_rows = pool_rows * head_count
    group_cap = capacity * head_count
    pack_len = PACKED_SLOTS
    head_dim = HEAD_SIZE
    ctx_index = lax.axis_index("ctx")

    all_lengths = shift_gather(seq_len, "ctx", ctx_count)
    pieces, work_heads = xor_gather(x_pool, "head", head_count)

    dest_grid = pool_dest.reshape(ctx_count, group_rows)
    my_dest = lax.dynamic_index_in_dim(dest_grid, ctx_index, 0, keepdims=False)
    to_work_order = lambda v: jnp.take(
        v.reshape(head_count, pool_rows), work_heads, axis=0
    ).reshape(-1)
    work_dest = to_work_order(my_dest)
    is_filled = work_dest >= 0
    owner = jnp.where(is_filled, work_dest // pack_len, 0)
    slot = jnp.where(is_filled, work_dest % pack_len, 0)
    seq_ends = jnp.cumsum(all_lengths, axis=1).astype(jnp.int32)
    owner_hot = owner[:, None, None] == jnp.arange(ctx_count, dtype=jnp.int32)[None, :, None]
    row_ends = jnp.sum(jnp.where(owner_hot, seq_ends[None], 0), axis=1)
    row_lengths = jnp.sum(jnp.where(owner_hot, all_lengths[None], 0), axis=1)
    finished = (row_ends <= slot[:, None]).astype(jnp.int32)
    sequence_starts = slot - jnp.sum(finished * row_lengths, axis=1)

    local_heads = w_query.shape[1] // head_dim
    local_kv = key_projection_weight.shape[1] // head_dim
    query_group_count = local_heads // local_kv

    def project(rows_x, starts):
        count = rows_x.shape[0]
        values_wide = rows_x.astype(jnp.float32)
        normalized_input = (
            values_wide
            * lax.rsqrt(jnp.mean(values_wide * values_wide, axis=-1, keepdims=True) + norm_eps)
            * norm_gain
        ).astype(jnp.bfloat16)
        query_matrix = (
            jnp.dot(normalized_input, w_query, preferred_element_type=jnp.float32) + q_bias
        )
        key_value = jnp.dot(
            normalized_input,
            jnp.concatenate([key_projection_weight, value_projection_weight], axis=1),
            preferred_element_type=jnp.float32,
        ) + jnp.concatenate([key_bias_vector, value_bias_vector])
        kv_cols = key_projection_weight.shape[1]
        query_matrix, key_value = lax.optimization_barrier((query_matrix, key_value))
        key_rows = key_value[:, :kv_cols]
        query_matrix = apply_rotary(
            query_matrix.reshape(count, local_heads, head_dim), starts, head_dim
        ).astype(jnp.bfloat16)
        key_rows = apply_rotary(
            key_rows.reshape(count, local_kv, head_dim), starts, head_dim
        ).astype(jnp.bfloat16)
        value_rows = key_value[:, kv_cols:].astype(jnp.bfloat16)
        return [
            query_matrix.reshape(count, local_heads * head_dim),
            key_rows.reshape(count, local_kv * head_dim),
            value_rows,
        ]

    qkv = project(jnp.concatenate(pieces, axis=0), sequence_starts)

    shift_order = ctx_count <= 8
    if shift_order:
        shifted_dest = jnp.where(
            my_dest >= 0,
            ((my_dest // pack_len - ctx_index) % ctx_count) * pack_len + my_dest % pack_len,
            -1,
        )
    else:
        shifted_dest = my_dest
    places = to_work_order(send_places(shifted_dest, ctx_count, group_cap, pack_len))
    send_hot = (
        places[None, :] == jnp.arange(ctx_count * group_cap, dtype=jnp.int32)[:, None]
    ).astype(jnp.bfloat16)
    outgoing = jnp.concatenate(
        [
            jnp.dot(send_hot, part, preferred_element_type=jnp.float32).astype(jnp.bfloat16)
            for part in qkv
        ],
        axis=1,
    )
    arrived = exchange(outgoing, "ctx", ctx_count)

    mine = (pool_dest >= 0) & (pool_dest // pack_len == ctx_index)
    mine_grid = mine.reshape(ctx_count, group_rows).astype(jnp.int32)
    rank_in = jnp.cumsum(mine_grid, axis=1) - mine_grid
    source_ctx = jnp.arange(ctx_count, dtype=jnp.int32)[:, None]
    if shift_order:
        source_ctx = (ctx_index - source_ctx) % ctx_count
    arrived_index = (
        source_ctx * group_cap + rank_in
    ).reshape(-1)
    my_slot_of_row = jnp.where(mine, pool_dest - ctx_index * pack_len, -1)
    slot_ids = jnp.arange(pack_len, dtype=jnp.int32)
    names_slot = my_slot_of_row[None, :] == slot_ids[:, None]
    source_of_slot = jnp.sum(jnp.where(names_slot, arrived_index[None, :], 0), axis=1)
    packed_qkv = select_rows(source_of_slot, arrived)

    q_width = local_heads * head_dim
    kv_width = local_kv * head_dim
    query_matrix = packed_qkv[:, :q_width].reshape(pack_len, local_kv, query_group_count, head_dim)
    projected_key_rows = packed_qkv[:, q_width : q_width + kv_width].reshape(
        pack_len, local_kv, head_dim
    )
    projected_value_rows = packed_qkv[:, q_width + kv_width :].reshape(pack_len, local_kv, head_dim)

    own_lengths = seq_len[0]
    own_ends = jnp.cumsum(own_lengths).astype(jnp.int32)
    segment = jnp.sum((own_ends[None, :] <= slot_ids[:, None]).astype(jnp.int32), axis=1)

    score_scale = 1.0 / math.sqrt(head_dim)
    chunk_count = 4 if pack_len % 32 == 0 else 1
    chunk_len = pack_len // chunk_count
    results = []
    for chunk in range(chunk_count):
        lo, hi = chunk * chunk_len, (chunk + 1) * chunk_len
        scores = (
            jnp.einsum(
                "qkgd,tkd->kgqt",
                query_matrix[lo:hi],
                projected_key_rows[:hi],
                preferred_element_type=jnp.float32,
            )
            * score_scale
        )
        allowed = (segment[lo:hi, None] == segment[None, :hi]) & (
            slot_ids[None, :hi] <= slot_ids[lo:hi, None]
        )
        scores = jnp.where(allowed[None, None], scores, -1e30)
        row_max = jnp.max(scores, axis=-1, keepdims=True)
        weights = jnp.exp(scores - row_max)
        row_total = jnp.sum(weights, axis=-1, keepdims=True)
        probability = (weights / row_total).astype(jnp.bfloat16)
        mixed_heads = jnp.einsum(
            "kgqt,tkd->qkgd",
            probability,
            projected_value_rows[:hi],
            preferred_element_type=jnp.float32,
        )
        mixed_heads = mixed_heads.astype(jnp.bfloat16).reshape(chunk_len, local_heads * head_dim)
        partial_out = jnp.dot(mixed_heads, w_out, preferred_element_type=jnp.float32)
        results.append(halving_scatter(partial_out, "head", head_count).astype(jnp.bfloat16))
    return jnp.concatenate(results, axis=0)


def shift_gather(part, axis_name, count):
    if count > 8:
        return doubling_gather(part, axis_name, count)
    me = lax.axis_index(axis_name)
    by_shift = [part] + [
        lax.ppermute(part, axis_name, [(i, (i + shift) % count) for i in range(count)])
        for shift in range(1, count)
    ]
    stacked = jnp.stack(by_shift)
    return jnp.take(stacked, (me - jnp.arange(count)) % count, axis=0).reshape(
        (count * part.shape[0],) + part.shape[1:]
    )


def exchange(outgoing, axis_name, count):
    if count > 8:
        return lax.all_to_all(outgoing, axis_name, split_axis=0, concat_axis=0, tiled=True)
    chunks = outgoing.reshape((count, -1) + outgoing.shape[1:])
    arrived = [chunks[0]]
    for shift in range(1, count):
        pairs = [(i, (i + shift) % count) for i in range(count)]
        arrived.append(lax.ppermute(chunks[shift], axis_name, pairs))
    return jnp.concatenate(arrived, axis=0)


def halving_scatter(partial, axis_name, count):
    bits = count.bit_length() - 1
    if count != 1 << bits or bits == 0:
        return lax.psum_scatter(partial, axis_name, scatter_dimension=1, tiled=True)
    block = partial.shape[1] // count
    me = lax.axis_index(axis_name)
    pieces = [(b, partial[:, b * block : (b + 1) * block]) for b in range(count)]
    for stage in range(bits):
        bit = (me >> stage) & 1
        lows = [(b, x) for b, x in pieces if not (b >> stage) & 1]
        highs = [x for b, x in pieces if (b >> stage) & 1]
        keep = [jnp.where(bit == 0, lo, hi) for (_, lo), hi in zip(lows, highs)]
        send = jnp.stack([jnp.where(bit == 0, hi, lo) for (_, lo), hi in zip(lows, highs)])
        pairs = [(i, i ^ (1 << stage)) for i in range(count)]
        got = lax.ppermute(send, axis_name, pairs)
        pieces = [(b, k + got[i]) for i, ((b, _), k) in enumerate(zip(lows, keep))]
    return pieces[0][1]


def doubling_gather(part, axis_name, count):
    bits = count.bit_length() - 1
    if count != 1 << bits or bits == 0:
        return lax.all_gather(part, axis_name, tiled=True)
    me = lax.axis_index(axis_name)
    have = part[None]
    for stage in reversed(range(bits)):
        bit = (me >> stage) & 1
        pairs = [(i, i ^ (1 << stage)) for i in range(count)]
        got = lax.ppermute(have, axis_name, pairs)
        first = jnp.where(bit == 0, have, got)
        second = jnp.where(bit == 0, got, have)
        have = jnp.stack([first, second], axis=1).reshape((-1,) + part.shape)
    return have.reshape((count * part.shape[0],) + part.shape[1:])


def xor_gather(part, axis_name, count):
    me = lax.axis_index(axis_name)
    bits = count.bit_length() - 1
    if count != 1 << bits:
        return [lax.all_gather(part, axis_name, tiled=True)], jnp.arange(count, dtype=jnp.int32)
    pieces, masks = [part], [0]
    for stage in reversed(range(bits)):
        pairs = [(i, i ^ (1 << stage)) for i in range(count)]
        pieces = pieces + [lax.ppermute(p, axis_name, pairs) for p in pieces]
        masks = masks + [m ^ (1 << stage) for m in masks]
    return pieces, me ^ jnp.asarray(masks, dtype=jnp.int32)


def solution(mesh):
    in_specs = (
        P(("ctx", "head"), None),
        P(),
        P("ctx", None),
        P(),
        P(None, "head"),
        P("head"),
        P(None, "head"),
        P("head"),
        P(None, "head"),
        P("head"),
        P("head", None),
    )
    out_specs = P("ctx", "head")
    return jax.shard_map(local, mesh=mesh, in_specs=in_specs, out_specs=out_specs, check_vma=False)
```

```python
import math

import jax
import jax.numpy as jnp
from jax import lax
from jax.sharding import PartitionSpec as P

HEAD_SIZE = 128
PACKED_SLOTS = 256


rope_base = 1000000.0
norm_eps = 1e-06


def send_places(targets, owner_count, capacity, pack_len):
    is_filled = targets >= 0
    owner_ids = jnp.where(is_filled, targets // pack_len, -1)
    membership = (owner_ids[:, None] == jnp.arange(owner_count, dtype=jnp.int32)[None, :]).astype(
        jnp.int32
    )
    earlier = jnp.cumsum(membership, axis=0) - membership
    rank_in = jnp.sum(earlier * membership, axis=1)
    return jnp.where(is_filled, owner_ids * capacity + rank_in, owner_count * capacity)


def one_hot_rows(index, count):
    return (index[:, None] == jnp.arange(count, dtype=jnp.int32)[None, :]).astype(jnp.bfloat16)


def select_rows(index, values):
    picked = jnp.dot(
        one_hot_rows(index, values.shape[0]), values, preferred_element_type=jnp.float32
    )
    return picked.astype(values.dtype)


def apply_rotary(values, sequence_starts, head_dim):
    half_dim = head_dim // 2
    frequency = jnp.exp(
        jnp.arange(half_dim, dtype=jnp.float32) * (-2.0 * math.log(rope_base) / head_dim)
    )
    angles = sequence_starts.astype(jnp.float32)[:, None] * frequency[None, :]
    cosine = jnp.cos(angles)[:, None, :]
    sine_table = jnp.sin(angles)[:, None, :]
    first_half = values[..., :half_dim]
    second_half = values[..., half_dim:]
    return jnp.concatenate(
        [
            first_half * cosine - second_half * sine_table,
            second_half * cosine + first_half * sine_table,
        ],
        axis=-1,
    )


def local(
    x_pool,
    pool_dest,
    seq_len,
    norm_gain,
    w_query,
    q_bias,
    key_projection_weight,
    key_bias_vector,
    value_projection_weight,
    value_bias_vector,
    w_out,
):
    ctx_count = lax.axis_size("ctx")
    head_count = lax.axis_size("head")
    pool_rows = x_pool.shape[0]
    capacity = pool_rows // ctx_count
    group_rows = pool_rows * head_count
    group_cap = capacity * head_count
    pack_len = PACKED_SLOTS
    head_dim = HEAD_SIZE
    ctx_index = lax.axis_index("ctx")

    all_lengths = shift_gather(seq_len, "ctx", ctx_count)
    pieces, work_heads = xor_gather(x_pool, "head", head_count)

    dest_grid = pool_dest.reshape(ctx_count, group_rows)
    my_dest = lax.dynamic_index_in_dim(dest_grid, ctx_index, 0, keepdims=False)
    to_work_order = lambda v: jnp.take(
        v.reshape(head_count, pool_rows), work_heads, axis=0
    ).reshape(-1)
    work_dest = to_work_order(my_dest)
    is_filled = work_dest >= 0
    owner = jnp.where(is_filled, work_dest // pack_len, 0)
    slot = jnp.where(is_filled, work_dest % pack_len, 0)
    seq_ends = jnp.cumsum(all_lengths, axis=1).astype(jnp.int32)
    owner_hot = owner[:, None, None] == jnp.arange(ctx_count, dtype=jnp.int32)[None, :, None]
    row_ends = jnp.sum(jnp.where(owner_hot, seq_ends[None], 0), axis=1)
    row_lengths = jnp.sum(jnp.where(owner_hot, all_lengths[None], 0), axis=1)
    finished = (row_ends <= slot[:, None]).astype(jnp.int32)
    sequence_starts = slot - jnp.sum(finished * row_lengths, axis=1)

    local_heads = w_query.shape[1] // head_dim
    local_kv = key_projection_weight.shape[1] // head_dim
    query_group_count = local_heads // local_kv

    def project(rows_x, starts):
        count = rows_x.shape[0]
        values_wide = rows_x.astype(jnp.float32)
        normalized_input = (
            values_wide
            * lax.rsqrt(jnp.mean(values_wide * values_wide, axis=-1, keepdims=True) + norm_eps)
            * norm_gain
        ).astype(jnp.bfloat16)
        query_matrix = (
            jnp.dot(normalized_input, w_query, preferred_element_type=jnp.float32) + q_bias
        )
        key_value = jnp.dot(
            normalized_input,
            jnp.concatenate([key_projection_weight, value_projection_weight], axis=1),
            preferred_element_type=jnp.float32,
        ) + jnp.concatenate([key_bias_vector, value_bias_vector])
        kv_cols = key_projection_weight.shape[1]
        query_matrix, key_value = lax.optimization_barrier((query_matrix, key_value))
        key_rows = key_value[:, :kv_cols]
        query_matrix = apply_rotary(
            query_matrix.reshape(count, local_heads, head_dim), starts, head_dim
        ).astype(jnp.bfloat16)
        key_rows = apply_rotary(
            key_rows.reshape(count, local_kv, head_dim), starts, head_dim
        ).astype(jnp.bfloat16)
        value_rows = key_value[:, kv_cols:].astype(jnp.bfloat16)
        return [
            query_matrix.reshape(count, local_heads * head_dim),
            key_rows.reshape(count, local_kv * head_dim),
            value_rows,
        ]

    qkv = project(jnp.concatenate(pieces, axis=0), sequence_starts)

    shift_order = ctx_count <= 8
    if shift_order:
        shifted_dest = jnp.where(
            my_dest >= 0,
            ((my_dest // pack_len - ctx_index) % ctx_count) * pack_len + my_dest % pack_len,
            -1,
        )
    else:
        shifted_dest = my_dest
    places = to_work_order(send_places(shifted_dest, ctx_count, group_cap, pack_len))
    send_hot = (
        places[None, :] == jnp.arange(ctx_count * group_cap, dtype=jnp.int32)[:, None]
    ).astype(jnp.bfloat16)
    outgoing = jnp.concatenate(
        [
            jnp.dot(send_hot, part, preferred_element_type=jnp.float32).astype(jnp.bfloat16)
            for part in qkv
        ],
        axis=1,
    )
    arrived = exchange(outgoing, "ctx", ctx_count)

    mine = (pool_dest >= 0) & (pool_dest // pack_len == ctx_index)
    mine_grid = mine.reshape(ctx_count, group_rows).astype(jnp.int32)
    rank_in = jnp.cumsum(mine_grid, axis=1) - mine_grid
    source_ctx = jnp.arange(ctx_count, dtype=jnp.int32)[:, None]
    if shift_order:
        source_ctx = (ctx_index - source_ctx) % ctx_count
    arrived_index = (
        source_ctx * group_cap + rank_in
    ).reshape(-1)
    my_slot_of_row = jnp.where(mine, pool_dest - ctx_index * pack_len, -1)
    slot_ids = jnp.arange(pack_len, dtype=jnp.int32)
    names_slot = my_slot_of_row[None, :] == slot_ids[:, None]
    source_of_slot = jnp.sum(jnp.where(names_slot, arrived_index[None, :], 0), axis=1)
    q_width = local_heads * head_dim
    kv_width = local_kv * head_dim
    packed_q = select_rows(source_of_slot, arrived[:, :q_width])
    packed_kv = select_rows(source_of_slot, arrived[:, q_width:])
    query_matrix = packed_q.reshape(pack_len, local_kv, query_group_count, head_dim)
    projected_key_rows = packed_kv[:, :kv_width].reshape(pack_len, local_kv, head_dim)
    projected_value_rows = packed_kv[:, kv_width:].reshape(pack_len, local_kv, head_dim)

    own_lengths = seq_len[0]
    own_ends = jnp.cumsum(own_lengths).astype(jnp.int32)
    segment = jnp.sum((own_ends[None, :] <= slot_ids[:, None]).astype(jnp.int32), axis=1)

    score_scale = 1.0 / math.sqrt(head_dim)
    chunk_count = 4 if pack_len % 32 == 0 else 1
    chunk_len = pack_len // chunk_count
    results = []
    for chunk in range(chunk_count):
        lo, hi = chunk * chunk_len, (chunk + 1) * chunk_len
        scores = (
            jnp.einsum(
                "qkgd,tkd->kgqt",
                query_matrix[lo:hi],
                projected_key_rows[:hi],
                preferred_element_type=jnp.float32,
            )
            * score_scale
        )
        allowed = (segment[lo:hi, None] == segment[None, :hi]) & (
            slot_ids[None, :hi] <= slot_ids[lo:hi, None]
        )
        scores = jnp.where(allowed[None, None], scores, -1e30)
        row_max = jnp.max(scores, axis=-1, keepdims=True)
        weights = jnp.exp(scores - row_max)
        row_total = jnp.sum(weights, axis=-1, keepdims=True)
        probability = (weights / row_total).astype(jnp.bfloat16)
        mixed_heads = jnp.einsum(
            "kgqt,tkd->qkgd",
            probability,
            projected_value_rows[:hi],
            preferred_element_type=jnp.float32,
        )
        mixed_heads = mixed_heads.astype(jnp.bfloat16).reshape(chunk_len, local_heads * head_dim)
        partial_out = jnp.dot(mixed_heads, w_out, preferred_element_type=jnp.float32)
        results.append(halving_scatter(partial_out, "head", head_count).astype(jnp.bfloat16))
    return jnp.concatenate(results, axis=0)


def shift_gather(part, axis_name, count):
    if count > 8:
        return doubling_gather(part, axis_name, count)
    me = lax.axis_index(axis_name)
    by_shift = [part] + [
        lax.ppermute(part, axis_name, [(i, (i + shift) % count) for i in range(count)])
        for shift in range(1, count)
    ]
    stacked = jnp.stack(by_shift)
    return jnp.take(stacked, (me - jnp.arange(count)) % count, axis=0).reshape(
        (count * part.shape[0],) + part.shape[1:]
    )


def exchange(outgoing, axis_name, count):
    if count > 8:
        return lax.all_to_all(outgoing, axis_name, split_axis=0, concat_axis=0, tiled=True)
    chunks = outgoing.reshape((count, -1) + outgoing.shape[1:])
    arrived = [chunks[0]]
    for shift in range(1, count):
        pairs = [(i, (i + shift) % count) for i in range(count)]
        arrived.append(lax.ppermute(chunks[shift], axis_name, pairs))
    return jnp.concatenate(arrived, axis=0)


def halving_scatter(partial, axis_name, count):
    bits = count.bit_length() - 1
    if count != 1 << bits or bits == 0:
        return lax.psum_scatter(partial, axis_name, scatter_dimension=1, tiled=True)
    block = partial.shape[1] // count
    me = lax.axis_index(axis_name)
    pieces = [(b, partial[:, b * block : (b + 1) * block]) for b in range(count)]
    for stage in range(bits):
        bit = (me >> stage) & 1
        lows = [(b, x) for b, x in pieces if not (b >> stage) & 1]
        highs = [x for b, x in pieces if (b >> stage) & 1]
        keep = [jnp.where(bit == 0, lo, hi) for (_, lo), hi in zip(lows, highs)]
        send = jnp.stack([jnp.where(bit == 0, hi, lo) for (_, lo), hi in zip(lows, highs)])
        pairs = [(i, i ^ (1 << stage)) for i in range(count)]
        got = lax.ppermute(send, axis_name, pairs)
        pieces = [(b, k + got[i]) for i, ((b, _), k) in enumerate(zip(lows, keep))]
    return pieces[0][1]


def doubling_gather(part, axis_name, count):
    bits = count.bit_length() - 1
    if count != 1 << bits or bits == 0:
        return lax.all_gather(part, axis_name, tiled=True)
    me = lax.axis_index(axis_name)
    have = part[None]
    for stage in reversed(range(bits)):
        bit = (me >> stage) & 1
        pairs = [(i, i ^ (1 << stage)) for i in range(count)]
        got = lax.ppermute(have, axis_name, pairs)
        first = jnp.where(bit == 0, have, got)
        second = jnp.where(bit == 0, got, have)
        have = jnp.stack([first, second], axis=1).reshape((-1,) + part.shape)
    return have.reshape((count * part.shape[0],) + part.shape[1:])


def xor_gather(part, axis_name, count):
    me = lax.axis_index(axis_name)
    bits = count.bit_length() - 1
    if count != 1 << bits:
        return [lax.all_gather(part, axis_name, tiled=True)], jnp.arange(count, dtype=jnp.int32)
    pieces, masks = [part], [0]
    for stage in reversed(range(bits)):
        pairs = [(i, i ^ (1 << stage)) for i in range(count)]
        pieces = pieces + [lax.ppermute(p, axis_name, pairs) for p in pieces]
        masks = masks + [m ^ (1 << stage) for m in masks]
    return pieces, me ^ jnp.asarray(masks, dtype=jnp.int32)


def solution(mesh):
    in_specs = (
        P(("ctx", "head"), None),
        P(),
        P("ctx", None),
        P(),
        P(None, "head"),
        P("head"),
        P(None, "head"),
        P("head"),
        P(None, "head"),
        P("head"),
        P("head", None),
    )
    out_specs = P("ctx", "head")
    return jax.shard_map(local, mesh=mesh, in_specs=in_specs, out_specs=out_specs, check_vma=False)
```
